128 devices in a mesh: feed: 8 (over y, core), chan: 16 (over z, x).
Axes of the slice: x: 4, y: 4, z: 4, core: 2. Of those that a mesh axis runs over, the one named last changes fastest.
Arguments:
- voltages: bfloat16 [2, 2, 16, 8192, 1024], P(None, None, 'chan', None, 'feed'), may hold values from -6 to 6
- history: bfloat16 [2, 2, 16, 48, 1024], P(None, None, 'chan', None, 'feed'), may hold values from -6 to 6
- gains: float32 [2, 2, 16, 1024], P(None, None, 'chan', 'feed'), may hold values from -4 to 4
- weights: bfloat16 [2, 16, 1024, 1024], P(None, 'chan'), may hold values from -0.09375 to 0.09375
- beam_lists: int32 [16, 128], replicated, may hold values from 0 to 1023, as said below
- beam_counts: int32 [16], replicated, may hold values from 1 to 128, as said below
Outputs:
- power_blocks: bfloat16 [256, 256, 2048], P('feed', None, 'chan')
The draws below stay inside these ranges and needn't reach their ends.
Inputs may be any that keep to these rules, and one draw needn't show every extreme that they name: `beam_lists`: row n holds in its first beam_counts[n] entries, in increasing order, the beams that node n owns, and 0 in the others; every beam is owned by exactly one node. `beam_counts`: the counts sum to 1024; some node owns exactly 128 beams.
All inputs are finite; a program needn't handle non-finite values.
Results may differ from the reference program's by a relative error of at most 0.013.
Values may be sent and summed in bfloat16 or wider, within the bound.
No kernel may reach another device: no remote copies, remote signals or barrier semaphores. Data moves between devices by JAX's collectives and lax.ppermute only.
A program may use at most 192 MiB of HBM per device.

```python
import math
import jax
import jax.numpy as jnp
from jax import lax

FEEDS = 1024
BEAMS = 1024
POLS = 2
U = 16
TAPS = 4
TINT = 2
NODES = 16
COARSE = 16
CHANS = 256
SPECTRA = 512
SAMPLES = 8192
HIST = 48
BINS = 256
MOST = 128


def owner_plan(key):
    base_key = jax.random.fold_in(key, 7)
    key_busy, key_swing, key_shuffle, key_beams = jax.random.split(base_key, 4)
    others = NODES - 1
    base_load = (BEAMS - MOST) // others
    remainder = (BEAMS - MOST) % others
    pair_count = others // 2
    busiest = jax.random.randint(key_busy, (), 0, NODES, dtype=jnp.int32)
    swing = jax.random.randint(key_swing, (pair_count,), -(base_load // 2), base_load // 2 + 1, dtype=jnp.int32)
    shifts = jnp.zeros((others,), jnp.int32)
    pair_ids = jnp.arange(pair_count, dtype=jnp.int32) * 2
    shifts = shifts.at[pair_ids].set(swing).at[pair_ids + 1].set(-swing)
    extra = (jnp.arange(others, dtype=jnp.int32) < remainder).astype(jnp.int32)
    other_counts = base_load + extra + shifts
    shuffle = jax.random.permutation(key_shuffle, others)
    other_counts = other_counts[shuffle]
    node_ids = jnp.arange(NODES, dtype=jnp.int32)
    pick = jnp.clip(node_ids - (node_ids > busiest).astype(jnp.int32), 0, others - 1)
    counts = jnp.where(node_ids == busiest, jnp.int32(MOST), other_counts[pick]).astype(jnp.int32)
    ends = jnp.cumsum(counts).astype(jnp.int32)
    starts = ends - counts
    positions = jnp.arange(BEAMS, dtype=jnp.int32)
    owner_pos = jnp.sum((positions[:, None] >= ends[None, :]).astype(jnp.int32), axis=1).astype(jnp.int32)
    beam_order = jax.random.permutation(key_beams, BEAMS).astype(jnp.int32)
    owner_of = jnp.zeros((BEAMS,), jnp.int32).at[beam_order].set(owner_pos)
    sorted_beams = jnp.argsort(owner_of * BEAMS + positions).astype(jnp.int32)
    slot_ids = jnp.arange(MOST, dtype=jnp.int32)
    index_at = jnp.clip(starts[:, None] + slot_ids[None, :], 0, BEAMS - 1)
    lists = jnp.where(slot_ids[None, :] < counts[:, None], sorted_beams[index_at], 0).astype(jnp.int32)
    return (counts, lists)


def draw_beam_lists(key, part):
    return owner_plan(key)[1]


def draw_beam_counts(key, part):
    return owner_plan(key)[0]


def level_of(key, shape, cuts, least, high):
    def one(axis_at, blocks):
        draws = jax.random.uniform(jax.random.fold_in(jax.random.fold_in(key, 6), axis_at), (blocks,), jnp.float32, least / len(cuts), high / len(cuts))
        return jnp.repeat(jnp.exp(draws), shape[axis_at] // blocks).reshape((-1,) + (1,) * (len(shape) - axis_at - 1))

    gain = one(*cuts[0])
    for cut in cuts[1:]:
        gain = gain * one(*cut)
    return gain


def centred(rng, dims, width, limit, cuts=(), kind=jnp.bfloat16):
    values = width * jax.random.normal(rng, dims, jnp.float32)
    if cuts:
        values = values * level_of(rng, dims, cuts, -0.22, 0.18)
    return jnp.clip(values, -limit, limit).astype(kind)


def setup_inputs(seed: int = 0) -> dict:
    key_of = jax.random.split(jax.random.key(seed), 7)
    return {
        "voltages": centred(key_of[0], (2, POLS, COARSE, SAMPLES, FEEDS), 1.0, 6.0, ((2, 16), (4, 8))),
        "history": centred(key_of[1], (2, POLS, COARSE, HIST, FEEDS), 1.0, 6.0, ((2, 16), (4, 8))),
        "gains": centred(key_of[2], (2, POLS, COARSE, FEEDS), 1.0, 4.0, ((2, 16), (3, 8)), jnp.float32),
        "weights": centred(key_of[3], (2, COARSE, FEEDS, BEAMS), (4 * FEEDS) ** -0.5, 0.09375, ((1, 16),)),
        "beam_lists": draw_beam_lists(jax.random.fold_in(key_of[6], 71), 0),
        "beam_counts": draw_beam_counts(jax.random.fold_in(key_of[6], 71), 0),
    }


def window_taps():
    length = TAPS * U
    positions = jnp.arange(length, dtype=jnp.float32)
    offsets = (positions - (length - 1) / 2.0) / U
    hann_taper = 0.5 - 0.5 * jnp.cos(2.0 * math.pi * (positions + 0.5) / length)
    taps_window = jnp.sinc(offsets) * hann_taper
    return taps_window / jnp.sqrt(jnp.sum(taps_window * taps_window) / U)

def dft_table():
    index_n = jnp.arange(U, dtype=jnp.int32)
    products = index_n[:, None] * index_n[None, :] % U
    phases = 2.0 * math.pi * products.astype(jnp.float32) / U
    cosine = jnp.cos(phases) / math.sqrt(U)
    sine = jnp.sin(phases) / math.sqrt(U)
    return jnp.stack([jnp.stack([cosine, -sine]), jnp.stack([sine, cosine])])

def filterbank(stream, frames, gains):
    shape_in = stream.shape
    taps_window = window_taps().reshape(TAPS, U)
    frames_data = stream.astype(jnp.float32).reshape(shape_in[0], shape_in[1], shape_in[2], frames + TAPS - 1, U, shape_in[4])
    filtered = taps_window[0][:, None] * frames_data[:, :, :, 0:frames]
    for tap_index in range(1, TAPS):
        filtered = filtered + taps_window[tap_index][:, None] * frames_data[:, :, :, tap_index:tap_index + frames]
    spectrum = jnp.einsum('rpctnf,rsnk->spctkf', filtered, dft_table(), precision=lax.Precision.HIGHEST)
    gain_cols = gains[:, :, :, None, None, :]
    real_part = gain_cols[0] * spectrum[0] - gain_cols[1] * spectrum[1]
    imag_part = gain_cols[0] * spectrum[1] + gain_cols[1] * spectrum[0]
    return jnp.stack([real_part, imag_part]).astype(jnp.bfloat16)

def detect(calibrated, weights):
    outputs = []
    spectra_here = calibrated.shape[3]
    fine_items = calibrated.shape[4]
    beam_total = weights.shape[3]
    for chan_index in range(calibrated.shape[2]):
        rows_in = calibrated[:, :, chan_index].reshape(2, -1, calibrated.shape[5]).astype(jnp.float32)
        products = jnp.einsum('rmf,sfb->rsmb', rows_in, weights[:, chan_index].astype(jnp.float32), precision=lax.Precision.HIGHEST)
        real_part = products[0, 0] - products[1, 1]
        imag_part = products[0, 1] + products[1, 0]
        power_sum = (real_part * real_part + imag_part * imag_part).reshape(2, spectra_here, fine_items, beam_total)
        power_sum = lax.optimization_barrier(jnp.sum(power_sum, axis=0)).reshape(spectra_here // TINT, TINT, fine_items, beam_total)
        power_sum = lax.optimization_barrier(jnp.sum(power_sum, axis=1)) * (1.0 / (4.0 * TINT))
        outputs.append(power_sum.astype(jnp.bfloat16))
    return jnp.stack(outputs, axis=1)

def reference(voltages, history, gains, weights, beam_lists, beam_counts):

    def per_coarse(pieces):
        volt_part, hist_part, gain_part, weight_part = pieces
        stream = jnp.concatenate([hist_part, volt_part], axis=2)[:, :, None]
        calibrated = filterbank(stream, SPECTRA, gain_part[:, :, None])
        return detect(calibrated, weight_part[:, None])[:, 0]
    per_chan = lax.map(per_coarse, (jnp.moveaxis(voltages, 2, 0), jnp.moveaxis(history, 2, 0), jnp.moveaxis(gains, 2, 0), jnp.moveaxis(weights, 1, 0)))
    detected = jnp.moveaxis(per_chan, 0, 1).reshape(BINS, CHANS, BEAMS)
    flat_ids = beam_lists.reshape(-1).astype(jnp.int32)
    live_slots = (jnp.arange(MOST, dtype=jnp.int32)[None, :] < beam_counts[:, None]).reshape(-1)
    picked = jnp.take(detected, flat_ids, axis=2)
    return jnp.where(live_slots, picked, jnp.zeros((), jnp.bfloat16))
```

```python
import math

import numpy as np
import jax
import jax.numpy as jnp
from jax import lax
from jax.experimental import pallas as pl
from jax.experimental.pallas import tpu as pltpu
from jax.sharding import PartitionSpec as P

U = 16
TAPS = 4
TINT = 2
IB = 4


def window_taps_np():
    length = TAPS * U
    positions = np.arange(length, dtype=np.float64)
    offsets = (positions - (length - 1) / 2.0) / U
    hann_taper = 0.5 - 0.5 * np.cos(2.0 * math.pi * (positions + 0.5) / length)
    taps_window = np.sinc(offsets) * hann_taper
    taps_window = taps_window / np.sqrt(np.sum(taps_window * taps_window) / U)
    return taps_window.astype(np.float32)


def _cmul_const(re, im, wr, wi):
    if wi == 0.0:
        if wr == 1.0:
            return re, im
        if wr == -1.0:
            return -re, -im
        return re * wr, im * wr
    if wr == 0.0:
        if wi == 1.0:
            return -im, re
        if wi == -1.0:
            return im, -re
        return -im * wi, re * wi
    return re * wr - im * wi, im * wr + re * wi


def _fft(xs):
    count = len(xs)
    if count == 1:
        return xs
    even = _fft(xs[0::2])
    odd = _fft(xs[1::2])
    out = [None] * count
    for k in range(count // 2):
        angle = -2.0 * math.pi * k / count
        wr, wi = math.cos(angle), math.sin(angle)
        wr = float(np.round(wr)) if abs(wr - np.round(wr)) < 1e-12 else wr
        wi = float(np.round(wi)) if abs(wi - np.round(wi)) < 1e-12 else wi
        tr, ti = _cmul_const(odd[k][0], odd[k][1], wr, wi)
        er, ei = even[k]
        out[k] = (er + tr, ei + ti)
        out[k + count // 2] = (er - tr, ei - ti)
    return out


def _filter_kernel(main_ref, pre0_ref, pre1_ref, pre2_ref, hist_ref, gain_ref, out_ref, xs_ref, sc_ref):
    tdev = pl.program_id(1)
    taps = (window_taps_np() * np.float32(0.25)).astype(np.float32)
    rows_main = main_ref.shape[3]
    for r in range(2):
        xs_ref[r, pl.ds(48, rows_main), :] = main_ref[r, 0, 0].astype(jnp.float32)

    @pl.when(tdev == 0)
    def _():
        for r in range(2):
            xs_ref[r, pl.ds(0, 48), :] = hist_ref[r, 0, 0].astype(jnp.float32)

    @pl.when(tdev != 0)
    def _():
        for r in range(2):
            for m, pre in enumerate((pre0_ref, pre1_ref, pre2_ref)):
                xs_ref[r, pl.ds(16 * m, 16), :] = pre[r, 0, 0].astype(jnp.float32)

    g_re = gain_ref[0, 0]
    g_im = gain_ref[1, 0]
    frames = rows_main // (U * TINT)
    for j in range(TINT):
        filt = []
        for n in range(U):
            parts = []
            for r in range(2):
                acc = None
                for q in range(TAPS):
                    x = xs_ref[r, pl.ds((j + q) * U + n, frames, stride=U * TINT), :]
                    term = np.float32(taps[q * U + n]) * x
                    acc = term if acc is None else acc + term
                parts.append(acc)
            filt.append((parts[0], parts[1]))
        spec = _fft(filt)
        for k in range(U):
            s_re, s_im = spec[k]
            c_re = g_re * s_re - g_im * s_im
            c_im = g_re * s_im + g_im * s_re
            sc_ref[0, j, pl.ds(k, frames, stride=U), :] = c_re
            sc_ref[1, j, pl.ds(k, frames, stride=U), :] = c_im
    nb = out_ref.shape[1]
    for s in range(2):
        for j in range(TINT):
            val = sc_ref[s, j].astype(jnp.bfloat16)
            out_ref[0, :, s, 0, j] = val.reshape(nb, IB, U, 128)


def filterbank(voltages, history, gains):
    _, pols, _, samples, feeds = voltages.shape
    nblk = 8
    rows_main = samples // nblk
    frames_blk = rows_main // U
    nb = frames_blk // TINT // IB

    def pre_map(m):
        def index(p, t):
            return (0, p, 0, jnp.maximum(t * (rows_main // 16) - 3 + m, 0), 0)

        return index

    return pl.pallas_call(
        _filter_kernel,
        grid=(pols, nblk),
        in_specs=[
            pl.BlockSpec((2, 1, 1, rows_main, feeds), lambda p, t: (0, p, 0, t, 0)),
            pl.BlockSpec((2, 1, 1, 16, feeds), pre_map(0)),
            pl.BlockSpec((2, 1, 1, 16, feeds), pre_map(1)),
            pl.BlockSpec((2, 1, 1, 16, feeds), pre_map(2)),
            pl.BlockSpec((2, 1, 1, 48, feeds), lambda p, t: (0, p, 0, 0, 0)),
            pl.BlockSpec((2, 1, 1, feeds), lambda p, t: (0, p, 0, 0)),
        ],
        out_specs=pl.BlockSpec((1, nb, 2, 1, 2, IB, U, feeds), lambda p, t: (t, 0, 0, p, 0, 0, 0, 0)),
        out_shape=jax.ShapeDtypeStruct((nblk, nb, 2, pols, 2, IB, U, feeds), jnp.bfloat16),
        scratch_shapes=[
            pltpu.VMEM((2, rows_main + 48, feeds), jnp.float32),
            pltpu.VMEM((2, TINT, frames_blk // TINT * U, feeds), jnp.float32),
        ],
        cost_estimate=pl.CostEstimate(
            flops=2 * 2 * pols * samples * feeds * 20,
            bytes_accessed=2 * voltages.size * 2,
            transcendentals=0,
        ),
    )(voltages, voltages, voltages, voltages, history, gains)


def _beam_kernel(cal_ref, w_ref, sel_ref, out_ref):
    nsrc = cal_ref.shape[0]
    rows = 2 * 2 * IB * U
    halves = []
    for s in range(2):
        pieces = [cal_ref[d, 0, s].reshape(rows, 128) for d in range(nsrc)]
        halves.append(jnp.concatenate(pieces, axis=1))
    lhs = jnp.concatenate(halves, axis=0)
    prod_re = jnp.dot(lhs, w_ref[0, 0], preferred_element_type=jnp.float32)
    prod_im = jnp.dot(lhs, w_ref[1, 0], preferred_element_type=jnp.float32)
    real_part = prod_re[:rows] - prod_im[rows:]
    imag_part = prod_im[:rows] + prod_re[rows:]
    power = real_part * real_part + imag_part * imag_part
    quarter = rows // 2
    power = power[:quarter] + power[quarter:]
    eighth = quarter // 2
    power = power[:eighth] + power[eighth:]
    detected = (power * (1.0 / (4.0 * TINT))).astype(jnp.bfloat16)
    picked = jnp.dot(detected, sel_ref[...], preferred_element_type=jnp.float32).astype(jnp.bfloat16)
    nodes = out_ref.shape[1]
    for n in range(nodes):
        out_ref[:, n] = picked[:, n * 128 : (n + 1) * 128].reshape(IB, U, 128)


def beamform(cal, weights, select):
    nsrc, nb = cal.shape[0], cal.shape[1]
    feeds, beams = weights.shape[2], weights.shape[3]
    slots = select.shape[1]
    nodes = slots // 128
    return pl.pallas_call(
        _beam_kernel,
        grid=(nb,),
        in_specs=[
            pl.BlockSpec((nsrc, 1, 2, 2, 2, IB, U, 128), lambda i: (0, i, 0, 0, 0, 0, 0, 0)),
            pl.BlockSpec((2, 1, feeds, beams), lambda i: (0, 0, 0, 0)),
            pl.BlockSpec((beams, slots), lambda i: (0, 0)),
        ],
        out_specs=pl.BlockSpec((IB, nodes, U, 128), lambda i: (i, 0, 0, 0)),
        out_shape=jax.ShapeDtypeStruct((nb * IB, nodes, U, 128), jnp.bfloat16),
        cost_estimate=pl.CostEstimate(
            flops=2 * 2 * (4 * nb * IB * U * TINT) * feeds * beams + 2 * nb * IB * U * beams * slots,
            bytes_accessed=cal.size * 2 + weights.size * 2 + select.size * 2 + nb * IB * U * slots * 2,
            transcendentals=0,
        ),
        compiler_params=pltpu.CompilerParams(vmem_limit_bytes=60 * 1024 * 1024),
    )(cal, weights, select)


def on_device(voltages, history, gains, weights, beam_lists, beam_counts):
    capacity = beam_lists.shape[1]
    beams = weights.shape[3]
    flat_ids = beam_lists.reshape(-1)
    live_slots = (jnp.arange(capacity, dtype=jnp.int32)[None, :] < beam_counts[:, None]).reshape(-1)
    select = (
        (jnp.arange(beams, dtype=jnp.int32)[:, None] == flat_ids[None, :]) & live_slots[None, :]
    ).astype(jnp.bfloat16)
    calibrated = filterbank(voltages, history, gains)
    gathered = lax.all_to_all(calibrated, "feed", split_axis=0, concat_axis=0, tiled=True)
    picked = beamform(gathered, weights, select)
    exchanged = lax.all_to_all(picked, "chan", split_axis=1, concat_axis=1, tiled=True)
    bins, nodes, fine, width = exchanged.shape
    return exchanged.reshape(bins, nodes * fine, width)


def solution(mesh):
    in_specs = (
        P(None, None, "chan", None, "feed"),
        P(None, None, "chan", None, "feed"),
        P(None, None, "chan", "feed"),
        P(None, "chan", None, None),
        P(),
        P(),
    )
    out_specs = P("feed", None, "chan")
    return jax.shard_map(
        on_device, mesh=mesh, in_specs=in_specs, out_specs=out_specs, check_vma=False
    )
```

```python
import math

import numpy as np
import jax
import jax.numpy as jnp
from jax import lax
from jax.experimental import pallas as pl
from jax.experimental.pallas import tpu as pltpu
from jax.sharding import PartitionSpec as P

U = 16
TAPS = 4
TINT = 2
IB = 4
CHUNKS = 4


def window_taps_np():
    length = TAPS * U
    positions = np.arange(length, dtype=np.float64)
    offsets = (positions - (length - 1) / 2.0) / U
    hann_taper = 0.5 - 0.5 * np.cos(2.0 * math.pi * (positions + 0.5) / length)
    taps_window = np.sinc(offsets) * hann_taper
    taps_window = taps_window / np.sqrt(np.sum(taps_window * taps_window) / U)
    return taps_window.astype(np.float32)


def _cmul_const(re, im, wr, wi):
    if wi == 0.0:
        if wr == 1.0:
            return re, im
        if wr == -1.0:
            return -re, -im
        return re * wr, im * wr
    if wr == 0.0:
        if wi == 1.0:
            return -im, re
        if wi == -1.0:
            return im, -re
        return -im * wi, re * wi
    return re * wr - im * wi, im * wr + re * wi


def _fft(xs):
    count = len(xs)
    if count == 1:
        return xs
    even = _fft(xs[0::2])
    odd = _fft(xs[1::2])
    out = [None] * count
    for k in range(count // 2):
        angle = -2.0 * math.pi * k / count
        wr, wi = math.cos(angle), math.sin(angle)
        wr = float(np.round(wr)) if abs(wr - np.round(wr)) < 1e-12 else wr
        wi = float(np.round(wi)) if abs(wi - np.round(wi)) < 1e-12 else wi
        tr, ti = _cmul_const(odd[k][0], odd[k][1], wr, wi)
        er, ei = even[k]
        out[k] = (er + tr, ei + ti)
        out[k + count // 2] = (er - tr, ei - ti)
    return out


def _filter_kernel(chunk, main_ref, pre0_ref, pre1_ref, pre2_ref, hist_ref, gain_ref, out_ref, xs_ref, sc_ref):
    taps = (window_taps_np() * np.float32(0.25)).astype(np.float32)
    rows_main = main_ref.shape[4]
    frames = rows_main // (U * TINT)
    nblk = main_ref.shape[2]
    nb = out_ref.shape[1]
    g_re = gain_ref[0, 0]
    g_im = gain_ref[1, 0]

    def block(tdev, carry):
        for r in range(2):
            xs_ref[r, pl.ds(48, rows_main), :] = main_ref[r, 0, tdev, 0].astype(jnp.float32)
        if chunk == 0:
            prev = jnp.maximum(tdev - 1, 0)
            for r in range(2):
                for m, pre in enumerate((pre0_ref, pre1_ref, pre2_ref)):
                    xs_ref[r, pl.ds(16 * m, 16), :] = pre[r, 0, prev, 0].astype(jnp.float32)

            @pl.when(tdev == 0)
            def _():
                for r in range(2):
                    xs_ref[r, pl.ds(0, 48), :] = hist_ref[r, 0, 0].astype(jnp.float32)
        else:
            for r in range(2):
                for m, pre in enumerate((pre0_ref, pre1_ref, pre2_ref)):
                    xs_ref[r, pl.ds(16 * m, 16), :] = pre[r, 0, tdev, 0].astype(jnp.float32)

        for j in range(TINT):
            filt = []
            for n in range(U):
                parts = []
                for r in range(2):
                    acc = None
                    for q in range(TAPS):
                        x = xs_ref[r, pl.ds((j + q) * U + n, frames, stride=U * TINT), :]
                        term = np.float32(taps[q * U + n]) * x
                        acc = term if acc is None else acc + term
                    parts.append(acc)
                filt.append((parts[0], parts[1]))
            spec = _fft(filt)
            for k in range(U):
                s_re, s_im = spec[k]
                c_re = g_re * s_re - g_im * s_im
                c_im = g_re * s_im + g_im * s_re
                sc_ref[0, j, pl.ds(k, frames, stride=U), :] = c_re
                sc_ref[1, j, pl.ds(k, frames, stride=U), :] = c_im
        for s in range(2):
            for j in range(TINT):
                val = sc_ref[s, j].astype(jnp.bfloat16)
                out_ref[tdev, :, s, 0, j] = val.reshape(nb, IB, U, 128)
        return carry

    lax.fori_loop(0, nblk, block, 0)


def filterbank(voltages, history, gains, chunk, chunks):
    _, pols, _, samples, feeds = voltages.shape
    nblk = 8
    rows_blk = samples // nblk
    rows_main = rows_blk // chunks
    frames = rows_main // U
    nb = frames // TINT // IB
    main = voltages.reshape(2, pols, nblk, chunks, rows_main, feeds)
    units = voltages.reshape(2, pols, nblk, rows_blk // 16, 16, feeds)
    if chunk == 0:
        first = rows_blk // 16 - 3
    else:
        first = chunk * rows_main // 16 - 3

    def pre_map(m):
        return lambda p: (0, p, 0, first + m, 0, 0)

    return pl.pallas_call(
        lambda *refs: _filter_kernel(chunk, *refs),
        grid=(pols,),
        in_specs=[
            pl.BlockSpec((2, 1, nblk, 1, rows_main, feeds), lambda p: (0, p, 0, chunk, 0, 0)),
            pl.BlockSpec((2, 1, nblk, 1, 16, feeds), pre_map(0)),
            pl.BlockSpec((2, 1, nblk, 1, 16, feeds), pre_map(1)),
            pl.BlockSpec((2, 1, nblk, 1, 16, feeds), pre_map(2)),
            pl.BlockSpec((2, 1, 1, 48, feeds), lambda p: (0, p, 0, 0, 0)),
            pl.BlockSpec((2, 1, 1, feeds), lambda p: (0, p, 0, 0)),
        ],
        out_specs=pl.BlockSpec((nblk, nb, 2, 1, 2, IB, U, feeds), lambda p: (0, 0, 0, p, 0, 0, 0, 0)),
        out_shape=jax.ShapeDtypeStruct((nblk, nb, 2, pols, 2, IB, U, feeds), jnp.bfloat16),
        scratch_shapes=[
            pltpu.VMEM((2, rows_main + 48, feeds), jnp.float32),
            pltpu.VMEM((2, TINT, frames // TINT * U, feeds), jnp.float32),
        ],
        cost_estimate=pl.CostEstimate(
            flops=2 * 2 * pols * samples * feeds * 20 // chunks,
            bytes_accessed=2 * voltages.size * 2 // chunks,
            transcendentals=0,
        ),
    )(main, units, units, units, history, gains)


def _beam_kernel(cal_ref, w_ref, sel_ref, out_ref):
    nsrc = cal_ref.shape[0]
    rows = 2 * 2 * IB * U
    halves = []
    for s in range(2):
        pieces = [cal_ref[d, 0, s].reshape(rows, 128) for d in range(nsrc)]
        halves.append(jnp.concatenate(pieces, axis=1))
    lhs = jnp.concatenate(halves, axis=0)
    prod_re = jnp.dot(lhs, w_ref[0, 0], preferred_element_type=jnp.float32)
    prod_im = jnp.dot(lhs, w_ref[1, 0], preferred_element_type=jnp.float32)
    real_part = prod_re[:rows] - prod_im[rows:]
    imag_part = prod_im[:rows] + prod_re[rows:]
    power = real_part * real_part + imag_part * imag_part
    quarter = rows // 2
    power = power[:quarter] + power[quarter:]
    eighth = quarter // 2
    power = power[:eighth] + power[eighth:]
    detected = (power * (1.0 / (4.0 * TINT))).astype(jnp.bfloat16)
    picked = jnp.dot(detected, sel_ref[...], preferred_element_type=jnp.float32).astype(jnp.bfloat16)
    nodes = out_ref.shape[1]
    for n in range(nodes):
        out_ref[:, n] = picked[:, n * 128 : (n + 1) * 128].reshape(IB, U, 128)


def beamform(cal, weights, select):
    nsrc, nb = cal.shape[0], cal.shape[1]
    feeds, beams = weights.shape[2], weights.shape[3]
    slots = select.shape[1]
    nodes = slots // 128
    return pl.pallas_call(
        _beam_kernel,
        grid=(nb,),
        in_specs=[
            pl.BlockSpec((nsrc, 1, 2, 2, 2, IB, U, 128), lambda i: (0, i, 0, 0, 0, 0, 0, 0)),
            pl.BlockSpec((2, 1, feeds, beams), lambda i: (0, 0, 0, 0)),
            pl.BlockSpec((beams, slots), lambda i: (0, 0)),
        ],
        out_specs=pl.BlockSpec((IB, nodes, U, 128), lambda i: (i, 0, 0, 0)),
        out_shape=jax.ShapeDtypeStruct((nb * IB, nodes, U, 128), jnp.bfloat16),
        cost_estimate=pl.CostEstimate(
            flops=2 * 2 * (4 * nb * IB * U * TINT) * feeds * beams + 2 * nb * IB * U * beams * slots,
            bytes_accessed=cal.size * 2 + weights.size * 2 + select.size * 2 + nb * IB * U * slots * 2,
            transcendentals=0,
        ),
        compiler_params=pltpu.CompilerParams(vmem_limit_bytes=60 * 1024 * 1024),
    )(cal, weights, select)


def on_device(voltages, history, gains, weights, beam_lists, beam_counts):
    capacity = beam_lists.shape[1]
    beams = weights.shape[3]
    flat_ids = beam_lists.reshape(-1)
    live_slots = (jnp.arange(capacity, dtype=jnp.int32)[None, :] < beam_counts[:, None]).reshape(-1)
    select = (
        (jnp.arange(beams, dtype=jnp.int32)[:, None] == flat_ids[None, :]) & live_slots[None, :]
    ).astype(jnp.bfloat16)
    outs = []
    for chunk in range(CHUNKS):
        calibrated = filterbank(voltages, history, gains, chunk, CHUNKS)
        gathered = lax.all_to_all(calibrated, "feed", split_axis=0, concat_axis=0, tiled=True)
        picked = beamform(gathered, weights, select)
        outs.append(lax.all_to_all(picked, "chan", split_axis=1, concat_axis=1, tiled=True))
    exchanged = jnp.concatenate(outs, axis=0)
    bins, nodes, fine, width = exchanged.shape
    return exchanged.reshape(bins, nodes * fine, width)


def solution(mesh):
    in_specs = (
        P(None, None, "chan", None, "feed"),
        P(None, None, "chan", None, "feed"),
        P(None, None, "chan", "feed"),
        P(None, "chan", None, None),
        P(),
        P(),
    )
    out_specs = P("feed", None, "chan")
    return jax.shard_map(
        on_device, mesh=mesh, in_specs=in_specs, out_specs=out_specs, check_vma=False
    )
```

```python
import math

import numpy as np
import jax
import jax.numpy as jnp
from jax import lax
from jax.experimental import pallas as pl
from jax.experimental.pallas import tpu as pltpu
from jax.sharding import PartitionSpec as P

U = 16
TAPS = 4
TINT = 2
IB = 4
CHUNKS = 4
FRAMES = 2 * IB


def window_taps_np():
    length = TAPS * U
    positions = np.arange(length, dtype=np.float64)
    offsets = (positions - (length - 1) / 2.0) / U
    hann_taper = 0.5 - 0.5 * np.cos(2.0 * math.pi * (positions + 0.5) / length)
    taps_window = np.sinc(offsets) * hann_taper
    taps_window = taps_window / np.sqrt(np.sum(taps_window * taps_window) / U)
    return taps_window.astype(np.float32)


def band_matrix():
    taps = window_taps_np().astype(np.float64)
    span = (FRAMES + TAPS - 1) * U
    index_n = np.arange(U)
    phases = 2.0 * math.pi * ((index_n[:, None] * index_n[None, :]) % U) / U
    cosine = np.cos(phases) / math.sqrt(U)
    sine = np.sin(phases) / math.sqrt(U)
    table = np.array([[cosine, -sine], [sine, cosine]])
    band = np.zeros((2, FRAMES, U, 2, span))
    for t in range(FRAMES):
        for m in range(TAPS * U):
            for r in range(2):
                band[:, t, :, r, t * U + m] = taps[m] * table[r, :, m % U, :]
    band = band.reshape(2 * FRAMES * U, 2 * span).astype(np.float32)
    high = band.astype(jnp.bfloat16)
    low = (band - high.astype(np.float32)).astype(jnp.bfloat16)
    return np.stack([high, low])


def _filter_kernel(chunk, main_ref, pre0_ref, pre1_ref, pre2_ref, hist_ref, gain_ref, band_ref, out_ref, xs_ref):
    rows_main = main_ref.shape[4]
    nblk = main_ref.shape[2]
    nb = out_ref.shape[1]
    span = (FRAMES + TAPS - 1) * U
    half = FRAMES * U
    g_re = gain_ref[0, 0]
    g_im = gain_ref[1, 0]

    def block(tdev, carry):
        for r in range(2):
            xs_ref[r, pl.ds(48, rows_main), :] = main_ref[r, 0, tdev, 0]
        if chunk == 0:
            prev = jnp.maximum(tdev - 1, 0)
            for r in range(2):
                for m, pre in enumerate((pre0_ref, pre1_ref, pre2_ref)):
                    xs_ref[r, pl.ds(16 * m, 16), :] = pre[r, 0, prev, 0]

            @pl.when(tdev == 0)
            def _():
                for r in range(2):
                    xs_ref[r, pl.ds(0, 48), :] = hist_ref[r, 0, 0]
        else:
            for r in range(2):
                for m, pre in enumerate((pre0_ref, pre1_ref, pre2_ref)):
                    xs_ref[r, pl.ds(16 * m, 16), :] = pre[r, 0, tdev, 0]

        for ib in range(nb):
            rhs = jnp.concatenate(
                [xs_ref[r, pl.ds(ib * half, span), :] for r in range(2)], axis=0
            )
            spec = jnp.dot(band_ref[0], rhs, preferred_element_type=jnp.float32)
            spec = spec + jnp.dot(band_ref[1], rhs, preferred_element_type=jnp.float32)
            s_re = spec[:half]
            s_im = spec[half:]
            c_re = g_re * s_re - g_im * s_im
            c_im = g_re * s_im + g_im * s_re
            out_ref[tdev, ib, 0, 0] = c_re.astype(jnp.bfloat16).reshape(IB, TINT, U, 128)
            out_ref[tdev, ib, 1, 0] = c_im.astype(jnp.bfloat16).reshape(IB, TINT, U, 128)
        return carry

    lax.fori_loop(0, nblk, block, 0)


def filterbank(voltages, history, gains, band, chunk, chunks):
    _, pols, _, samples, feeds = voltages.shape
    nblk = 8
    rows_blk = samples // nblk
    rows_main = rows_blk // chunks
    nb = rows_main // U // FRAMES
    main = voltages.reshape(2, pols, nblk, chunks, rows_main, feeds)
    units = voltages.reshape(2, pols, nblk, rows_blk // 16, 16, feeds)
    if chunk == 0:
        first = rows_blk // 16 - 3
    else:
        first = chunk * rows_main // 16 - 3

    def pre_map(m):
        return lambda p: (0, p, 0, first + m, 0, 0)

    return pl.pallas_call(
        lambda *refs: _filter_kernel(chunk, *refs),
        grid=(pols,),
        in_specs=[
            pl.BlockSpec((2, 1, nblk, 1, rows_main, feeds), lambda p: (0, p, 0, chunk, 0, 0)),
            pl.BlockSpec((2, 1, nblk, 1, 16, feeds), pre_map(0)),
            pl.BlockSpec((2, 1, nblk, 1, 16, feeds), pre_map(1)),
            pl.BlockSpec((2, 1, nblk, 1, 16, feeds), pre_map(2)),
            pl.BlockSpec((2, 1, 1, 48, feeds), lambda p: (0, p, 0, 0, 0)),
            pl.BlockSpec((2, 1, 1, feeds), lambda p: (0, p, 0, 0)),
            pl.BlockSpec(band.shape, lambda p: (0, 0, 0)),
        ],
        out_specs=pl.BlockSpec((nblk, nb, 2, 1, IB, TINT, U, feeds), lambda p: (0, 0, 0, p, 0, 0, 0, 0)),
        out_shape=jax.ShapeDtypeStruct((nblk, nb, 2, pols, IB, TINT, U, feeds), jnp.bfloat16),
        scratch_shapes=[
            pltpu.VMEM((2, rows_main + 48, feeds), jnp.bfloat16),
        ],
        cost_estimate=pl.CostEstimate(
            flops=2 * band.size * feeds * pols * nblk * nb,
            bytes_accessed=2 * voltages.size * 2 // chunks,
            transcendentals=0,
        ),
    )(main, units, units, units, history, gains, band)


def _beam_kernel(cal_ref, w_ref, sel_ref, out_ref):
    nsrc = cal_ref.shape[0]
    rows = 2 * 2 * IB * U
    halves = []
    for s in range(2):
        pieces = [cal_ref[d, 0, s].reshape(rows, 128) for d in range(nsrc)]
        halves.append(jnp.concatenate(pieces, axis=1))
    lhs = jnp.concatenate(halves, axis=0)
    prod_re = jnp.dot(lhs, w_ref[0, 0], preferred_element_type=jnp.float32)
    prod_im = jnp.dot(lhs, w_ref[1, 0], preferred_element_type=jnp.float32)
    real_part = prod_re[:rows] - prod_im[rows:]
    imag_part = prod_im[:rows] + prod_re[rows:]
    power = real_part * real_part + imag_part * imag_part
    quarter = rows // 2
    power = power[:quarter] + power[quarter:]
    power = power.reshape(IB, TINT, U, power.shape[-1])
    power = (power[:, 0] + power[:, 1]).reshape(IB * U, power.shape[-1])
    detected = (power * (1.0 / (4.0 * TINT))).astype(jnp.bfloat16)
    picked = jnp.dot(detected, sel_ref[...], preferred_element_type=jnp.float32).astype(jnp.bfloat16)
    nodes = out_ref.shape[1]
    for n in range(nodes):
        out_ref[:, n] = picked[:, n * 128 : (n + 1) * 128].reshape(IB, U, 128)


def beamform(cal, weights, select):
    nsrc, nb = cal.shape[0], cal.shape[1]
    feeds, beams = weights.shape[2], weights.shape[3]
    slots = select.shape[1]
    nodes = slots // 128
    return pl.pallas_call(
        _beam_kernel,
        grid=(nb,),
        in_specs=[
            pl.BlockSpec((nsrc, 1, 2, 2, IB, TINT, U, 128), lambda i: (0, i, 0, 0, 0, 0, 0, 0)),
            pl.BlockSpec((2, 1, feeds, beams), lambda i: (0, 0, 0, 0)),
            pl.BlockSpec((beams, slots), lambda i: (0, 0)),
        ],
        out_specs=pl.BlockSpec((IB, nodes, U, 128), lambda i: (i, 0, 0, 0)),
        out_shape=jax.ShapeDtypeStruct((nb * IB, nodes, U, 128), jnp.bfloat16),
        cost_estimate=pl.CostEstimate(
            flops=2 * 2 * (4 * nb * IB * U * TINT) * feeds * beams + 2 * nb * IB * U * beams * slots,
            bytes_accessed=cal.size * 2 + weights.size * 2 + select.size * 2 + nb * IB * U * slots * 2,
            transcendentals=0,
        ),
        compiler_params=pltpu.CompilerParams(vmem_limit_bytes=60 * 1024 * 1024),
    )(cal, weights, select)


def on_device(voltages, history, gains, weights, beam_lists, beam_counts):
    capacity = beam_lists.shape[1]
    beams = weights.shape[3]
    flat_ids = beam_lists.reshape(-1)
    live_slots = (jnp.arange(capacity, dtype=jnp.int32)[None, :] < beam_counts[:, None]).reshape(-1)
    select = (
        (jnp.arange(beams, dtype=jnp.int32)[:, None] == flat_ids[None, :]) & live_slots[None, :]
    ).astype(jnp.bfloat16)
    band = jnp.asarray(band_matrix())
    outs = []
    for chunk in range(CHUNKS):
        calibrated = filterbank(voltages, history, gains, band, chunk, CHUNKS)
        gathered = lax.all_to_all(calibrated, "feed", split_axis=0, concat_axis=0, tiled=True)
        picked = beamform(gathered, weights, select)
        outs.append(lax.all_to_all(picked, "chan", split_axis=1, concat_axis=1, tiled=True))
    exchanged = jnp.concatenate(outs, axis=0)
    bins, nodes, fine, width = exchanged.shape
    return exchanged.reshape(bins, nodes * fine, width)


def solution(mesh):
    in_specs = (
        P(None, None, "chan", None, "feed"),
        P(None, None, "chan", None, "feed"),
        P(None, None, "chan", "feed"),
        P(None, "chan", None, None),
        P(),
        P(),
    )
    out_specs = P("feed", None, "chan")
    return jax.shard_map(
        on_device, mesh=mesh, in_specs=in_specs, out_specs=out_specs, check_vma=False
    )
```

```python
import math

import numpy as np
import jax
import jax.numpy as jnp
from jax import lax
from jax.experimental import pallas as pl
from jax.experimental.pallas import tpu as pltpu
from jax.sharding import PartitionSpec as P

U = 16
TAPS = 4
TINT = 2
IB = 4
CHUNKS = 4
FRAMES = 2 * IB


def window_taps_np():
    length = TAPS * U
    positions = np.arange(length, dtype=np.float64)
    offsets = (positions - (length - 1) / 2.0) / U
    hann_taper = 0.5 - 0.5 * np.cos(2.0 * math.pi * (positions + 0.5) / length)
    taps_window = np.sinc(offsets) * hann_taper
    taps_window = taps_window / np.sqrt(np.sum(taps_window * taps_window) / U)
    return taps_window.astype(np.float32)


def band_matrix():
    taps = window_taps_np().astype(np.float64)
    span = (FRAMES + TAPS - 1) * U
    index_n = np.arange(U)
    phases = 2.0 * math.pi * ((index_n[:, None] * index_n[None, :]) % U) / U
    cosine = np.cos(phases) / math.sqrt(U)
    sine = np.sin(phases) / math.sqrt(U)
    table = np.array([[cosine, -sine], [sine, cosine]])
    band = np.zeros((2, FRAMES, U, 2, span))
    for t in range(FRAMES):
        for m in range(TAPS * U):
            for r in range(2):
                band[:, t, :, r, t * U + m] = taps[m] * table[r, :, m % U, :]
    band = band.reshape(2 * FRAMES * U, 2 * span).astype(np.float32)
    high = band.astype(jnp.bfloat16)
    low = (band - high.astype(np.float32)).astype(jnp.bfloat16)
    return np.stack([high, low])


def _filter_kernel(chunk, me_ref, main_ref, pre0_ref, pre1_ref, pre2_ref, hist_ref, gain_ref, band_ref, out_ref, xs_ref):
    rows_main = main_ref.shape[4]
    nblk = main_ref.shape[2]
    nb = out_ref.shape[1]
    span = (FRAMES + TAPS - 1) * U
    half = FRAMES * U
    g_re = gain_ref[0, 0]
    g_im = gain_ref[1, 0]

    def block(shift, carry):
        tdev = lax.rem(me_ref[0] + shift, nblk)
        for r in range(2):
            xs_ref[r, pl.ds(48, rows_main), :] = main_ref[r, 0, tdev, 0]
        if chunk == 0:
            prev = jnp.maximum(tdev - 1, 0)
            for r in range(2):
                for m, pre in enumerate((pre0_ref, pre1_ref, pre2_ref)):
                    xs_ref[r, pl.ds(16 * m, 16), :] = pre[r, 0, prev, 0]

            @pl.when(tdev == 0)
            def _():
                for r in range(2):
                    xs_ref[r, pl.ds(0, 48), :] = hist_ref[r, 0, 0]
        else:
            for r in range(2):
                for m, pre in enumerate((pre0_ref, pre1_ref, pre2_ref)):
                    xs_ref[r, pl.ds(16 * m, 16), :] = pre[r, 0, tdev, 0]

        for ib in range(nb):
            rhs = jnp.concatenate(
                [xs_ref[r, pl.ds(ib * half, span), :] for r in range(2)], axis=0
            )
            spec = jnp.dot(band_ref[0], rhs, preferred_element_type=jnp.float32)
            spec = spec + jnp.dot(band_ref[1], rhs, preferred_element_type=jnp.float32)
            s_re = spec[:half]
            s_im = spec[half:]
            c_re = g_re * s_re - g_im * s_im
            c_im = g_re * s_im + g_im * s_re
            out_ref[shift, ib, 0, 0] = c_re.astype(jnp.bfloat16).reshape(IB, TINT, U, 128)
            out_ref[shift, ib, 1, 0] = c_im.astype(jnp.bfloat16).reshape(IB, TINT, U, 128)
        return carry

    lax.fori_loop(0, nblk, block, 0)


def filterbank(me, voltages, history, gains, band, chunk, chunks):
    _, pols, _, samples, feeds = voltages.shape
    nblk = 8
    rows_blk = samples // nblk
    rows_main = rows_blk // chunks
    nb = rows_main // U // FRAMES
    main = voltages.reshape(2, pols, nblk, chunks, rows_main, feeds)
    units = voltages.reshape(2, pols, nblk, rows_blk // 16, 16, feeds)
    if chunk == 0:
        first = rows_blk // 16 - 3
    else:
        first = chunk * rows_main // 16 - 3

    def pre_map(m):
        return lambda p: (0, p, 0, first + m, 0, 0)

    return pl.pallas_call(
        lambda *refs: _filter_kernel(chunk, *refs),
        grid=(pols,),
        in_specs=[
            pl.BlockSpec(memory_space=pltpu.SMEM),
            pl.BlockSpec((2, 1, nblk, 1, rows_main, feeds), lambda p: (0, p, 0, chunk, 0, 0)),
            pl.BlockSpec((2, 1, nblk, 1, 16, feeds), pre_map(0)),
            pl.BlockSpec((2, 1, nblk, 1, 16, feeds), pre_map(1)),
            pl.BlockSpec((2, 1, nblk, 1, 16, feeds), pre_map(2)),
            pl.BlockSpec((2, 1, 1, 48, feeds), lambda p: (0, p, 0, 0, 0)),
            pl.BlockSpec((2, 1, 1, feeds), lambda p: (0, p, 0, 0)),
            pl.BlockSpec(band.shape, lambda p: (0, 0, 0)),
        ],
        out_specs=pl.BlockSpec((nblk, nb, 2, 1, IB, TINT, U, feeds), lambda p: (0, 0, 0, p, 0, 0, 0, 0)),
        out_shape=jax.ShapeDtypeStruct((nblk, nb, 2, pols, IB, TINT, U, feeds), jnp.bfloat16),
        scratch_shapes=[
            pltpu.VMEM((2, rows_main + 48, feeds), jnp.bfloat16),
        ],
        cost_estimate=pl.CostEstimate(
            flops=2 * band.size * feeds * pols * nblk * nb,
            bytes_accessed=2 * voltages.size * 2 // chunks,
            transcendentals=0,
        ),
    )(me, main, units, units, units, history, gains, band)


def _beam_kernel(*refs):
    cal_refs = refs[:-3]
    w_ref, sel_ref, out_ref = refs[-3:]
    rows = 2 * 2 * IB * U
    halves = []
    for s in range(2):
        pieces = [c[0, 0, s].reshape(rows, 128) for c in cal_refs]
        halves.append(jnp.concatenate(pieces, axis=1))
    lhs = jnp.concatenate(halves, axis=0)
    prod_re = jnp.dot(lhs, w_ref[0, 0], preferred_element_type=jnp.float32)
    prod_im = jnp.dot(lhs, w_ref[1, 0], preferred_element_type=jnp.float32)
    real_part = prod_re[:rows] - prod_im[rows:]
    imag_part = prod_im[:rows] + prod_re[rows:]
    power = real_part * real_part + imag_part * imag_part
    quarter = rows // 2
    power = power[:quarter] + power[quarter:]
    power = power.reshape(IB, TINT, U, power.shape[-1])
    power = (power[:, 0] + power[:, 1]).reshape(IB * U, power.shape[-1])
    detected = (power * (1.0 / (4.0 * TINT))).astype(jnp.bfloat16)
    picked = jnp.dot(detected, sel_ref[...], preferred_element_type=jnp.float32).astype(jnp.bfloat16)
    nodes = out_ref.shape[1]
    for n in range(nodes):
        out_ref[:, n] = picked[:, n * 128 : (n + 1) * 128].reshape(IB, U, 128)


def beamform(pieces, weights, select):
    nsrc, nb = len(pieces), pieces[0].shape[1]
    feeds, beams = weights.shape[2], weights.shape[3]
    slots = select.shape[1]
    nodes = slots // 128
    piece_spec = pl.BlockSpec((1, 1, 2, 2, IB, TINT, U, 128), lambda i: (0, i, 0, 0, 0, 0, 0, 0))
    return pl.pallas_call(
        _beam_kernel,
        grid=(nb,),
        in_specs=[piece_spec] * nsrc
        + [
            pl.BlockSpec((2, 1, feeds, beams), lambda i: (0, 0, 0, 0)),
            pl.BlockSpec((beams, slots), lambda i: (0, 0)),
        ],
        out_specs=pl.BlockSpec((IB, nodes, U, 128), lambda i: (i, 0, 0, 0)),
        out_shape=jax.ShapeDtypeStruct((nb * IB, nodes, U, 128), jnp.bfloat16),
        cost_estimate=pl.CostEstimate(
            flops=2 * 2 * (4 * nb * IB * U * TINT) * feeds * beams + 2 * nb * IB * U * beams * slots,
            bytes_accessed=sum(p.size for p in pieces) * 2 + weights.size * 2 + select.size * 2 + nb * IB * U * slots * 2,
            transcendentals=0,
        ),
        compiler_params=pltpu.CompilerParams(vmem_limit_bytes=60 * 1024 * 1024),
    )(*pieces, weights, select)


def on_device(voltages, history, gains, weights, beam_lists, beam_counts):
    capacity = beam_lists.shape[1]
    beams = weights.shape[3]
    flat_ids = beam_lists.reshape(-1)
    live_slots = (jnp.arange(capacity, dtype=jnp.int32)[None, :] < beam_counts[:, None]).reshape(-1)
    select = (
        (jnp.arange(beams, dtype=jnp.int32)[:, None] == flat_ids[None, :]) & live_slots[None, :]
    ).astype(jnp.bfloat16)
    band = jnp.asarray(band_matrix())
    nfeed = lax.axis_size("feed")
    me = lax.axis_index("feed")
    order = lax.rem(me - jnp.arange(nfeed, dtype=jnp.int32) + nfeed, nfeed)
    feeds_local = weights.shape[2] // nfeed
    wperm = jnp.take(weights.reshape(2, 1, nfeed, feeds_local, beams), order, axis=2).reshape(weights.shape)
    me_arr = me.astype(jnp.int32).reshape(1)
    outs = []
    for chunk in range(CHUNKS):
        calibrated = filterbank(me_arr, voltages, history, gains, band, chunk, CHUNKS)
        pieces = [calibrated[0:1]]
        for shift in range(1, nfeed):
            pairs = [(i, (i + shift) % nfeed) for i in range(nfeed)]
            pieces.append(lax.ppermute(calibrated[shift : shift + 1], "feed", perm=pairs))
        picked = beamform(pieces, wperm, select)
        outs.append(lax.all_to_all(picked, "chan", split_axis=1, concat_axis=1, tiled=True))
    exchanged = jnp.concatenate(outs, axis=0)
    bins, nodes, fine, width = exchanged.shape
    return exchanged.reshape(bins, nodes * fine, width)


def solution(mesh):
    in_specs = (
        P(None, None, "chan", None, "feed"),
        P(None, None, "chan", None, "feed"),
        P(None, None, "chan", "feed"),
        P(None, "chan", None, None),
        P(),
        P(),
    )
    out_specs = P("feed", None, "chan")
    return jax.shard_map(
        on_device, mesh=mesh, in_specs=in_specs, out_specs=out_specs, check_vma=False
    )
```

```python
import math

import numpy as np
import jax
import jax.numpy as jnp
from jax import lax
from jax.experimental import pallas as pl
from jax.experimental.pallas import tpu as pltpu
from jax.sharding import PartitionSpec as P

U = 16
TAPS = 4
TINT = 2
IB = 4
CHUNKS = 2
FRAMES = 2 * IB


def window_taps_np():
    length = TAPS * U
    positions = np.arange(length, dtype=np.float64)
    offsets = (positions - (length - 1) / 2.0) / U
    hann_taper = 0.5 - 0.5 * np.cos(2.0 * math.pi * (positions + 0.5) / length)
    taps_window = np.sinc(offsets) * hann_taper
    taps_window = taps_window / np.sqrt(np.sum(taps_window * taps_window) / U)
    return taps_window.astype(np.float32)


def band_matrix():
    taps = window_taps_np().astype(np.float64)
    span = (FRAMES + TAPS - 1) * U
    index_n = np.arange(U)
    phases = 2.0 * math.pi * ((index_n[:, None] * index_n[None, :]) % U) / U
    cosine = np.cos(phases) / math.sqrt(U)
    sine = np.sin(phases) / math.sqrt(U)
    table = np.array([[cosine, -sine], [sine, cosine]])
    band = np.zeros((2, FRAMES, U, 2, span))
    for t in range(FRAMES):
        for m in range(TAPS * U):
            for r in range(2):
                band[:, t, :, r, t * U + m] = taps[m] * table[r, :, m % U, :]
    band = band.reshape(2 * FRAMES * U, 2 * span).astype(np.float32)
    high = band.astype(jnp.bfloat16)
    low = (band - high.astype(np.float32)).astype(jnp.bfloat16)
    return np.concatenate([high, low], axis=0)


def _filter_kernel(chunk, main_ref, pre0_ref, pre1_ref, pre2_ref, hist_ref, gain_ref, band_ref, *rest):
    out_ref = rest[-1]
    tdev = pl.program_id(0)
    rows_main = main_ref.shape[4]
    nb = out_ref.shape[1]
    span = (FRAMES + TAPS - 1) * U
    half = FRAMES * U
    lanes = main_ref.shape[5]
    g_re = jnp.concatenate([gain_ref[0, p] for p in range(2)], axis=1)
    g_im = jnp.concatenate([gain_ref[1, p] for p in range(2)], axis=1)

    def rows_of(r, start, size):
        return jnp.concatenate([main_ref[r, p, 0, 0, pl.ds(start, size), :] for p in range(2)], axis=1)

    def prefix_of(r):
        pre = [jnp.concatenate([ref[r, p, 0, 0] for p in range(2)], axis=1) for ref in (pre0_ref, pre1_ref, pre2_ref)]
        pre = jnp.concatenate(pre, axis=0)
        if chunk == 0:
            hist = jnp.concatenate([hist_ref[r, p, 0] for p in range(2)], axis=1)
            pre = jnp.where(tdev == 0, hist, pre)
        return pre

    for ib in range(nb):
        parts = []
        for r in range(2):
            if ib == 0:
                parts.append(jnp.concatenate([prefix_of(r), rows_of(r, 0, span - 48)], axis=0))
            else:
                parts.append(rows_of(r, ib * half - 48, span))
        rhs = jnp.concatenate(parts, axis=0)
        both = jnp.dot(band_ref[...], rhs, preferred_element_type=jnp.float32)
        rows = both.shape[0] // 2
        spec = both[:rows] + both[rows:]
        s_re = spec[:half]
        s_im = spec[half:]
        c_re = (g_re * s_re - g_im * s_im).astype(jnp.bfloat16)
        c_im = (g_re * s_im + g_im * s_re).astype(jnp.bfloat16)
        for p in range(2):
            out_ref[0, ib, 0, p] = c_re[:, p * lanes : (p + 1) * lanes].reshape(IB, TINT, U, lanes)
            out_ref[0, ib, 1, p] = c_im[:, p * lanes : (p + 1) * lanes].reshape(IB, TINT, U, lanes)


def filterbank(voltages, history, gains, band, chunk, chunks, after=None):
    _, pols, _, samples, feeds = voltages.shape
    nblk = 8
    rows_blk = samples // nblk
    rows_main = rows_blk // chunks
    nb = rows_main // U // FRAMES
    main = voltages.reshape(2, pols, nblk, chunks, rows_main, feeds)
    units = voltages.reshape(2, pols, nblk, rows_blk // 16, 16, feeds)

    def pre_map(m):
        if chunk == 0:
            return lambda t: (0, 0, jnp.maximum(t - 1, 0), rows_blk // 16 - 3 + m, 0, 0)
        return lambda t: (0, 0, t, chunk * rows_main // 16 - 3 + m, 0, 0)

    extra = [] if after is None else [after]
    return pl.pallas_call(
        lambda *refs: _filter_kernel(chunk, *refs),
        grid=(nblk,),
        in_specs=[
            pl.BlockSpec((2, pols, 1, 1, rows_main, feeds), lambda t: (0, 0, t, chunk, 0, 0)),
            pl.BlockSpec((2, pols, 1, 1, 16, feeds), pre_map(0)),
            pl.BlockSpec((2, pols, 1, 1, 16, feeds), pre_map(1)),
            pl.BlockSpec((2, pols, 1, 1, 16, feeds), pre_map(2)),
            pl.BlockSpec((2, pols, 1, 48, feeds), lambda t: (0, 0, 0, 0, 0)),
            pl.BlockSpec((2, pols, 1, feeds), lambda t: (0, 0, 0, 0)),
            pl.BlockSpec(band.shape, lambda t: (0, 0)),
        ]
        + [pl.BlockSpec((1, 1, U, 128), lambda t: (0, 0, 0, 0)) for _ in extra],
        out_specs=pl.BlockSpec((1, nb, 2, pols, IB, TINT, U, feeds), lambda t: (t, 0, 0, 0, 0, 0, 0, 0)),
        out_shape=jax.ShapeDtypeStruct((nblk, nb, 2, pols, IB, TINT, U, feeds), jnp.bfloat16),
        cost_estimate=pl.CostEstimate(
            flops=2 * band.size * feeds * pols * nblk * nb,
            bytes_accessed=2 * voltages.size * 2 // chunks,
            transcendentals=0,
        ),
    )(main, units, units, units, history, gains, band, *extra)


def _beam_kernel(cal_ref, w_ref, sel_ref, out_ref):
    nsrc = cal_ref.shape[0]
    rows = 2 * 2 * IB * U
    halves = []
    for s in range(2):
        pieces = [cal_ref[d, 0, s].reshape(rows, 128) for d in range(nsrc)]
        halves.append(jnp.concatenate(pieces, axis=1))
    lhs = jnp.concatenate(halves, axis=0)
    prod_re = jnp.dot(lhs, w_ref[0, 0], preferred_element_type=jnp.float32)
    prod_im = jnp.dot(lhs, w_ref[1, 0], preferred_element_type=jnp.float32)
    real_part = prod_re[:rows] - prod_im[rows:]
    imag_part = prod_im[:rows] + prod_re[rows:]
    power = real_part * real_part + imag_part * imag_part
    quarter = rows // 2
    power = power[:quarter] + power[quarter:]
    power = power.reshape(IB, TINT, U, power.shape[-1])
    power = (power[:, 0] + power[:, 1]).reshape(IB * U, power.shape[-1])
    detected = (power * (1.0 / (4.0 * TINT))).astype(jnp.bfloat16)
    picked = jnp.dot(detected, sel_ref[...], preferred_element_type=jnp.float32).astype(jnp.bfloat16)
    nodes = out_ref.shape[1]
    for n in range(nodes):
        out_ref[:, n] = picked[:, n * 128 : (n + 1) * 128].reshape(IB, U, 128)


def beamform(cal, weights, select):
    nsrc, nb = cal.shape[0], cal.shape[1]
    feeds, beams = weights.shape[2], weights.shape[3]
    slots = select.shape[1]
    nodes = slots // 128
    return pl.pallas_call(
        _beam_kernel,
        grid=(nb,),
        in_specs=[
            pl.BlockSpec((nsrc, 1, 2, 2, IB, TINT, U, 128), lambda i: (0, i, 0, 0, 0, 0, 0, 0)),
            pl.BlockSpec((2, 1, feeds, beams), lambda i: (0, 0, 0, 0)),
            pl.BlockSpec((beams, slots), lambda i: (0, 0)),
        ],
        out_specs=pl.BlockSpec((IB, nodes, U, 128), lambda i: (i, 0, 0, 0)),
        out_shape=jax.ShapeDtypeStruct((nb * IB, nodes, U, 128), jnp.bfloat16),
        cost_estimate=pl.CostEstimate(
            flops=2 * 2 * (4 * nb * IB * U * TINT) * feeds * beams + 2 * nb * IB * U * beams * slots,
            bytes_accessed=cal.size * 2 + weights.size * 2 + select.size * 2 + nb * IB * U * slots * 2,
            transcendentals=0,
        ),
        compiler_params=pltpu.CompilerParams(vmem_limit_bytes=60 * 1024 * 1024),
    )(cal, weights, select)


def on_device(voltages, history, gains, weights, beam_lists, beam_counts):
    capacity = beam_lists.shape[1]
    beams = weights.shape[3]
    flat_ids = beam_lists.reshape(-1)
    live_slots = (jnp.arange(capacity, dtype=jnp.int32)[None, :] < beam_counts[:, None]).reshape(-1)
    select = (
        (jnp.arange(beams, dtype=jnp.int32)[:, None] == flat_ids[None, :]) & live_slots[None, :]
    ).astype(jnp.bfloat16)
    band = jnp.asarray(band_matrix())
    gathered = []
    outs = []
    for chunk in range(CHUNKS + 1):
        if chunk < CHUNKS:
            after = outs[-1] if outs else None
            calibrated = filterbank(voltages, history, gains, band, chunk, CHUNKS, after)
            gathered.append(lax.all_to_all(calibrated, "feed", split_axis=0, concat_axis=0, tiled=True))
        if chunk >= 1:
            picked = beamform(gathered[chunk - 1], weights, select)
            outs.append(lax.all_to_all(picked, "chan", split_axis=1, concat_axis=1, tiled=True))
    exchanged = jnp.concatenate(outs, axis=0)
    bins, nodes, fine, width = exchanged.shape
    return exchanged.reshape(bins, nodes * fine, width)


def solution(mesh):
    in_specs = (
        P(None, None, "chan", None, "feed"),
        P(None, None, "chan", None, "feed"),
        P(None, None, "chan", "feed"),
        P(None, "chan", None, None),
        P(),
        P(),
    )
    out_specs = P("feed", None, "chan")
    return jax.shard_map(
        on_device, mesh=mesh, in_specs=in_specs, out_specs=out_specs, check_vma=False
    )
```

```python
import math

import numpy as np
import jax
import jax.numpy as jnp
from jax import lax
from jax.experimental import pallas as pl
from jax.experimental.pallas import tpu as pltpu
from jax.sharding import PartitionSpec as P

U = 16
TAPS = 4
TINT = 2
IB = 4
CHUNKS = 2
FRAMES = 2 * IB


def window_taps_np():
    length = TAPS * U
    positions = np.arange(length, dtype=np.float64)
    offsets = (positions - (length - 1) / 2.0) / U
    hann_taper = 0.5 - 0.5 * np.cos(2.0 * math.pi * (positions + 0.5) / length)
    taps_window = np.sinc(offsets) * hann_taper
    taps_window = taps_window / np.sqrt(np.sum(taps_window * taps_window) / U)
    return taps_window.astype(np.float32)


def band_matrix():
    taps = window_taps_np().astype(np.float64)
    span = (FRAMES + TAPS - 1) * U
    index_n = np.arange(U)
    phases = 2.0 * math.pi * ((index_n[:, None] * index_n[None, :]) % U) / U
    cosine = np.cos(phases) / math.sqrt(U)
    sine = np.sin(phases) / math.sqrt(U)
    table = np.array([[cosine, -sine], [sine, cosine]])
    band = np.zeros((2, FRAMES, U, 2, span))
    for t in range(FRAMES):
        for m in range(TAPS * U):
            for r in range(2):
                band[:, t, :, r, t * U + m] = taps[m] * table[r, :, m % U, :]
    band = band.reshape(2 * FRAMES * U, 2 * span).astype(np.float32)
    high = band.astype(jnp.bfloat16)
    low = (band - high.astype(np.float32)).astype(jnp.bfloat16)
    return np.concatenate([high, low], axis=0)


def _filter_kernel(chunk, main_ref, pre0_ref, pre1_ref, pre2_ref, hist_ref, gain_ref, band_ref, *rest):
    out_ref = rest[-1]
    tdev = pl.program_id(0)
    rows_main = main_ref.shape[4]
    nb = out_ref.shape[1]
    span = (FRAMES + TAPS - 1) * U
    half = FRAMES * U
    lanes = main_ref.shape[5]
    g_re = jnp.concatenate([gain_ref[0, p] for p in range(2)], axis=1)
    g_im = jnp.concatenate([gain_ref[1, p] for p in range(2)], axis=1)

    def rows_of(r, start, size):
        return jnp.concatenate([main_ref[r, p, 0, 0, pl.ds(start, size), :] for p in range(2)], axis=1)

    def prefix_of(r):
        pre = [jnp.concatenate([ref[r, p, 0, 0] for p in range(2)], axis=1) for ref in (pre0_ref, pre1_ref, pre2_ref)]
        pre = jnp.concatenate(pre, axis=0)
        if chunk == 0:
            hist = jnp.concatenate([hist_ref[r, p, 0] for p in range(2)], axis=1)
            pre = jnp.where(tdev == 0, hist, pre)
        return pre

    for ib in range(nb):
        parts = []
        for r in range(2):
            if ib == 0:
                parts.append(jnp.concatenate([prefix_of(r), rows_of(r, 0, span - 48)], axis=0))
            else:
                parts.append(rows_of(r, ib * half - 48, span))
        rhs = jnp.concatenate(parts, axis=0)
        both = jnp.dot(band_ref[...], rhs, preferred_element_type=jnp.float32)
        rows = both.shape[0] // 2
        spec = both[:rows] + both[rows:]
        s_re = spec[:half]
        s_im = spec[half:]
        c_re = (g_re * s_re - g_im * s_im).astype(jnp.bfloat16)
        c_im = (g_re * s_im + g_im * s_re).astype(jnp.bfloat16)
        for p in range(2):
            out_ref[0, ib, 0, p] = c_re[:, p * lanes : (p + 1) * lanes].reshape(IB, TINT, U, lanes)
            out_ref[0, ib, 1, p] = c_im[:, p * lanes : (p + 1) * lanes].reshape(IB, TINT, U, lanes)


def filterbank(voltages, history, gains, band, chunk, chunks, after=None):
    _, pols, _, samples, feeds = voltages.shape
    nblk = 8
    rows_blk = samples // nblk
    rows_main = rows_blk // chunks
    nb = rows_main // U // FRAMES
    main = voltages.reshape(2, pols, nblk, chunks, rows_main, feeds)
    units = voltages.reshape(2, pols, nblk, rows_blk // 16, 16, feeds)

    def pre_map(m):
        if chunk == 0:
            return lambda t: (0, 0, jnp.maximum(t - 1, 0), rows_blk // 16 - 3 + m, 0, 0)
        return lambda t: (0, 0, t, chunk * rows_main // 16 - 3 + m, 0, 0)

    extra = [] if after is None else [after]
    return pl.pallas_call(
        lambda *refs: _filter_kernel(chunk, *refs),
        grid=(nblk,),
        in_specs=[
            pl.BlockSpec((2, pols, 1, 1, rows_main, feeds), lambda t: (0, 0, t, chunk, 0, 0)),
            pl.BlockSpec((2, pols, 1, 1, 16, feeds), pre_map(0)),
            pl.BlockSpec((2, pols, 1, 1, 16, feeds), pre_map(1)),
            pl.BlockSpec((2, pols, 1, 1, 16, feeds), pre_map(2)),
            pl.BlockSpec((2, pols, 1, 48, feeds), lambda t: (0, 0, 0, 0, 0)),
            pl.BlockSpec((2, pols, 1, feeds), lambda t: (0, 0, 0, 0)),
            pl.BlockSpec(band.shape, lambda t: (0, 0)),
        ]
        + [pl.BlockSpec((1, 1, U, 128), lambda t: (0, 0, 0, 0)) for _ in extra],
        out_specs=pl.BlockSpec((1, nb, 2, pols, IB, TINT, U, feeds), lambda t: (t, 0, 0, 0, 0, 0, 0, 0)),
        out_shape=jax.ShapeDtypeStruct((nblk, nb, 2, pols, IB, TINT, U, feeds), jnp.bfloat16),
        cost_estimate=pl.CostEstimate(
            flops=2 * band.size * feeds * pols * nblk * nb,
            bytes_accessed=2 * voltages.size * 2 // chunks,
            transcendentals=0,
        ),
    )(main, units, units, units, history, gains, band, *extra)


def _beam_kernel(cal_ref, w_ref, sel_ref, out_ref):
    nsrc = cal_ref.shape[0]
    rows = 2 * 2 * IB * U
    halves = []
    for s in range(2):
        pieces = [cal_ref[d, 0, s].reshape(rows, 128) for d in range(nsrc)]
        halves.append(jnp.concatenate(pieces, axis=1))
    lhs = jnp.concatenate(halves, axis=0)
    prod_re = jnp.dot(lhs, w_ref[0, 0], preferred_element_type=jnp.float32)
    prod_im = jnp.dot(lhs, w_ref[1, 0], preferred_element_type=jnp.float32)
    real_part = prod_re[:rows] - prod_im[rows:]
    imag_part = prod_im[:rows] + prod_re[rows:]
    power = real_part * real_part + imag_part * imag_part
    quarter = rows // 2
    power = power[:quarter] + power[quarter:]
    power = power.reshape(IB, TINT, U, power.shape[-1])
    power = (power[:, 0] + power[:, 1]).reshape(IB * U, power.shape[-1])
    detected = (power * (1.0 / (4.0 * TINT))).astype(jnp.bfloat16)
    picked = jnp.dot(detected, sel_ref[...], preferred_element_type=jnp.float32).astype(jnp.bfloat16)
    nodes = out_ref.shape[0]
    for n in range(nodes):
        out_ref[n] = picked[:, n * 128 : (n + 1) * 128].reshape(IB, U, 128)


def beamform(cal, weights, select):
    nsrc, nb = cal.shape[0], cal.shape[1]
    feeds, beams = weights.shape[2], weights.shape[3]
    slots = select.shape[1]
    nodes = slots // 128
    return pl.pallas_call(
        _beam_kernel,
        grid=(nb,),
        in_specs=[
            pl.BlockSpec((nsrc, 1, 2, 2, IB, TINT, U, 128), lambda i: (0, i, 0, 0, 0, 0, 0, 0)),
            pl.BlockSpec((2, 1, feeds, beams), lambda i: (0, 0, 0, 0)),
            pl.BlockSpec((beams, slots), lambda i: (0, 0)),
        ],
        out_specs=pl.BlockSpec((nodes, IB, U, 128), lambda i: (0, i, 0, 0)),
        out_shape=jax.ShapeDtypeStruct((nodes, nb * IB, U, 128), jnp.bfloat16),
        cost_estimate=pl.CostEstimate(
            flops=2 * 2 * (4 * nb * IB * U * TINT) * feeds * beams + 2 * nb * IB * U * beams * slots,
            bytes_accessed=cal.size * 2 + weights.size * 2 + select.size * 2 + nb * IB * U * slots * 2,
            transcendentals=0,
        ),
        compiler_params=pltpu.CompilerParams(vmem_limit_bytes=60 * 1024 * 1024),
    )(cal, weights, select)


def on_device(voltages, history, gains, weights, beam_lists, beam_counts):
    capacity = beam_lists.shape[1]
    beams = weights.shape[3]
    flat_ids = beam_lists.reshape(-1)
    live_slots = (jnp.arange(capacity, dtype=jnp.int32)[None, :] < beam_counts[:, None]).reshape(-1)
    select = (
        (jnp.arange(beams, dtype=jnp.int32)[:, None] == flat_ids[None, :]) & live_slots[None, :]
    ).astype(jnp.bfloat16)
    band = jnp.asarray(band_matrix())
    gathered = []
    outs = []
    for chunk in range(CHUNKS + 1):
        if chunk < CHUNKS:
            after = outs[-1] if outs else None
            calibrated = filterbank(voltages, history, gains, band, chunk, CHUNKS, after)
            gathered.append(lax.all_to_all(calibrated, "feed", split_axis=0, concat_axis=0, tiled=True))
        if chunk >= 1:
            picked = beamform(gathered[chunk - 1], weights, select)
            outs.append(lax.all_to_all(picked, "chan", split_axis=0, concat_axis=0, tiled=True))
    exchanged = jnp.concatenate(outs, axis=1)
    nodes, bins, fine, width = exchanged.shape
    return jnp.transpose(exchanged, (1, 0, 2, 3)).reshape(bins, nodes * fine, width)


def solution(mesh):
    in_specs = (
        P(None, None, "chan", None, "feed"),
        P(None, None, "chan", None, "feed"),
        P(None, None, "chan", "feed"),
        P(None, "chan", None, None),
        P(),
        P(),
    )
    out_specs = P("feed", None, "chan")
    return jax.shard_map(
        on_device, mesh=mesh, in_specs=in_specs, out_specs=out_specs, check_vma=False
    )
```

```python
import math

import numpy as np
import jax
import jax.numpy as jnp
from jax import lax
from jax.experimental import pallas as pl
from jax.experimental.pallas import tpu as pltpu
from jax.sharding import PartitionSpec as P

U = 16
TAPS = 4
TINT = 2
IB = 4
CHUNK_BLOCKS = (6, 2)
FRAMES = 2 * IB


def window_taps_np():
    length = TAPS * U
    positions = np.arange(length, dtype=np.float64)
    offsets = (positions - (length - 1) / 2.0) / U
    hann_taper = 0.5 - 0.5 * np.cos(2.0 * math.pi * (positions + 0.5) / length)
    taps_window = np.sinc(offsets) * hann_taper
    taps_window = taps_window / np.sqrt(np.sum(taps_window * taps_window) / U)
    return taps_window.astype(np.float32)


def band_matrix():
    taps = window_taps_np().astype(np.float64)
    span = (FRAMES + TAPS - 1) * U
    index_n = np.arange(U)
    phases = 2.0 * math.pi * ((index_n[:, None] * index_n[None, :]) % U) / U
    cosine = np.cos(phases) / math.sqrt(U)
    sine = np.sin(phases) / math.sqrt(U)
    table = np.array([[cosine, -sine], [sine, cosine]])
    band = np.zeros((2, FRAMES, U, 2, span))
    for t in range(FRAMES):
        for m in range(TAPS * U):
            for r in range(2):
                band[:, t, :, r, t * U + m] = taps[m] * table[r, :, m % U, :]
    band = band.reshape(2 * FRAMES * U, 2 * span).astype(np.float32)
    high = band.astype(jnp.bfloat16)
    low = (band - high.astype(np.float32)).astype(jnp.bfloat16)
    return np.concatenate([high, low], axis=0)


def _filter_kernel(chunk, main_ref, pre0_ref, pre1_ref, pre2_ref, hist_ref, gain_ref, band_ref, *rest):
    out_ref = rest[-1]
    tdev = pl.program_id(0)
    nb = out_ref.shape[1]
    span = (FRAMES + TAPS - 1) * U
    half = FRAMES * U
    lanes = main_ref.shape[4]
    g_re = jnp.concatenate([gain_ref[0, p] for p in range(2)], axis=1)
    g_im = jnp.concatenate([gain_ref[1, p] for p in range(2)], axis=1)

    def rows_of(r, start, size):
        return jnp.concatenate([main_ref[r, p, 0, pl.ds(start, size), :] for p in range(2)], axis=1)

    def prefix_of(r):
        pre = [jnp.concatenate([ref[r, p, 0, 0] for p in range(2)], axis=1) for ref in (pre0_ref, pre1_ref, pre2_ref)]
        pre = jnp.concatenate(pre, axis=0)
        if chunk == 0:
            hist = jnp.concatenate([hist_ref[r, p, 0] for p in range(2)], axis=1)
            pre = jnp.where(tdev == 0, hist, pre)
        return pre

    for ib in range(nb):
        parts = []
        for r in range(2):
            if ib == 0:
                parts.append(jnp.concatenate([prefix_of(r), rows_of(r, 0, span - 48)], axis=0))
            else:
                parts.append(rows_of(r, ib * half - 48, span))
        rhs = jnp.concatenate(parts, axis=0)
        both = jnp.dot(band_ref[...], rhs, preferred_element_type=jnp.float32)
        rows = both.shape[0] // 2
        spec = both[:rows] + both[rows:]
        s_re = spec[:half]
        s_im = spec[half:]
        c_re = (g_re * s_re - g_im * s_im).astype(jnp.bfloat16)
        c_im = (g_re * s_im + g_im * s_re).astype(jnp.bfloat16)
        for p in range(2):
            out_ref[0, ib, 0, p] = c_re[:, p * lanes : (p + 1) * lanes].reshape(IB, TINT, U, lanes)
            out_ref[0, ib, 1, p] = c_im[:, p * lanes : (p + 1) * lanes].reshape(IB, TINT, U, lanes)


def filterbank(voltages, history, gains, band, first_blk, nb, after=None):
    _, pols, _, samples, feeds = voltages.shape
    nblk = 8
    rows_blk = samples // nblk
    rows_main = nb * FRAMES * U
    assert (first_blk * FRAMES * U) % rows_main == 0
    chunk = first_blk * FRAMES * U // rows_main
    main = voltages.reshape(2, pols, nblk, rows_blk, feeds)
    units = voltages.reshape(2, pols, nblk, rows_blk // 16, 16, feeds)

    def pre_map(m):
        if first_blk == 0:
            return lambda t: (0, 0, jnp.maximum(t - 1, 0), rows_blk // 16 - 3 + m, 0, 0)
        return lambda t: (0, 0, t, first_blk * FRAMES - 3 + m, 0, 0)

    extra = [] if after is None else [after]
    return pl.pallas_call(
        lambda *refs: _filter_kernel(first_blk, *refs),
        grid=(nblk,),
        in_specs=[
            pl.BlockSpec((2, pols, 1, rows_main, feeds), lambda t: (0, 0, t, chunk, 0)),
            pl.BlockSpec((2, pols, 1, 1, 16, feeds), pre_map(0)),
            pl.BlockSpec((2, pols, 1, 1, 16, feeds), pre_map(1)),
            pl.BlockSpec((2, pols, 1, 1, 16, feeds), pre_map(2)),
            pl.BlockSpec((2, pols, 1, 48, feeds), lambda t: (0, 0, 0, 0, 0)),
            pl.BlockSpec((2, pols, 1, feeds), lambda t: (0, 0, 0, 0)),
            pl.BlockSpec(band.shape, lambda t: (0, 0)),
        ]
        + [pl.BlockSpec((1, 1, U, 128), lambda t: (0, 0, 0, 0)) for _ in extra],
        out_specs=pl.BlockSpec((1, nb, 2, pols, IB, TINT, U, feeds), lambda t: (t, 0, 0, 0, 0, 0, 0, 0)),
        out_shape=jax.ShapeDtypeStruct((nblk, nb, 2, pols, IB, TINT, U, feeds), jnp.bfloat16),
        cost_estimate=pl.CostEstimate(
            flops=2 * band.size * feeds * pols * nblk * nb,
            bytes_accessed=2 * voltages.size * 2 * nb // (rows_blk // (FRAMES * U)),
            transcendentals=0,
        ),
    )(main, units, units, units, history, gains, band, *extra)


def _beam_kernel(cal_ref, w_ref, sel_ref, *rest):
    out_ref = rest[-1]
    nsrc = cal_ref.shape[0]
    rows = 2 * 2 * IB * U
    halves = []
    for s in range(2):
        pieces = [cal_ref[d, 0, s].reshape(rows, 128) for d in range(nsrc)]
        halves.append(jnp.concatenate(pieces, axis=1))
    lhs = jnp.concatenate(halves, axis=0)
    prod_re = jnp.dot(lhs, w_ref[0, 0], preferred_element_type=jnp.float32)
    prod_im = jnp.dot(lhs, w_ref[1, 0], preferred_element_type=jnp.float32)
    real_part = prod_re[:rows] - prod_im[rows:]
    imag_part = prod_im[:rows] + prod_re[rows:]
    power = real_part * real_part + imag_part * imag_part
    quarter = rows // 2
    power = power[:quarter] + power[quarter:]
    power = power.reshape(IB, TINT, U, power.shape[-1])
    power = (power[:, 0] + power[:, 1]).reshape(IB * U, power.shape[-1])
    detected = (power * (1.0 / (4.0 * TINT))).astype(jnp.bfloat16)
    picked = jnp.dot(detected, sel_ref[...], preferred_element_type=jnp.float32).astype(jnp.bfloat16)
    nodes = out_ref.shape[0]
    for n in range(nodes):
        out_ref[n] = picked[:, n * 128 : (n + 1) * 128].reshape(IB, U, 128)


def beamform(cal, weights, select, after=None):
    extra = [] if after is None else [after]
    nsrc, nb = cal.shape[0], cal.shape[1]
    feeds, beams = weights.shape[2], weights.shape[3]
    slots = select.shape[1]
    nodes = slots // 128
    return pl.pallas_call(
        _beam_kernel,
        grid=(nb,),
        in_specs=[
            pl.BlockSpec((nsrc, 1, 2, 2, IB, TINT, U, 128), lambda i: (0, i, 0, 0, 0, 0, 0, 0)),
            pl.BlockSpec((2, 1, feeds, beams), lambda i: (0, 0, 0, 0)),
            pl.BlockSpec((beams, slots), lambda i: (0, 0)),
        ]
        + [pl.BlockSpec((1, 1, U, 128), lambda i: (0, 0, 0, 0)) for _ in extra],
        out_specs=pl.BlockSpec((nodes, IB, U, 128), lambda i: (0, i, 0, 0)),
        out_shape=jax.ShapeDtypeStruct((nodes, nb * IB, U, 128), jnp.bfloat16),
        cost_estimate=pl.CostEstimate(
            flops=2 * 2 * (4 * nb * IB * U * TINT) * feeds * beams + 2 * nb * IB * U * beams * slots,
            bytes_accessed=cal.size * 2 + weights.size * 2 + select.size * 2 + nb * IB * U * slots * 2,
            transcendentals=0,
        ),
        compiler_params=pltpu.CompilerParams(vmem_limit_bytes=60 * 1024 * 1024),
    )(cal, weights, select, *extra)


def on_device(voltages, history, gains, weights, beam_lists, beam_counts):
    capacity = beam_lists.shape[1]
    beams = weights.shape[3]
    flat_ids = beam_lists.reshape(-1)
    live_slots = (jnp.arange(capacity, dtype=jnp.int32)[None, :] < beam_counts[:, None]).reshape(-1)
    select = (
        (jnp.arange(beams, dtype=jnp.int32)[:, None] == flat_ids[None, :]) & live_slots[None, :]
    ).astype(jnp.bfloat16)
    band = jnp.asarray(band_matrix())
    starts = [sum(CHUNK_BLOCKS[:c]) for c in range(len(CHUNK_BLOCKS))]
    gathered = []
    calibrated = []
    outs = []
    for chunk in range(len(CHUNK_BLOCKS)):
        after = None if chunk == 0 else gathered[-1].reshape(-1, 1, U, 128)
        calibrated.append(filterbank(voltages, history, gains, band, starts[chunk], CHUNK_BLOCKS[chunk], after))
        gathered.append(lax.all_to_all(calibrated[-1], "feed", split_axis=0, concat_axis=0, tiled=True))
    for chunk in range(len(CHUNK_BLOCKS)):
        after = calibrated[chunk + 1].reshape(-1, 1, U, 128) if chunk + 1 < len(CHUNK_BLOCKS) else None
        picked = beamform(gathered[chunk], weights, select, after)
        outs.append(lax.all_to_all(picked, "chan", split_axis=0, concat_axis=0, tiled=True))
    exchanged = jnp.concatenate(outs, axis=1)
    nodes, bins, fine, width = exchanged.shape
    return jnp.transpose(exchanged, (1, 0, 2, 3)).reshape(bins, nodes * fine, width)


def solution(mesh):
    in_specs = (
        P(None, None, "chan", None, "feed"),
        P(None, None, "chan", None, "feed"),
        P(None, None, "chan", "feed"),
        P(None, "chan", None, None),
        P(),
        P(),
    )
    out_specs = P("feed", None, "chan")
    return jax.shard_map(
        on_device, mesh=mesh, in_specs=in_specs, out_specs=out_specs, check_vma=False
    )
```

```python
import math

import numpy as np
import jax
import jax.numpy as jnp
from jax import lax
from jax.experimental import pallas as pl
from jax.experimental.pallas import tpu as pltpu
from jax.sharding import PartitionSpec as P

U = 16
TAPS = 4
TINT = 2
IB = 4
CHUNKS = 2
FRAMES = 2 * IB


def window_taps_np():
    length = TAPS * U
    positions = np.arange(length, dtype=np.float64)
    offsets = (positions - (length - 1) / 2.0) / U
    hann_taper = 0.5 - 0.5 * np.cos(2.0 * math.pi * (positions + 0.5) / length)
    taps_window = np.sinc(offsets) * hann_taper
    taps_window = taps_window / np.sqrt(np.sum(taps_window * taps_window) / U)
    return taps_window.astype(np.float32)


def band_matrix():
    taps = window_taps_np().astype(np.float64)
    span = (FRAMES + TAPS - 1) * U
    index_n = np.arange(U)
    phases = 2.0 * math.pi * ((index_n[:, None] * index_n[None, :]) % U) / U
    cosine = np.cos(phases) / math.sqrt(U)
    sine = np.sin(phases) / math.sqrt(U)
    table = np.array([[cosine, -sine], [sine, cosine]])
    band = np.zeros((2, FRAMES, U, 2, span))
    for t in range(FRAMES):
        for m in range(TAPS * U):
            for r in range(2):
                band[:, t, :, r, t * U + m] = taps[m] * table[r, :, m % U, :]
    band = band.reshape(2 * FRAMES * U, 2 * span).astype(np.float32)
    high = band.astype(jnp.bfloat16)
    low = (band - high.astype(np.float32)).astype(jnp.bfloat16)
    return np.concatenate([high, low], axis=0)


def _filter_kernel(chunk, main_ref, pre0_ref, pre1_ref, pre2_ref, hist_ref, gain_ref, band_ref, *rest):
    out_ref = rest[-1]
    tdev = pl.program_id(0)
    rows_main = main_ref.shape[4]
    nb = out_ref.shape[1]
    span = (FRAMES + TAPS - 1) * U
    half = FRAMES * U
    lanes = main_ref.shape[5]
    g_re = jnp.concatenate([gain_ref[0, p] for p in range(2)], axis=1)
    g_im = jnp.concatenate([gain_ref[1, p] for p in range(2)], axis=1)

    def rows_of(r, start, size):
        return jnp.concatenate([main_ref[r, p, 0, 0, pl.ds(start, size), :] for p in range(2)], axis=1)

    def prefix_of(r):
        pre = [jnp.concatenate([ref[r, p, 0, 0] for p in range(2)], axis=1) for ref in (pre0_ref, pre1_ref, pre2_ref)]
        pre = jnp.concatenate(pre, axis=0)
        if chunk == 0:
            hist = jnp.concatenate([hist_ref[r, p, 0] for p in range(2)], axis=1)
            pre = jnp.where(tdev == 0, hist, pre)
        return pre

    for ib in range(nb):
        parts = []
        for r in range(2):
            if ib == 0:
                parts.append(jnp.concatenate([prefix_of(r), rows_of(r, 0, span - 48)], axis=0))
            else:
                parts.append(rows_of(r, ib * half - 48, span))
        rhs = jnp.concatenate(parts, axis=0)
        both = jnp.dot(band_ref[...], rhs, preferred_element_type=jnp.float32)
        rows = both.shape[0] // 2
        spec = both[:rows] + both[rows:]
        s_re = spec[:half]
        s_im = spec[half:]
        c_re = (g_re * s_re - g_im * s_im).astype(jnp.bfloat16)
        c_im = (g_re * s_im + g_im * s_re).astype(jnp.bfloat16)
        for p in range(2):
            out_ref[0, ib, 0, p] = c_re[:, p * lanes : (p + 1) * lanes].reshape(IB, TINT, U, lanes)
            out_ref[0, ib, 1, p] = c_im[:, p * lanes : (p + 1) * lanes].reshape(IB, TINT, U, lanes)


def filterbank(voltages, history, gains, band, chunk, chunks, after=None):
    _, pols, _, samples, feeds = voltages.shape
    nblk = 8
    rows_blk = samples // nblk
    rows_main = rows_blk // chunks
    nb = rows_main // U // FRAMES
    main = voltages.reshape(2, pols, nblk, chunks, rows_main, feeds)
    units = voltages.reshape(2, pols, nblk, rows_blk // 16, 16, feeds)

    def pre_map(m):
        if chunk == 0:
            return lambda t: (0, 0, jnp.maximum(t - 1, 0), rows_blk // 16 - 3 + m, 0, 0)
        return lambda t: (0, 0, t, chunk * rows_main // 16 - 3 + m, 0, 0)

    extra = [] if after is None else [after]
    return pl.pallas_call(
        lambda *refs: _filter_kernel(chunk, *refs),
        grid=(nblk,),
        in_specs=[
            pl.BlockSpec((2, pols, 1, 1, rows_main, feeds), lambda t: (0, 0, t, chunk, 0, 0)),
            pl.BlockSpec((2, pols, 1, 1, 16, feeds), pre_map(0)),
            pl.BlockSpec((2, pols, 1, 1, 16, feeds), pre_map(1)),
            pl.BlockSpec((2, pols, 1, 1, 16, feeds), pre_map(2)),
            pl.BlockSpec((2, pols, 1, 48, feeds), lambda t: (0, 0, 0, 0, 0)),
            pl.BlockSpec((2, pols, 1, feeds), lambda t: (0, 0, 0, 0)),
            pl.BlockSpec(band.shape, lambda t: (0, 0)),
        ]
        + [pl.BlockSpec((1, 1, U, 128), lambda t: (0, 0, 0, 0)) for _ in extra],
        out_specs=pl.BlockSpec((1, nb, 2, pols, IB, TINT, U, feeds), lambda t: (t, 0, 0, 0, 0, 0, 0, 0)),
        out_shape=jax.ShapeDtypeStruct((nblk, nb, 2, pols, IB, TINT, U, feeds), jnp.bfloat16),
        cost_estimate=pl.CostEstimate(
            flops=2 * band.size * feeds * pols * nblk * nb,
            bytes_accessed=2 * voltages.size * 2 // chunks,
            transcendentals=0,
        ),
    )(main, units, units, units, history, gains, band, *extra)


def _beam_kernel(cal_ref, w_ref, sel_ref, out_ref):
    nsrc = cal_ref.shape[0]
    rows = 2 * 2 * IB * U
    halves = []
    for s in range(2):
        pieces = [cal_ref[d, 0, s].reshape(rows, 128) for d in range(nsrc)]
        halves.append(jnp.concatenate(pieces, axis=1))
    lhs = jnp.concatenate(halves, axis=0)
    prod_re = jnp.dot(lhs, w_ref[0, 0], preferred_element_type=jnp.float32)
    prod_im = jnp.dot(lhs, w_ref[1, 0], preferred_element_type=jnp.float32)
    real_part = prod_re[:rows] - prod_im[rows:]
    imag_part = prod_im[:rows] + prod_re[rows:]
    power = real_part * real_part + imag_part * imag_part
    quarter = rows // 2
    power = power[:quarter] + power[quarter:]
    power = power.reshape(IB, TINT, U, power.shape[-1])
    power = (power[:, 0] + power[:, 1]).reshape(IB * U, power.shape[-1])
    detected = (power * (1.0 / (4.0 * TINT))).astype(jnp.bfloat16)
    picked = jnp.dot(detected, sel_ref[...], preferred_element_type=jnp.float32).astype(jnp.bfloat16)
    nodes = out_ref.shape[0]
    for n in range(nodes):
        out_ref[n] = picked[:, n * 128 : (n + 1) * 128].reshape(IB, U, 128)


def beamform(cal, weights, select):
    nsrc, nb = cal.shape[0], cal.shape[1]
    feeds, beams = weights.shape[2], weights.shape[3]
    slots = select.shape[1]
    nodes = slots // 128
    return pl.pallas_call(
        _beam_kernel,
        grid=(nb,),
        in_specs=[
            pl.BlockSpec((nsrc, 1, 2, 2, IB, TINT, U, 128), lambda i: (0, i, 0, 0, 0, 0, 0, 0)),
            pl.BlockSpec((2, 1, feeds, beams), lambda i: (0, 0, 0, 0)),
            pl.BlockSpec((beams, slots), lambda i: (0, 0)),
        ],
        out_specs=pl.BlockSpec((nodes, IB, U, 128), lambda i: (0, i, 0, 0)),
        out_shape=jax.ShapeDtypeStruct((nodes, nb * IB, U, 128), jnp.bfloat16),
        cost_estimate=pl.CostEstimate(
            flops=2 * 2 * (4 * nb * IB * U * TINT) * feeds * beams + 2 * nb * IB * U * beams * slots,
            bytes_accessed=cal.size * 2 + weights.size * 2 + select.size * 2 + nb * IB * U * slots * 2,
            transcendentals=0,
        ),
        compiler_params=pltpu.CompilerParams(vmem_limit_bytes=60 * 1024 * 1024),
    )(cal, weights, select)


def exchange_by_permutes(blocks, axis):
    count = lax.axis_size(axis)
    me = lax.axis_index(axis)
    received = [lax.dynamic_index_in_dim(blocks, me, axis=0, keepdims=False)]
    for shift in range(1, count):
        pairs = [(i, (i + shift) % count) for i in range(count)]
        piece = lax.dynamic_index_in_dim(blocks, lax.rem(me + shift, count), axis=0, keepdims=False)
        received.append(lax.ppermute(piece, axis, perm=pairs))
    stacked = jnp.stack(received)
    order = lax.rem(me - jnp.arange(count, dtype=jnp.int32) + count, count)
    return jnp.take(stacked, order, axis=0)


def on_device(voltages, history, gains, weights, beam_lists, beam_counts):
    capacity = beam_lists.shape[1]
    beams = weights.shape[3]
    flat_ids = beam_lists.reshape(-1)
    live_slots = (jnp.arange(capacity, dtype=jnp.int32)[None, :] < beam_counts[:, None]).reshape(-1)
    select = (
        (jnp.arange(beams, dtype=jnp.int32)[:, None] == flat_ids[None, :]) & live_slots[None, :]
    ).astype(jnp.bfloat16)
    band = jnp.asarray(band_matrix())
    gathered = []
    outs = []
    for chunk in range(CHUNKS + 1):
        if chunk < CHUNKS:
            after = outs[-1] if outs else None
            calibrated = filterbank(voltages, history, gains, band, chunk, CHUNKS, after)
            gathered.append(lax.all_to_all(calibrated, "feed", split_axis=0, concat_axis=0, tiled=True))
        if chunk >= 1:
            picked = beamform(gathered[chunk - 1], weights, select)
            if chunk < CHUNKS:
                outs.append(exchange_by_permutes(picked, "chan"))
            else:
                outs.append(lax.all_to_all(picked, "chan", split_axis=0, concat_axis=0, tiled=True))
    exchanged = jnp.concatenate(outs, axis=1)
    nodes, bins, fine, width = exchanged.shape
    return jnp.transpose(exchanged, (1, 0, 2, 3)).reshape(bins, nodes * fine, width)


def solution(mesh):
    in_specs = (
        P(None, None, "chan", None, "feed"),
        P(None, None, "chan", None, "feed"),
        P(None, None, "chan", "feed"),
        P(None, "chan", None, None),
        P(),
        P(),
    )
    out_specs = P("feed", None, "chan")
    return jax.shard_map(
        on_device, mesh=mesh, in_specs=in_specs, out_specs=out_specs, check_vma=False
    )
```

```python
import math

import numpy as np
import jax
import jax.numpy as jnp
from jax import lax
from jax.experimental import pallas as pl
from jax.experimental.pallas import tpu as pltpu
from jax.sharding import PartitionSpec as P

U = 16
TAPS = 4
TINT = 2
IB = 4
CHUNKS = 2
FRAMES = 2 * IB


def window_taps_np():
    length = TAPS * U
    positions = np.arange(length, dtype=np.float64)
    offsets = (positions - (length - 1) / 2.0) / U
    hann_taper = 0.5 - 0.5 * np.cos(2.0 * math.pi * (positions + 0.5) / length)
    taps_window = np.sinc(offsets) * hann_taper
    taps_window = taps_window / np.sqrt(np.sum(taps_window * taps_window) / U)
    return taps_window.astype(np.float32)


def band_matrix():
    taps = window_taps_np().astype(np.float64)
    span = (FRAMES + TAPS - 1) * U
    index_n = np.arange(U)
    phases = 2.0 * math.pi * ((index_n[:, None] * index_n[None, :]) % U) / U
    cosine = np.cos(phases) / math.sqrt(U)
    sine = np.sin(phases) / math.sqrt(U)
    table = np.array([[cosine, -sine], [sine, cosine]])
    band = np.zeros((2, FRAMES, U, 2, span))
    for t in range(FRAMES):
        for m in range(TAPS * U):
            for r in range(2):
                band[:, t, :, r, t * U + m] = taps[m] * table[r, :, m % U, :]
    band = band.reshape(2 * FRAMES * U, 2 * span).astype(np.float32)
    high = band.astype(jnp.bfloat16)
    low = (band - high.astype(np.float32)).astype(jnp.bfloat16)
    return np.concatenate([high, low], axis=0)


def _filter_kernel(chunk, main_ref, pre0_ref, pre1_ref, pre2_ref, hist_ref, gain_ref, band_ref, *rest):
    out_ref = rest[-1]
    tdev = pl.program_id(0)
    rows_main = main_ref.shape[4]
    nb = out_ref.shape[1]
    span = (FRAMES + TAPS - 1) * U
    half = FRAMES * U
    lanes = main_ref.shape[5]
    g_re = jnp.concatenate([gain_ref[0, p] for p in range(2)], axis=1)
    g_im = jnp.concatenate([gain_ref[1, p] for p in range(2)], axis=1)

    def rows_of(r, start, size):
        return jnp.concatenate([main_ref[r, p, 0, 0, pl.ds(start, size), :] for p in range(2)], axis=1)

    def prefix_of(r):
        pre = [jnp.concatenate([ref[r, p, 0, 0] for p in range(2)], axis=1) for ref in (pre0_ref, pre1_ref, pre2_ref)]
        pre = jnp.concatenate(pre, axis=0)
        if chunk == 0:
            hist = jnp.concatenate([hist_ref[r, p, 0] for p in range(2)], axis=1)
            pre = jnp.where(tdev == 0, hist, pre)
        return pre

    for ib in range(nb):
        parts = []
        for r in range(2):
            if ib == 0:
                parts.append(jnp.concatenate([prefix_of(r), rows_of(r, 0, span - 48)], axis=0))
            else:
                parts.append(rows_of(r, ib * half - 48, span))
        rhs = jnp.concatenate(parts, axis=0)
        both = jnp.dot(band_ref[...], rhs, preferred_element_type=jnp.float32)
        rows = both.shape[0] // 2
        spec = both[:rows] + both[rows:]
        s_re = spec[:half]
        s_im = spec[half:]
        c_re = (g_re * s_re - g_im * s_im).astype(jnp.bfloat16)
        c_im = (g_re * s_im + g_im * s_re).astype(jnp.bfloat16)
        for p in range(2):
            out_ref[0, ib, 0, p] = c_re[:, p * lanes : (p + 1) * lanes].reshape(IB, TINT, U, lanes)
            out_ref[0, ib, 1, p] = c_im[:, p * lanes : (p + 1) * lanes].reshape(IB, TINT, U, lanes)


def filterbank(voltages, history, gains, band, chunk, chunks, after=None):
    _, pols, _, samples, feeds = voltages.shape
    nblk = 8
    rows_blk = samples // nblk
    rows_main = rows_blk // chunks
    nb = rows_main // U // FRAMES
    main = voltages.reshape(2, pols, nblk, chunks, rows_main, feeds)
    units = voltages.reshape(2, pols, nblk, rows_blk // 16, 16, feeds)

    def pre_map(m):
        if chunk == 0:
            return lambda t: (0, 0, jnp.maximum(t - 1, 0), rows_blk // 16 - 3 + m, 0, 0)
        return lambda t: (0, 0, t, chunk * rows_main // 16 - 3 + m, 0, 0)

    extra = [] if after is None else [after]
    return pl.pallas_call(
        lambda *refs: _filter_kernel(chunk, *refs),
        grid=(nblk,),
        in_specs=[
            pl.BlockSpec((2, pols, 1, 1, rows_main, feeds), lambda t: (0, 0, t, chunk, 0, 0)),
            pl.BlockSpec((2, pols, 1, 1, 16, feeds), pre_map(0)),
            pl.BlockSpec((2, pols, 1, 1, 16, feeds), pre_map(1)),
            pl.BlockSpec((2, pols, 1, 1, 16, feeds), pre_map(2)),
            pl.BlockSpec((2, pols, 1, 48, feeds), lambda t: (0, 0, 0, 0, 0)),
            pl.BlockSpec((2, pols, 1, feeds), lambda t: (0, 0, 0, 0)),
            pl.BlockSpec(band.shape, lambda t: (0, 0)),
        ]
        + [pl.BlockSpec((1, 1, U, 128), lambda t: (0, 0, 0, 0)) for _ in extra],
        out_specs=pl.BlockSpec((1, nb, 2, pols, IB, TINT, U, feeds), lambda t: (t, 0, 0, 0, 0, 0, 0, 0)),
        out_shape=jax.ShapeDtypeStruct((nblk, nb, 2, pols, IB, TINT, U, feeds), jnp.bfloat16),
        cost_estimate=pl.CostEstimate(
            flops=2 * band.size * feeds * pols * nblk * nb,
            bytes_accessed=2 * voltages.size * 2 // chunks,
            transcendentals=0,
        ),
    )(main, units, units, units, history, gains, band, *extra)


def _beam_kernel(cal_ref, w_ref, sel_ref, out_ref):
    nsrc = cal_ref.shape[0]
    rows = 2 * 2 * IB * U
    halves = []
    for s in range(2):
        pieces = [cal_ref[d, 0, s].reshape(rows, 128) for d in range(nsrc)]
        halves.append(jnp.concatenate(pieces, axis=1))
    lhs = jnp.concatenate(halves, axis=0)
    prod_re = jnp.dot(lhs, w_ref[0, 0], preferred_element_type=jnp.float32)
    prod_im = jnp.dot(lhs, w_ref[1, 0], preferred_element_type=jnp.float32)
    real_part = prod_re[:rows] - prod_im[rows:]
    imag_part = prod_im[:rows] + prod_re[rows:]
    power = real_part * real_part + imag_part * imag_part
    quarter = rows // 2
    power = power[:quarter] + power[quarter:]
    power = power.reshape(IB, TINT, U, power.shape[-1])
    power = (power[:, 0] + power[:, 1]).reshape(IB * U, power.shape[-1])
    detected = (power * (1.0 / (4.0 * TINT))).astype(jnp.bfloat16)
    picked = jnp.dot(detected, sel_ref[...], preferred_element_type=jnp.float32).astype(jnp.bfloat16)
    nodes = out_ref.shape[0]
    for n in range(nodes):
        out_ref[n] = picked[:, n * 128 : (n + 1) * 128].reshape(IB, U, 128)


def beamform(cal, weights, select):
    nsrc, nb = cal.shape[0], cal.shape[1]
    feeds, beams = weights.shape[2], weights.shape[3]
    slots = select.shape[1]
    nodes = slots // 128
    return pl.pallas_call(
        _beam_kernel,
        grid=(nb,),
        in_specs=[
            pl.BlockSpec((nsrc, 1, 2, 2, IB, TINT, U, 128), lambda i: (0, i, 0, 0, 0, 0, 0, 0)),
            pl.BlockSpec((2, 1, feeds, beams), lambda i: (0, 0, 0, 0)),
            pl.BlockSpec((beams, slots), lambda i: (0, 0)),
        ],
        out_specs=pl.BlockSpec((nodes, IB, U, 128), lambda i: (0, i, 0, 0)),
        out_shape=jax.ShapeDtypeStruct((nodes, nb * IB, U, 128), jnp.bfloat16),
        cost_estimate=pl.CostEstimate(
            flops=2 * 2 * (4 * nb * IB * U * TINT) * feeds * beams + 2 * nb * IB * U * beams * slots,
            bytes_accessed=cal.size * 2 + weights.size * 2 + select.size * 2 + nb * IB * U * slots * 2,
            transcendentals=0,
        ),
        compiler_params=pltpu.CompilerParams(vmem_limit_bytes=60 * 1024 * 1024),
    )(cal, weights, select)


def exchange_by_permutes(blocks, axis, inner):
    count = lax.axis_size(axis)
    outer = count // inner
    me = lax.axis_index(axis)
    lo, hi = lax.rem(me, inner), me // inner
    rest = blocks.shape[1:]
    grid = blocks.reshape((outer, inner) + rest)

    def stage(values, mine, size, place):
        got = [lax.dynamic_index_in_dim(values, mine, axis=1, keepdims=False)]
        for shift in range(1, size):
            pairs = [(i, place(i, shift)) for i in range(count)]
            piece = lax.dynamic_index_in_dim(values, lax.rem(mine + shift, size), axis=1, keepdims=False)
            got.append(lax.ppermute(piece, axis, perm=pairs))
        return jnp.stack(got)

    first = stage(
        grid, lo, inner,
        lambda i, s: (i // inner) * inner + (i % inner + s) % inner,
    )
    second = stage(first, hi, outer, lambda i, s: ((i // inner + s) % outer) * inner + i % inner)
    order_hi = lax.rem(hi - jnp.arange(outer, dtype=jnp.int32) + outer, outer)
    order_lo = lax.rem(lo - jnp.arange(inner, dtype=jnp.int32) + inner, inner)
    out = jnp.take(jnp.take(second, order_hi, axis=0), order_lo, axis=1)
    return out.reshape((count,) + rest)


def on_device(voltages, history, gains, weights, beam_lists, beam_counts):
    capacity = beam_lists.shape[1]
    beams = weights.shape[3]
    flat_ids = beam_lists.reshape(-1)
    live_slots = (jnp.arange(capacity, dtype=jnp.int32)[None, :] < beam_counts[:, None]).reshape(-1)
    select = (
        (jnp.arange(beams, dtype=jnp.int32)[:, None] == flat_ids[None, :]) & live_slots[None, :]
    ).astype(jnp.bfloat16)
    band = jnp.asarray(band_matrix())
    gathered = []
    outs = []
    for chunk in range(CHUNKS + 1):
        if chunk < CHUNKS:
            after = outs[-1] if outs else None
            calibrated = filterbank(voltages, history, gains, band, chunk, CHUNKS, after)
            gathered.append(lax.all_to_all(calibrated, "feed", split_axis=0, concat_axis=0, tiled=True))
        if chunk >= 1:
            picked = beamform(gathered[chunk - 1], weights, select)
            if chunk < CHUNKS:
                outs.append(exchange_by_permutes(picked, "chan", 4))
            else:
                outs.append(lax.all_to_all(picked, "chan", split_axis=0, concat_axis=0, tiled=True))
    exchanged = jnp.concatenate(outs, axis=1)
    nodes, bins, fine, width = exchanged.shape
    return jnp.transpose(exchanged, (1, 0, 2, 3)).reshape(bins, nodes * fine, width)


def solution(mesh):
    in_specs = (
        P(None, None, "chan", None, "feed"),
        P(None, None, "chan", None, "feed"),
        P(None, None, "chan", "feed"),
        P(None, "chan", None, None),
        P(),
        P(),
    )
    out_specs = P("feed", None, "chan")
    return jax.shard_map(
        on_device, mesh=mesh, in_specs=in_specs, out_specs=out_specs, check_vma=False
    )
```

```python
import math

import numpy as np
import jax
import jax.numpy as jnp
from jax import lax
from jax.experimental import pallas as pl
from jax.experimental.pallas import tpu as pltpu
from jax.sharding import PartitionSpec as P

U = 16
TAPS = 4
TINT = 2
IB = 4
CHUNKS = 2
FRAMES = 2 * IB


def window_taps_np():
    length = TAPS * U
    positions = np.arange(length, dtype=np.float64)
    offsets = (positions - (length - 1) / 2.0) / U
    hann_taper = 0.5 - 0.5 * np.cos(2.0 * math.pi * (positions + 0.5) / length)
    taps_window = np.sinc(offsets) * hann_taper
    taps_window = taps_window / np.sqrt(np.sum(taps_window * taps_window) / U)
    return taps_window.astype(np.float32)


def band_matrix():
    taps = window_taps_np().astype(np.float64)
    span = (FRAMES + TAPS - 1) * U
    index_n = np.arange(U)
    phases = 2.0 * math.pi * ((index_n[:, None] * index_n[None, :]) % U) / U
    cosine = np.cos(phases) / math.sqrt(U)
    sine = np.sin(phases) / math.sqrt(U)
    table = np.array([[cosine, -sine], [sine, cosine]])
    band = np.zeros((2, FRAMES, U, 2, span))
    for t in range(FRAMES):
        for m in range(TAPS * U):
            for r in range(2):
                band[:, t, :, r, t * U + m] = taps[m] * table[r, :, m % U, :]
    band = band.reshape(2 * FRAMES * U, 2 * span).astype(np.float32)
    high = band.astype(jnp.bfloat16)
    low = (band - high.astype(np.float32)).astype(jnp.bfloat16)
    return np.concatenate([high, low], axis=0)


def _filter_kernel(chunk, main_ref, pre0_ref, pre1_ref, pre2_ref, hist_ref, gain_ref, band_ref, *rest):
    out_ref = rest[-1]
    tdev = pl.program_id(0)
    rows_main = main_ref.shape[4]
    nb = out_ref.shape[1]
    span = (FRAMES + TAPS - 1) * U
    half = FRAMES * U
    lanes = main_ref.shape[5]
    g_re = jnp.concatenate([gain_ref[0, p] for p in range(2)], axis=1)
    g_im = jnp.concatenate([gain_ref[1, p] for p in range(2)], axis=1)

    def rows_of(r, start, size):
        return jnp.concatenate([main_ref[r, p, 0, 0, pl.ds(start, size), :] for p in range(2)], axis=1)

    def prefix_of(r):
        pre = [jnp.concatenate([ref[r, p, 0, 0] for p in range(2)], axis=1) for ref in (pre0_ref, pre1_ref, pre2_ref)]
        pre = jnp.concatenate(pre, axis=0)
        if chunk == 0:
            hist = jnp.concatenate([hist_ref[r, p, 0] for p in range(2)], axis=1)
            pre = jnp.where(tdev == 0, hist, pre)
        return pre

    for ib in range(nb):
        parts = []
        for r in range(2):
            if ib == 0:
                parts.append(jnp.concatenate([prefix_of(r), rows_of(r, 0, span - 48)], axis=0))
            else:
                parts.append(rows_of(r, ib * half - 48, span))
        rhs = jnp.concatenate(parts, axis=0)
        both = jnp.dot(band_ref[...], rhs, preferred_element_type=jnp.float32)
        rows = both.shape[0] // 2
        spec = both[:rows] + both[rows:]
        s_re = spec[:half]
        s_im = spec[half:]
        c_re = (g_re * s_re - g_im * s_im).astype(jnp.bfloat16)
        c_im = (g_re * s_im + g_im * s_re).astype(jnp.bfloat16)
        for p in range(2):
            out_ref[0, ib, 0, p] = c_re[:, p * lanes : (p + 1) * lanes].reshape(IB, TINT, U, lanes)
            out_ref[0, ib, 1, p] = c_im[:, p * lanes : (p + 1) * lanes].reshape(IB, TINT, U, lanes)


def filterbank(voltages, history, gains, band, chunk, chunks, after=None):
    _, pols, _, samples, feeds = voltages.shape
    nblk = 8
    rows_blk = samples // nblk
    rows_main = rows_blk // chunks
    nb = rows_main // U // FRAMES
    main = voltages.reshape(2, pols, nblk, chunks, rows_main, feeds)
    units = voltages.reshape(2, pols, nblk, rows_blk // 16, 16, feeds)

    def pre_map(m):
        if chunk == 0:
            return lambda t: (0, 0, jnp.maximum(t - 1, 0), rows_blk // 16 - 3 + m, 0, 0)
        return lambda t: (0, 0, t, chunk * rows_main // 16 - 3 + m, 0, 0)

    extra = [] if after is None else [after]
    return pl.pallas_call(
        lambda *refs: _filter_kernel(chunk, *refs),
        grid=(nblk,),
        in_specs=[
            pl.BlockSpec((2, pols, 1, 1, rows_main, feeds), lambda t: (0, 0, t, chunk, 0, 0)),
            pl.BlockSpec((2, pols, 1, 1, 16, feeds), pre_map(0)),
            pl.BlockSpec((2, pols, 1, 1, 16, feeds), pre_map(1)),
            pl.BlockSpec((2, pols, 1, 1, 16, feeds), pre_map(2)),
            pl.BlockSpec((2, pols, 1, 48, feeds), lambda t: (0, 0, 0, 0, 0)),
            pl.BlockSpec((2, pols, 1, feeds), lambda t: (0, 0, 0, 0)),
            pl.BlockSpec(band.shape, lambda t: (0, 0)),
        ]
        + [pl.BlockSpec((1, 1, U, 128), lambda t: (0, 0, 0, 0)) for _ in extra],
        out_specs=pl.BlockSpec((1, nb, 2, pols, IB, TINT, U, feeds), lambda t: (t, 0, 0, 0, 0, 0, 0, 0)),
        out_shape=jax.ShapeDtypeStruct((nblk, nb, 2, pols, IB, TINT, U, feeds), jnp.bfloat16),
        cost_estimate=pl.CostEstimate(
            flops=2 * band.size * feeds * pols * nblk * nb,
            bytes_accessed=2 * voltages.size * 2 // chunks,
            transcendentals=0,
        ),
    )(main, units, units, units, history, gains, band, *extra)


def _beam_kernel(cal_ref, w_ref, sel_ref, *rest):
    out_ref = rest[-1]
    nsrc = cal_ref.shape[0]
    rows = 2 * 2 * IB * U
    halves = []
    for s in range(2):
        pieces = [cal_ref[d, 0, s].reshape(rows, 128) for d in range(nsrc)]
        halves.append(jnp.concatenate(pieces, axis=1))
    lhs = jnp.concatenate(halves, axis=0)
    prod_re = jnp.dot(lhs, w_ref[0, 0], preferred_element_type=jnp.float32)
    prod_im = jnp.dot(lhs, w_ref[1, 0], preferred_element_type=jnp.float32)
    real_part = prod_re[:rows] - prod_im[rows:]
    imag_part = prod_im[:rows] + prod_re[rows:]
    power = real_part * real_part + imag_part * imag_part
    quarter = rows // 2
    power = power[:quarter] + power[quarter:]
    power = power.reshape(IB, TINT, U, power.shape[-1])
    power = (power[:, 0] + power[:, 1]).reshape(IB * U, power.shape[-1])
    detected = (power * (1.0 / (4.0 * TINT))).astype(jnp.bfloat16)
    picked = jnp.dot(detected, sel_ref[...], preferred_element_type=jnp.float32).astype(jnp.bfloat16)
    nodes = out_ref.shape[0]
    for n in range(nodes):
        out_ref[n] = picked[:, n * 128 : (n + 1) * 128].reshape(IB, U, 128)


def beamform(cal, weights, select, after=None):
    extra = [] if after is None else [after]
    nsrc, nb = cal.shape[0], cal.shape[1]
    feeds, beams = weights.shape[2], weights.shape[3]
    slots = select.shape[1]
    nodes = slots // 128
    return pl.pallas_call(
        _beam_kernel,
        grid=(nb,),
        in_specs=[
            pl.BlockSpec((nsrc, 1, 2, 2, IB, TINT, U, 128), lambda i: (0, i, 0, 0, 0, 0, 0, 0)),
            pl.BlockSpec((2, 1, feeds, beams), lambda i: (0, 0, 0, 0)),
            pl.BlockSpec((beams, slots), lambda i: (0, 0)),
        ]
        + [pl.BlockSpec((1, 1, U, 128), lambda i: (0, 0, 0, 0)) for _ in extra],
        out_specs=pl.BlockSpec((nodes, IB, U, 128), lambda i: (0, i, 0, 0)),
        out_shape=jax.ShapeDtypeStruct((nodes, nb * IB, U, 128), jnp.bfloat16),
        cost_estimate=pl.CostEstimate(
            flops=2 * 2 * (4 * nb * IB * U * TINT) * feeds * beams + 2 * nb * IB * U * beams * slots,
            bytes_accessed=cal.size * 2 + weights.size * 2 + select.size * 2 + nb * IB * U * slots * 2,
            transcendentals=0,
        ),
        compiler_params=pltpu.CompilerParams(vmem_limit_bytes=60 * 1024 * 1024),
    )(cal, weights, select, *extra)


def exchange_by_permutes(blocks, axis, inner):
    count = lax.axis_size(axis)
    outer = count // inner
    me = lax.axis_index(axis)
    lo, hi = lax.rem(me, inner), me // inner
    rest = blocks.shape[1:]
    grid = blocks.reshape((outer, inner) + rest)

    def stage(values, mine, size, place):
        got = [lax.dynamic_index_in_dim(values, mine, axis=1, keepdims=False)]
        for shift in range(1, size):
            pairs = [(i, place(i, shift)) for i in range(count)]
            piece = lax.dynamic_index_in_dim(values, lax.rem(mine + shift, size), axis=1, keepdims=False)
            got.append(lax.ppermute(piece, axis, perm=pairs))
        return jnp.stack(got)

    first = stage(
        grid, lo, inner,
        lambda i, s: (i // inner) * inner + (i % inner + s) % inner,
    )
    second = stage(first, hi, outer, lambda i, s: ((i // inner + s) % outer) * inner + i % inner)
    order_hi = lax.rem(hi - jnp.arange(outer, dtype=jnp.int32) + outer, outer)
    order_lo = lax.rem(lo - jnp.arange(inner, dtype=jnp.int32) + inner, inner)
    out = jnp.take(jnp.take(second, order_hi, axis=0), order_lo, axis=1)
    return out.reshape((count,) + rest)


def on_device(voltages, history, gains, weights, beam_lists, beam_counts):
    capacity = beam_lists.shape[1]
    beams = weights.shape[3]
    flat_ids = beam_lists.reshape(-1)
    live_slots = (jnp.arange(capacity, dtype=jnp.int32)[None, :] < beam_counts[:, None]).reshape(-1)
    select = (
        (jnp.arange(beams, dtype=jnp.int32)[:, None] == flat_ids[None, :]) & live_slots[None, :]
    ).astype(jnp.bfloat16)
    band = jnp.asarray(band_matrix())
    gathered = []
    outs = []
    for chunk in range(CHUNKS + 1):
        if chunk < CHUNKS:
            after = outs[-1] if outs else None
            calibrated = filterbank(voltages, history, gains, band, chunk, CHUNKS, after)
            gathered.append(lax.all_to_all(calibrated, "feed", split_axis=0, concat_axis=0, tiled=True))
        if chunk >= 1:
            after = outs[-1].reshape(-1, 1, U, 128) if outs else None
            picked = beamform(gathered[chunk - 1], weights, select, after)
            if chunk < CHUNKS:
                outs.append(exchange_by_permutes(picked, "chan", 4))
            else:
                outs.append(lax.all_to_all(picked, "chan", split_axis=0, concat_axis=0, tiled=True))
    exchanged = jnp.concatenate(outs, axis=1)
    nodes, bins, fine, width = exchanged.shape
    return jnp.transpose(exchanged, (1, 0, 2, 3)).reshape(bins, nodes * fine, width)


def solution(mesh):
    in_specs = (
        P(None, None, "chan", None, "feed"),
        P(None, None, "chan", None, "feed"),
        P(None, None, "chan", "feed"),
        P(None, "chan", None, None),
        P(),
        P(),
    )
    out_specs = P("feed", None, "chan")
    return jax.shard_map(
        on_device, mesh=mesh, in_specs=in_specs, out_specs=out_specs, check_vma=False
    )
```

```python
import math

import numpy as np
import jax
import jax.numpy as jnp
from jax import lax
from jax.experimental import pallas as pl
from jax.experimental.pallas import tpu as pltpu
from jax.sharding import PartitionSpec as P

U = 16
TAPS = 4
TINT = 2
IB = 4
CHUNKS = 2
FRAMES = 2 * IB


def window_taps_np():
    length = TAPS * U
    positions = np.arange(length, dtype=np.float64)
    offsets = (positions - (length - 1) / 2.0) / U
    hann_taper = 0.5 - 0.5 * np.cos(2.0 * math.pi * (positions + 0.5) / length)
    taps_window = np.sinc(offsets) * hann_taper
    taps_window = taps_window / np.sqrt(np.sum(taps_window * taps_window) / U)
    return taps_window.astype(np.float32)


def band_matrix():
    taps = window_taps_np().astype(np.float64)
    span = (FRAMES + TAPS - 1) * U
    index_n = np.arange(U)
    phases = 2.0 * math.pi * ((index_n[:, None] * index_n[None, :]) % U) / U
    cosine = np.cos(phases) / math.sqrt(U)
    sine = np.sin(phases) / math.sqrt(U)
    table = np.array([[cosine, -sine], [sine, cosine]])
    band = np.zeros((2, FRAMES, U, 2, span))
    for t in range(FRAMES):
        for m in range(TAPS * U):
            for r in range(2):
                band[:, t, :, r, t * U + m] = taps[m] * table[r, :, m % U, :]
    band = band.reshape(2 * FRAMES * U, 2 * span).astype(np.float32)
    high = band.astype(jnp.bfloat16)
    low = (band - high.astype(np.float32)).astype(jnp.bfloat16)
    return np.concatenate([high, low], axis=0)


def _filter_kernel(chunk, main_ref, pre0_ref, pre1_ref, pre2_ref, hist_ref, gain_ref, band_ref, *rest):
    out_ref = rest[-1]
    tdev = pl.program_id(0)
    rows_main = main_ref.shape[4]
    nb = out_ref.shape[1]
    span = (FRAMES + TAPS - 1) * U
    half = FRAMES * U
    lanes = main_ref.shape[5]
    g_re = jnp.concatenate([gain_ref[0, p] for p in range(2)], axis=1)
    g_im = jnp.concatenate([gain_ref[1, p] for p in range(2)], axis=1)

    def rows_of(r, start, size):
        return jnp.concatenate([main_ref[r, p, 0, 0, pl.ds(start, size), :] for p in range(2)], axis=1)

    def prefix_of(r):
        pre = [jnp.concatenate([ref[r, p, 0, 0] for p in range(2)], axis=1) for ref in (pre0_ref, pre1_ref, pre2_ref)]
        pre = jnp.concatenate(pre, axis=0)
        if chunk == 0:
            hist = jnp.concatenate([hist_ref[r, p, 0] for p in range(2)], axis=1)
            pre = jnp.where(tdev == 0, hist, pre)
        return pre

    for ib in range(nb):
        parts = []
        for r in range(2):
            if ib == 0:
                parts.append(jnp.concatenate([prefix_of(r), rows_of(r, 0, span - 48)], axis=0))
            else:
                parts.append(rows_of(r, ib * half - 48, span))
        rhs = jnp.concatenate(parts, axis=0)
        both = jnp.dot(band_ref[...], rhs, preferred_element_type=jnp.float32)
        rows = both.shape[0] // 2
        spec = both[:rows] + both[rows:]
        s_re = spec[:half]
        s_im = spec[half:]
        c_re = (g_re * s_re - g_im * s_im).astype(jnp.bfloat16)
        c_im = (g_re * s_im + g_im * s_re).astype(jnp.bfloat16)
        for p in range(2):
            out_ref[0, ib, 0, p] = c_re[:, p * lanes : (p + 1) * lanes].reshape(IB, TINT, U, lanes)
            out_ref[0, ib, 1, p] = c_im[:, p * lanes : (p + 1) * lanes].reshape(IB, TINT, U, lanes)


def filterbank(voltages, history, gains, band, chunk, chunks, after=None):
    _, pols, _, samples, feeds = voltages.shape
    nblk = 8
    rows_blk = samples // nblk
    rows_main = rows_blk // chunks
    nb = rows_main // U // FRAMES
    main = voltages.reshape(2, pols, nblk, chunks, rows_main, feeds)
    units = voltages.reshape(2, pols, nblk, rows_blk // 16, 16, feeds)

    def pre_map(m):
        if chunk == 0:
            return lambda t: (0, 0, jnp.maximum(t - 1, 0), rows_blk // 16 - 3 + m, 0, 0)
        return lambda t: (0, 0, t, chunk * rows_main // 16 - 3 + m, 0, 0)

    extra = [] if after is None else [after]
    return pl.pallas_call(
        lambda *refs: _filter_kernel(chunk, *refs),
        grid=(nblk,),
        in_specs=[
            pl.BlockSpec((2, pols, 1, 1, rows_main, feeds), lambda t: (0, 0, t, chunk, 0, 0)),
            pl.BlockSpec((2, pols, 1, 1, 16, feeds), pre_map(0)),
            pl.BlockSpec((2, pols, 1, 1, 16, feeds), pre_map(1)),
            pl.BlockSpec((2, pols, 1, 1, 16, feeds), pre_map(2)),
            pl.BlockSpec((2, pols, 1, 48, feeds), lambda t: (0, 0, 0, 0, 0)),
            pl.BlockSpec((2, pols, 1, feeds), lambda t: (0, 0, 0, 0)),
            pl.BlockSpec(band.shape, lambda t: (0, 0)),
        ]
        + [pl.BlockSpec((1, 1, U, 128), lambda t: (0, 0, 0, 0)) for _ in extra],
        out_specs=pl.BlockSpec((1, nb, 2, pols, IB, TINT, U, feeds), lambda t: (t, 0, 0, 0, 0, 0, 0, 0)),
        out_shape=jax.ShapeDtypeStruct((nblk, nb, 2, pols, IB, TINT, U, feeds), jnp.bfloat16),
        cost_estimate=pl.CostEstimate(
            flops=2 * band.size * feeds * pols * nblk * nb,
            bytes_accessed=2 * voltages.size * 2 // chunks,
            transcendentals=0,
        ),
    )(main, units, units, units, history, gains, band, *extra)


def _beam_kernel(cal_ref, w_ref, sel_ref, out_ref):
    nsrc = cal_ref.shape[0]
    rows = 2 * 2 * IB * U
    halves = []
    for s in range(2):
        pieces = [cal_ref[d, 0, s].reshape(rows, 128) for d in range(nsrc)]
        halves.append(jnp.concatenate(pieces, axis=1))
    lhs = jnp.concatenate(halves, axis=0)
    prod_re = jnp.dot(lhs, w_ref[0, 0], preferred_element_type=jnp.float32)
    prod_im = jnp.dot(lhs, w_ref[1, 0], preferred_element_type=jnp.float32)
    real_part = prod_re[:rows] - prod_im[rows:]
    imag_part = prod_im[:rows] + prod_re[rows:]
    power = real_part * real_part + imag_part * imag_part
    quarter = rows // 2
    power = power[:quarter] + power[quarter:]
    power = power.reshape(IB, TINT, U, power.shape[-1])
    power = (power[:, 0] + power[:, 1]).reshape(IB * U, power.shape[-1])
    detected = (power * (1.0 / (4.0 * TINT))).astype(jnp.bfloat16)
    picked = jnp.dot(detected, sel_ref[...], preferred_element_type=jnp.float32).astype(jnp.bfloat16)
    nodes = out_ref.shape[0]
    for n in range(nodes):
        out_ref[n] = picked[:, n * 128 : (n + 1) * 128].reshape(IB, U, 128)


def _beam_pieces_kernel(*refs):
    count = len(refs) - 3

    class Stacked:
        def __getitem__(self, index):
            return refs[index[0]][(0,) + index[1:]]

    shape = (count,) + refs[0].shape[1:]
    stacked = Stacked()
    stacked.shape = shape
    _beam_kernel(stacked, *refs[count:])


def beamform_pieces(pieces, weights, select):
    nb = pieces[0].shape[1]
    feeds, beams = weights.shape[2], weights.shape[3]
    slots = select.shape[1]
    nodes = slots // 128
    piece_spec = pl.BlockSpec((1, 1, 2, 2, IB, TINT, U, 128), lambda i: (0, i, 0, 0, 0, 0, 0, 0))
    return pl.pallas_call(
        _beam_pieces_kernel,
        grid=(nb,),
        in_specs=[piece_spec] * len(pieces)
        + [
            pl.BlockSpec((2, 1, feeds, beams), lambda i: (0, 0, 0, 0)),
            pl.BlockSpec((beams, slots), lambda i: (0, 0)),
        ],
        out_specs=pl.BlockSpec((nodes, IB, U, 128), lambda i: (0, i, 0, 0)),
        out_shape=jax.ShapeDtypeStruct((nodes, nb * IB, U, 128), jnp.bfloat16),
        cost_estimate=pl.CostEstimate(
            flops=2 * 2 * (4 * nb * IB * U * TINT) * feeds * beams + 2 * nb * IB * U * beams * slots,
            bytes_accessed=sum(p.size for p in pieces) * 2 + weights.size * 2 + select.size * 2 + nb * IB * U * slots * 2,
            transcendentals=0,
        ),
        compiler_params=pltpu.CompilerParams(vmem_limit_bytes=60 * 1024 * 1024),
    )(*pieces, weights, select)


def beamform(cal, weights, select):
    nsrc, nb = cal.shape[0], cal.shape[1]
    feeds, beams = weights.shape[2], weights.shape[3]
    slots = select.shape[1]
    nodes = slots // 128
    return pl.pallas_call(
        _beam_kernel,
        grid=(nb,),
        in_specs=[
            pl.BlockSpec((nsrc, 1, 2, 2, IB, TINT, U, 128), lambda i: (0, i, 0, 0, 0, 0, 0, 0)),
            pl.BlockSpec((2, 1, feeds, beams), lambda i: (0, 0, 0, 0)),
            pl.BlockSpec((beams, slots), lambda i: (0, 0)),
        ],
        out_specs=pl.BlockSpec((nodes, IB, U, 128), lambda i: (0, i, 0, 0)),
        out_shape=jax.ShapeDtypeStruct((nodes, nb * IB, U, 128), jnp.bfloat16),
        cost_estimate=pl.CostEstimate(
            flops=2 * 2 * (4 * nb * IB * U * TINT) * feeds * beams + 2 * nb * IB * U * beams * slots,
            bytes_accessed=cal.size * 2 + weights.size * 2 + select.size * 2 + nb * IB * U * slots * 2,
            transcendentals=0,
        ),
        compiler_params=pltpu.CompilerParams(vmem_limit_bytes=60 * 1024 * 1024),
    )(cal, weights, select)


def on_device(voltages, history, gains, weights, beam_lists, beam_counts):
    capacity = beam_lists.shape[1]
    beams = weights.shape[3]
    flat_ids = beam_lists.reshape(-1)
    live_slots = (jnp.arange(capacity, dtype=jnp.int32)[None, :] < beam_counts[:, None]).reshape(-1)
    select = (
        (jnp.arange(beams, dtype=jnp.int32)[:, None] == flat_ids[None, :]) & live_slots[None, :]
    ).astype(jnp.bfloat16)
    band = jnp.asarray(band_matrix())
    nfeed = lax.axis_size("feed")
    me = lax.axis_index("feed")
    order = lax.rem(me - jnp.arange(nfeed, dtype=jnp.int32) + nfeed, nfeed)
    feeds_local = weights.shape[2] // nfeed
    wperm = jnp.take(weights.reshape(2, 1, nfeed, feeds_local, beams), order, axis=2).reshape(weights.shape)
    first = filterbank(voltages, history, gains, band, 0, CHUNKS)
    gathered = lax.all_to_all(first, "feed", split_axis=0, concat_axis=0, tiled=True)
    second = filterbank(voltages, history, gains, band, 1, CHUNKS)
    pieces = [lax.dynamic_slice_in_dim(second, me, 1, axis=0)]
    for shift in range(1, nfeed):
        pairs = [(i, (i + shift) % nfeed) for i in range(nfeed)]
        piece = lax.dynamic_slice_in_dim(second, lax.rem(me + shift, nfeed), 1, axis=0)
        pieces.append(lax.ppermute(piece, "feed", perm=pairs))
    outs = []
    picked = beamform(gathered, weights, select)
    outs.append(lax.all_to_all(picked, "chan", split_axis=0, concat_axis=0, tiled=True))
    picked = beamform_pieces(pieces, wperm, select)
    outs.append(lax.all_to_all(picked, "chan", split_axis=0, concat_axis=0, tiled=True))
    exchanged = jnp.concatenate(outs, axis=1)
    nodes, bins, fine, width = exchanged.shape
    return jnp.transpose(exchanged, (1, 0, 2, 3)).reshape(bins, nodes * fine, width)


def solution(mesh):
    in_specs = (
        P(None, None, "chan", None, "feed"),
        P(None, None, "chan", None, "feed"),
        P(None, None, "chan", "feed"),
        P(None, "chan", None, None),
        P(),
        P(),
    )
    out_specs = P("feed", None, "chan")
    return jax.shard_map(
        on_device, mesh=mesh, in_specs=in_specs, out_specs=out_specs, check_vma=False
    )
```

```python
import math

import numpy as np
import jax
import jax.numpy as jnp
from jax import lax
from jax.experimental import pallas as pl
from jax.experimental.pallas import tpu as pltpu
from jax.sharding import PartitionSpec as P

U = 16
TAPS = 4
TINT = 2
IB = 4
CHUNKS = 2
FRAMES = 2 * IB


def window_taps_np():
    length = TAPS * U
    positions = np.arange(length, dtype=np.float64)
    offsets = (positions - (length - 1) / 2.0) / U
    hann_taper = 0.5 - 0.5 * np.cos(2.0 * math.pi * (positions + 0.5) / length)
    taps_window = np.sinc(offsets) * hann_taper
    taps_window = taps_window / np.sqrt(np.sum(taps_window * taps_window) / U)
    return taps_window.astype(np.float32)


def band_matrix():
    taps = window_taps_np().astype(np.float64)
    span = (FRAMES + TAPS - 1) * U
    index_n = np.arange(U)
    phases = 2.0 * math.pi * ((index_n[:, None] * index_n[None, :]) % U) / U
    cosine = np.cos(phases) / math.sqrt(U)
    sine = np.sin(phases) / math.sqrt(U)
    table = np.array([[cosine, -sine], [sine, cosine]])
    band = np.zeros((2, FRAMES, U, 2, span))
    for t in range(FRAMES):
        for m in range(TAPS * U):
            for r in range(2):
                band[:, t, :, r, t * U + m] = taps[m] * table[r, :, m % U, :]
    band = band.reshape(2 * FRAMES * U, 2 * span).astype(np.float32)
    high = band.astype(jnp.bfloat16)
    low = (band - high.astype(np.float32)).astype(jnp.bfloat16)
    return np.concatenate([high, low], axis=0)


def _filter_kernel(chunk, main_ref, pre0_ref, pre1_ref, pre2_ref, hist_ref, gain_ref, band_ref, *rest):
    out_ref = rest[-1]
    tdev = pl.program_id(0)
    rows_main = main_ref.shape[4]
    nb = out_ref.shape[1]
    span = (FRAMES + TAPS - 1) * U
    half = FRAMES * U
    lanes = main_ref.shape[5]
    g_re = jnp.concatenate([gain_ref[0, p] for p in range(2)], axis=1)
    g_im = jnp.concatenate([gain_ref[1, p] for p in range(2)], axis=1)

    def rows_of(r, start, size):
        return jnp.concatenate([main_ref[r, p, 0, 0, pl.ds(start, size), :] for p in range(2)], axis=1)

    def prefix_of(r):
        pre = [jnp.concatenate([ref[r, p, 0, 0] for p in range(2)], axis=1) for ref in (pre0_ref, pre1_ref, pre2_ref)]
        pre = jnp.concatenate(pre, axis=0)
        if chunk == 0:
            hist = jnp.concatenate([hist_ref[r, p, 0] for p in range(2)], axis=1)
            pre = jnp.where(tdev == 0, hist, pre)
        return pre

    for ib in range(nb):
        parts = []
        for r in range(2):
            if ib == 0:
                parts.append(jnp.concatenate([prefix_of(r), rows_of(r, 0, span - 48)], axis=0))
            else:
                parts.append(rows_of(r, ib * half - 48, span))
        rhs = jnp.concatenate(parts, axis=0)
        both = jnp.dot(band_ref[...], rhs, preferred_element_type=jnp.float32)
        rows = both.shape[0] // 2
        spec = both[:rows] + both[rows:]
        s_re = spec[:half]
        s_im = spec[half:]
        c_re = (g_re * s_re - g_im * s_im).astype(jnp.bfloat16)
        c_im = (g_re * s_im + g_im * s_re).astype(jnp.bfloat16)
        for p in range(2):
            out_ref[0, ib, 0, p] = c_re[:, p * lanes : (p + 1) * lanes].reshape(IB, TINT, U, lanes)
            out_ref[0, ib, 1, p] = c_im[:, p * lanes : (p + 1) * lanes].reshape(IB, TINT, U, lanes)


def filterbank(voltages, history, gains, band, chunk, chunks, after=None):
    _, pols, _, samples, feeds = voltages.shape
    nblk = 8
    rows_blk = samples // nblk
    rows_main = rows_blk // chunks
    nb = rows_main // U // FRAMES
    main = voltages.reshape(2, pols, nblk, chunks, rows_main, feeds)
    units = voltages.reshape(2, pols, nblk, rows_blk // 16, 16, feeds)

    def pre_map(m):
        if chunk == 0:
            return lambda t: (0, 0, jnp.maximum(t - 1, 0), rows_blk // 16 - 3 + m, 0, 0)
        return lambda t: (0, 0, t, chunk * rows_main // 16 - 3 + m, 0, 0)

    extra = [] if after is None else [after]
    return pl.pallas_call(
        lambda *refs: _filter_kernel(chunk, *refs),
        grid=(nblk,),
        in_specs=[
            pl.BlockSpec((2, pols, 1, 1, rows_main, feeds), lambda t: (0, 0, t, chunk, 0, 0)),
            pl.BlockSpec((2, pols, 1, 1, 16, feeds), pre_map(0)),
            pl.BlockSpec((2, pols, 1, 1, 16, feeds), pre_map(1)),
            pl.BlockSpec((2, pols, 1, 1, 16, feeds), pre_map(2)),
            pl.BlockSpec((2, pols, 1, 48, feeds), lambda t: (0, 0, 0, 0, 0)),
            pl.BlockSpec((2, pols, 1, feeds), lambda t: (0, 0, 0, 0)),
            pl.BlockSpec(band.shape, lambda t: (0, 0)),
        ]
        + [pl.BlockSpec((1, 1, U, 128), lambda t: (0, 0, 0, 0)) for _ in extra],
        out_specs=pl.BlockSpec((1, nb, 2, pols, IB, TINT, U, feeds), lambda t: (t, 0, 0, 0, 0, 0, 0, 0)),
        out_shape=jax.ShapeDtypeStruct((nblk, nb, 2, pols, IB, TINT, U, feeds), jnp.bfloat16),
        cost_estimate=pl.CostEstimate(
            flops=2 * band.size * feeds * pols * nblk * nb,
            bytes_accessed=2 * voltages.size * 2 // chunks,
            transcendentals=0,
        ),
    )(main, units, units, units, history, gains, band, *extra)


def _beam_kernel(cal_ref, w_ref, sel_ref, out_ref):
    nsrc = cal_ref.shape[0]
    rows = 2 * 2 * IB * U
    halves = []
    for s in range(2):
        pieces = [cal_ref[d, 0, s].reshape(rows, 128) for d in range(nsrc)]
        halves.append(jnp.concatenate(pieces, axis=1))
    lhs = jnp.concatenate(halves, axis=0)
    prod_re = jnp.dot(lhs, w_ref[0, 0], preferred_element_type=jnp.float32)
    prod_im = jnp.dot(lhs, w_ref[1, 0], preferred_element_type=jnp.float32)
    real_part = prod_re[:rows] - prod_im[rows:]
    imag_part = prod_im[:rows] + prod_re[rows:]
    power = real_part * real_part + imag_part * imag_part
    quarter = rows // 2
    power = power[:quarter] + power[quarter:]
    power = power.reshape(IB, TINT, U, power.shape[-1])
    power = (power[:, 0] + power[:, 1]).reshape(IB * U, power.shape[-1])
    detected = (power * (1.0 / (4.0 * TINT))).astype(jnp.bfloat16)
    picked = jnp.dot(detected, sel_ref[...], preferred_element_type=jnp.float32).astype(jnp.bfloat16)
    nodes = out_ref.shape[0]
    for n in range(nodes):
        out_ref[n] = picked[:, n * 128 : (n + 1) * 128].reshape(IB, U, 128)


def _beam_pieces_kernel(count, *refs):
    refs = refs[:count + 2] + refs[-1:]

    class Stacked:
        def __getitem__(self, index):
            return refs[index[0]][(0,) + index[1:]]

    shape = (count,) + refs[0].shape[1:]
    stacked = Stacked()
    stacked.shape = shape
    _beam_kernel(stacked, *refs[count:])


def beamform_pieces(pieces, weights, select, after):
    nb = pieces[0].shape[1]
    feeds, beams = weights.shape[2], weights.shape[3]
    slots = select.shape[1]
    nodes = slots // 128
    piece_spec = pl.BlockSpec((1, 1, 2, 2, IB, TINT, U, 128), lambda i: (0, i, 0, 0, 0, 0, 0, 0))
    return pl.pallas_call(
        lambda *refs: _beam_pieces_kernel(len(pieces), *refs),
        grid=(nb,),
        in_specs=[piece_spec] * len(pieces)
        + [
            pl.BlockSpec((2, 1, feeds, beams), lambda i: (0, 0, 0, 0)),
            pl.BlockSpec((beams, slots), lambda i: (0, 0)),
            pl.BlockSpec((1, 1, U, 128), lambda i: (0, 0, 0, 0)),
        ],
        out_specs=pl.BlockSpec((nodes, IB, U, 128), lambda i: (0, i, 0, 0)),
        out_shape=jax.ShapeDtypeStruct((nodes, nb * IB, U, 128), jnp.bfloat16),
        cost_estimate=pl.CostEstimate(
            flops=2 * 2 * (4 * nb * IB * U * TINT) * feeds * beams + 2 * nb * IB * U * beams * slots,
            bytes_accessed=sum(p.size for p in pieces) * 2 + weights.size * 2 + select.size * 2 + nb * IB * U * slots * 2,
            transcendentals=0,
        ),
        compiler_params=pltpu.CompilerParams(vmem_limit_bytes=60 * 1024 * 1024),
    )(*pieces, weights, select, after)


def beamform(cal, weights, select):
    nsrc, nb = cal.shape[0], cal.shape[1]
    feeds, beams = weights.shape[2], weights.shape[3]
    slots = select.shape[1]
    nodes = slots // 128
    return pl.pallas_call(
        _beam_kernel,
        grid=(nb,),
        in_specs=[
            pl.BlockSpec((nsrc, 1, 2, 2, IB, TINT, U, 128), lambda i: (0, i, 0, 0, 0, 0, 0, 0)),
            pl.BlockSpec((2, 1, feeds, beams), lambda i: (0, 0, 0, 0)),
            pl.BlockSpec((beams, slots), lambda i: (0, 0)),
        ],
        out_specs=pl.BlockSpec((nodes, IB, U, 128), lambda i: (0, i, 0, 0)),
        out_shape=jax.ShapeDtypeStruct((nodes, nb * IB, U, 128), jnp.bfloat16),
        cost_estimate=pl.CostEstimate(
            flops=2 * 2 * (4 * nb * IB * U * TINT) * feeds * beams + 2 * nb * IB * U * beams * slots,
            bytes_accessed=cal.size * 2 + weights.size * 2 + select.size * 2 + nb * IB * U * slots * 2,
            transcendentals=0,
        ),
        compiler_params=pltpu.CompilerParams(vmem_limit_bytes=60 * 1024 * 1024),
    )(cal, weights, select)


def on_device(voltages, history, gains, weights, beam_lists, beam_counts):
    capacity = beam_lists.shape[1]
    beams = weights.shape[3]
    flat_ids = beam_lists.reshape(-1)
    live_slots = (jnp.arange(capacity, dtype=jnp.int32)[None, :] < beam_counts[:, None]).reshape(-1)
    select = (
        (jnp.arange(beams, dtype=jnp.int32)[:, None] == flat_ids[None, :]) & live_slots[None, :]
    ).astype(jnp.bfloat16)
    band = jnp.asarray(band_matrix())
    nfeed = lax.axis_size("feed")
    me = lax.axis_index("feed")
    order = lax.rem(me - jnp.arange(nfeed, dtype=jnp.int32) + nfeed, nfeed)
    feeds_local = weights.shape[2] // nfeed
    wperm = jnp.take(weights.reshape(2, 1, nfeed, feeds_local, beams), order, axis=2).reshape(weights.shape)
    first = filterbank(voltages, history, gains, band, 0, CHUNKS)
    gathered = lax.all_to_all(first, "feed", split_axis=0, concat_axis=0, tiled=True)
    second = filterbank(voltages, history, gains, band, 1, CHUNKS)
    pieces = [lax.dynamic_slice_in_dim(second, me, 1, axis=0)]
    for shift in range(1, nfeed):
        pairs = [(i, (i + shift) % nfeed) for i in range(nfeed)]
        piece = lax.dynamic_slice_in_dim(second, lax.rem(me + shift, nfeed), 1, axis=0)
        pieces.append(lax.ppermute(piece, "feed", perm=pairs))
    outs = []
    picked = beamform(gathered, weights, select)
    outs.append(lax.all_to_all(picked, "chan", split_axis=0, concat_axis=0, tiled=True))
    picked = beamform_pieces(pieces, wperm, select, outs[0].reshape(-1, 1, U, 128))
    outs.append(lax.all_to_all(picked, "chan", split_axis=0, concat_axis=0, tiled=True))
    exchanged = jnp.concatenate(outs, axis=1)
    nodes, bins, fine, width = exchanged.shape
    return jnp.transpose(exchanged, (1, 0, 2, 3)).reshape(bins, nodes * fine, width)


def solution(mesh):
    in_specs = (
        P(None, None, "chan", None, "feed"),
        P(None, None, "chan", None, "feed"),
        P(None, None, "chan", "feed"),
        P(None, "chan", None, None),
        P(),
        P(),
    )
    out_specs = P("feed", None, "chan")
    return jax.shard_map(
        on_device, mesh=mesh, in_specs=in_specs, out_specs=out_specs, check_vma=False
    )
```

```python
import math

import numpy as np
import jax
import jax.numpy as jnp
from jax import lax
from jax.experimental import pallas as pl
from jax.experimental.pallas import tpu as pltpu
from jax.sharding import PartitionSpec as P

U = 16
TAPS = 4
TINT = 2
IB = 4
CHUNKS = 2
FRAMES = 2 * IB


def window_taps_np():
    length = TAPS * U
    positions = np.arange(length, dtype=np.float64)
    offsets = (positions - (length - 1) / 2.0) / U
    hann_taper = 0.5 - 0.5 * np.cos(2.0 * math.pi * (positions + 0.5) / length)
    taps_window = np.sinc(offsets) * hann_taper
    taps_window = taps_window / np.sqrt(np.sum(taps_window * taps_window) / U)
    return taps_window.astype(np.float32)


def band_matrix():
    taps = window_taps_np().astype(np.float64)
    span = (FRAMES + TAPS - 1) * U
    index_n = np.arange(U)
    phases = 2.0 * math.pi * ((index_n[:, None] * index_n[None, :]) % U) / U
    cosine = np.cos(phases) / math.sqrt(U)
    sine = np.sin(phases) / math.sqrt(U)
    table = np.array([[cosine, -sine], [sine, cosine]])
    band = np.zeros((2, FRAMES, U, 2, span))
    for t in range(FRAMES):
        for m in range(TAPS * U):
            for r in range(2):
                band[:, t, :, r, t * U + m] = taps[m] * table[r, :, m % U, :]
    band = band.reshape(2 * FRAMES * U, 2 * span).astype(np.float32)
    high = band.astype(jnp.bfloat16)
    low = (band - high.astype(np.float32)).astype(jnp.bfloat16)
    return np.concatenate([high, low], axis=0)


def _filter_kernel(chunk, shifted, *refs):
    if shifted:
        refs = refs[1:]
    _filter_body(chunk, *refs)


def _filter_body(chunk, main_ref, pre0_ref, pre1_ref, pre2_ref, hist_ref, gain_ref, band_ref, *rest):
    out_ref = rest[-1]
    tdev = pl.program_id(0)
    rows_main = main_ref.shape[4]
    nb = out_ref.shape[1]
    span = (FRAMES + TAPS - 1) * U
    half = FRAMES * U
    lanes = main_ref.shape[5]
    g_re = jnp.concatenate([gain_ref[0, p] for p in range(2)], axis=1)
    g_im = jnp.concatenate([gain_ref[1, p] for p in range(2)], axis=1)

    def rows_of(r, start, size):
        return jnp.concatenate([main_ref[r, p, 0, 0, pl.ds(start, size), :] for p in range(2)], axis=1)

    def prefix_of(r):
        pre = [jnp.concatenate([ref[r, p, 0, 0] for p in range(2)], axis=1) for ref in (pre0_ref, pre1_ref, pre2_ref)]
        pre = jnp.concatenate(pre, axis=0)
        if chunk == 0:
            hist = jnp.concatenate([hist_ref[r, p, 0] for p in range(2)], axis=1)
            pre = jnp.where(tdev == 0, hist, pre)
        return pre

    for ib in range(nb):
        parts = []
        for r in range(2):
            if ib == 0:
                parts.append(jnp.concatenate([prefix_of(r), rows_of(r, 0, span - 48)], axis=0))
            else:
                parts.append(rows_of(r, ib * half - 48, span))
        rhs = jnp.concatenate(parts, axis=0)
        both = jnp.dot(band_ref[...], rhs, preferred_element_type=jnp.float32)
        rows = both.shape[0] // 2
        spec = both[:rows] + both[rows:]
        s_re = spec[:half]
        s_im = spec[half:]
        c_re = (g_re * s_re - g_im * s_im).astype(jnp.bfloat16)
        c_im = (g_re * s_im + g_im * s_re).astype(jnp.bfloat16)
        for p in range(2):
            out_ref[0, ib, 0, p] = c_re[:, p * lanes : (p + 1) * lanes].reshape(IB, TINT, U, lanes)
            out_ref[0, ib, 1, p] = c_im[:, p * lanes : (p + 1) * lanes].reshape(IB, TINT, U, lanes)


def filterbank(voltages, history, gains, band, chunk, chunks, after=None, me=None):
    _, pols, _, samples, feeds = voltages.shape
    nblk = 8
    rows_blk = samples // nblk
    rows_main = rows_blk // chunks
    nb = rows_main // U // FRAMES
    main = voltages.reshape(2, pols, nblk, chunks, rows_main, feeds)
    units = voltages.reshape(2, pols, nblk, rows_blk // 16, 16, feeds)

    def pre_map(m):
        if chunk == 0:
            return lambda t: (0, 0, jnp.maximum(t - 1, 0), rows_blk // 16 - 3 + m, 0, 0)
        return lambda t: (0, 0, t, chunk * rows_main // 16 - 3 + m, 0, 0)

    extra = [] if after is None else [after]
    shifted = me is not None

    def spec(shape, index):
        if shifted:
            return pl.BlockSpec(shape, lambda t, me_ref: index(t))
        return pl.BlockSpec(shape, index)

    if shifted:
        out_spec = pl.BlockSpec(
            (1, nb, 2, pols, IB, TINT, U, feeds),
            lambda t, me_ref: (lax.rem(t - me_ref[0] + nblk, nblk), 0, 0, 0, 0, 0, 0, 0),
        )
    else:
        out_spec = pl.BlockSpec((1, nb, 2, pols, IB, TINT, U, feeds), lambda t: (t, 0, 0, 0, 0, 0, 0, 0))
    in_specs = [
        spec((2, pols, 1, 1, rows_main, feeds), lambda t: (0, 0, t, chunk, 0, 0)),
        spec((2, pols, 1, 1, 16, feeds), pre_map(0)),
        spec((2, pols, 1, 1, 16, feeds), pre_map(1)),
        spec((2, pols, 1, 1, 16, feeds), pre_map(2)),
        spec((2, pols, 1, 48, feeds), lambda t: (0, 0, 0, 0, 0)),
        spec((2, pols, 1, feeds), lambda t: (0, 0, 0, 0)),
        spec(band.shape, lambda t: (0, 0)),
    ] + [spec((1, 1, U, 128), lambda t: (0, 0, 0, 0)) for _ in extra]
    grid_spec = pltpu.PrefetchScalarGridSpec(
        num_scalar_prefetch=1 if shifted else 0, grid=(nblk,), in_specs=in_specs, out_specs=out_spec
    )
    lead = [me] if shifted else []
    return pl.pallas_call(
        lambda *refs: _filter_kernel(chunk, shifted, *refs),
        grid_spec=grid_spec,
        out_shape=jax.ShapeDtypeStruct((nblk, nb, 2, pols, IB, TINT, U, feeds), jnp.bfloat16),
        cost_estimate=pl.CostEstimate(
            flops=2 * band.size * feeds * pols * nblk * nb,
            bytes_accessed=2 * voltages.size * 2 // chunks,
            transcendentals=0,
        ),
    )(*lead, main, units, units, units, history, gains, band, *extra)


def _beam_kernel(cal_ref, w_ref, sel_ref, out_ref):
    nsrc = cal_ref.shape[0]
    rows = 2 * 2 * IB * U
    halves = []
    for s in range(2):
        pieces = [cal_ref[d, 0, s].reshape(rows, 128) for d in range(nsrc)]
        halves.append(jnp.concatenate(pieces, axis=1))
    lhs = jnp.concatenate(halves, axis=0)
    prod_re = jnp.dot(lhs, w_ref[0, 0], preferred_element_type=jnp.float32)
    prod_im = jnp.dot(lhs, w_ref[1, 0], preferred_element_type=jnp.float32)
    real_part = prod_re[:rows] - prod_im[rows:]
    imag_part = prod_im[:rows] + prod_re[rows:]
    power = real_part * real_part + imag_part * imag_part
    quarter = rows // 2
    power = power[:quarter] + power[quarter:]
    power = power.reshape(IB, TINT, U, power.shape[-1])
    power = (power[:, 0] + power[:, 1]).reshape(IB * U, power.shape[-1])
    detected = (power * (1.0 / (4.0 * TINT))).astype(jnp.bfloat16)
    picked = jnp.dot(detected, sel_ref[...], preferred_element_type=jnp.float32).astype(jnp.bfloat16)
    nodes = out_ref.shape[0]
    for n in range(nodes):
        out_ref[n] = picked[:, n * 128 : (n + 1) * 128].reshape(IB, U, 128)


def _beam_pieces_kernel(count, *refs):
    refs = refs[:count + 2] + refs[-1:]

    class Stacked:
        def __getitem__(self, index):
            return refs[index[0]][(0,) + index[1:]]

    shape = (count,) + refs[0].shape[1:]
    stacked = Stacked()
    stacked.shape = shape
    _beam_kernel(stacked, *refs[count:])


def beamform_pieces(pieces, weights, select, after):
    nb = pieces[0].shape[1]
    feeds, beams = weights.shape[2], weights.shape[3]
    slots = select.shape[1]
    nodes = slots // 128
    piece_spec = pl.BlockSpec((1, 1, 2, 2, IB, TINT, U, 128), lambda i: (0, i, 0, 0, 0, 0, 0, 0))
    return pl.pallas_call(
        lambda *refs: _beam_pieces_kernel(len(pieces), *refs),
        grid=(nb,),
        in_specs=[piece_spec] * len(pieces)
        + [
            pl.BlockSpec((2, 1, feeds, beams), lambda i: (0, 0, 0, 0)),
            pl.BlockSpec((beams, slots), lambda i: (0, 0)),
            pl.BlockSpec((1, 1, U, 128), lambda i: (0, 0, 0, 0)),
        ],
        out_specs=pl.BlockSpec((nodes, IB, U, 128), lambda i: (0, i, 0, 0)),
        out_shape=jax.ShapeDtypeStruct((nodes, nb * IB, U, 128), jnp.bfloat16),
        cost_estimate=pl.CostEstimate(
            flops=2 * 2 * (4 * nb * IB * U * TINT) * feeds * beams + 2 * nb * IB * U * beams * slots,
            bytes_accessed=sum(p.size for p in pieces) * 2 + weights.size * 2 + select.size * 2 + nb * IB * U * slots * 2,
            transcendentals=0,
        ),
        compiler_params=pltpu.CompilerParams(vmem_limit_bytes=60 * 1024 * 1024),
    )(*pieces, weights, select, after)


def beamform(cal, weights, select):
    nsrc, nb = cal.shape[0], cal.shape[1]
    feeds, beams = weights.shape[2], weights.shape[3]
    slots = select.shape[1]
    nodes = slots // 128
    return pl.pallas_call(
        _beam_kernel,
        grid=(nb,),
        in_specs=[
            pl.BlockSpec((nsrc, 1, 2, 2, IB, TINT, U, 128), lambda i: (0, i, 0, 0, 0, 0, 0, 0)),
            pl.BlockSpec((2, 1, feeds, beams), lambda i: (0, 0, 0, 0)),
            pl.BlockSpec((beams, slots), lambda i: (0, 0)),
        ],
        out_specs=pl.BlockSpec((nodes, IB, U, 128), lambda i: (0, i, 0, 0)),
        out_shape=jax.ShapeDtypeStruct((nodes, nb * IB, U, 128), jnp.bfloat16),
        cost_estimate=pl.CostEstimate(
            flops=2 * 2 * (4 * nb * IB * U * TINT) * feeds * beams + 2 * nb * IB * U * beams * slots,
            bytes_accessed=cal.size * 2 + weights.size * 2 + select.size * 2 + nb * IB * U * slots * 2,
            transcendentals=0,
        ),
        compiler_params=pltpu.CompilerParams(vmem_limit_bytes=60 * 1024 * 1024),
    )(cal, weights, select)


def on_device(voltages, history, gains, weights, beam_lists, beam_counts):
    capacity = beam_lists.shape[1]
    beams = weights.shape[3]
    flat_ids = beam_lists.reshape(-1)
    live_slots = (jnp.arange(capacity, dtype=jnp.int32)[None, :] < beam_counts[:, None]).reshape(-1)
    select = (
        (jnp.arange(beams, dtype=jnp.int32)[:, None] == flat_ids[None, :]) & live_slots[None, :]
    ).astype(jnp.bfloat16)
    band = jnp.asarray(band_matrix())
    nfeed = lax.axis_size("feed")
    me = lax.axis_index("feed")
    order = lax.rem(me - jnp.arange(nfeed, dtype=jnp.int32) + nfeed, nfeed)
    feeds_local = weights.shape[2] // nfeed
    wperm = jnp.take(weights.reshape(2, 1, nfeed, feeds_local, beams), order, axis=2).reshape(weights.shape)
    first = filterbank(voltages, history, gains, band, 0, CHUNKS)
    gathered = lax.all_to_all(first, "feed", split_axis=0, concat_axis=0, tiled=True)
    second = filterbank(voltages, history, gains, band, 1, CHUNKS, me=me.astype(jnp.int32).reshape(1))
    pieces = [second[0:1]]
    for shift in range(1, nfeed):
        pairs = [(i, (i + shift) % nfeed) for i in range(nfeed)]
        pieces.append(lax.ppermute(second[shift : shift + 1], "feed", perm=pairs))
    outs = []
    picked = beamform(gathered, weights, select)
    outs.append(lax.all_to_all(picked, "chan", split_axis=0, concat_axis=0, tiled=True))
    picked = beamform_pieces(pieces, wperm, select, outs[0].reshape(-1, 1, U, 128))
    outs.append(lax.all_to_all(picked, "chan", split_axis=0, concat_axis=0, tiled=True))
    exchanged = jnp.concatenate(outs, axis=1)
    nodes, bins, fine, width = exchanged.shape
    return jnp.transpose(exchanged, (1, 0, 2, 3)).reshape(bins, nodes * fine, width)


def solution(mesh):
    in_specs = (
        P(None, None, "chan", None, "feed"),
        P(None, None, "chan", None, "feed"),
        P(None, None, "chan", "feed"),
        P(None, "chan", None, None),
        P(),
        P(),
    )
    out_specs = P("feed", None, "chan")
    return jax.shard_map(
        on_device, mesh=mesh, in_specs=in_specs, out_specs=out_specs, check_vma=False
    )
```

```python
import math

import numpy as np
import jax
import jax.numpy as jnp
from jax import lax
from jax.experimental import pallas as pl
from jax.experimental.pallas import tpu as pltpu
from jax.sharding import PartitionSpec as P

U = 16
TAPS = 4
TINT = 2
IB = 4
CHUNKS = 2
FRAMES = 2 * IB


def window_taps_np():
    length = TAPS * U
    positions = np.arange(length, dtype=np.float64)
    offsets = (positions - (length - 1) / 2.0) / U
    hann_taper = 0.5 - 0.5 * np.cos(2.0 * math.pi * (positions + 0.5) / length)
    taps_window = np.sinc(offsets) * hann_taper
    taps_window = taps_window / np.sqrt(np.sum(taps_window * taps_window) / U)
    return taps_window.astype(np.float32)


def band_matrix():
    taps = window_taps_np().astype(np.float64)
    span = (FRAMES + TAPS - 1) * U
    index_n = np.arange(U)
    phases = 2.0 * math.pi * ((index_n[:, None] * index_n[None, :]) % U) / U
    cosine = np.cos(phases) / math.sqrt(U)
    sine = np.sin(phases) / math.sqrt(U)
    table = np.array([[cosine, -sine], [sine, cosine]])
    band = np.zeros((2, FRAMES, U, 2, span))
    for t in range(FRAMES):
        for m in range(TAPS * U):
            for r in range(2):
                band[:, t, :, r, t * U + m] = taps[m] * table[r, :, m % U, :]
    band = band.reshape(2 * FRAMES * U, 2 * span).astype(np.float32)
    high = band.astype(jnp.bfloat16)
    low = (band - high.astype(np.float32)).astype(jnp.bfloat16)
    return np.concatenate([high, low], axis=0)


def _filter_kernel(chunk, shifted, *refs):
    if shifted:
        refs = refs[1:]
    _filter_body(chunk, *refs)


def _filter_body(chunk, main_ref, pre0_ref, pre1_ref, pre2_ref, hist_ref, gain_ref, band_ref, *rest):
    out_ref = rest[-1]
    tdev = pl.program_id(0)
    rows_main = main_ref.shape[4]
    nb = out_ref.shape[1]
    span = (FRAMES + TAPS - 1) * U
    half = FRAMES * U
    lanes = main_ref.shape[5]
    g_re = jnp.concatenate([gain_ref[0, p] for p in range(2)], axis=1)
    g_im = jnp.concatenate([gain_ref[1, p] for p in range(2)], axis=1)

    def rows_of(r, start, size):
        return jnp.concatenate([main_ref[r, p, 0, 0, pl.ds(start, size), :] for p in range(2)], axis=1)

    def prefix_of(r):
        pre = [jnp.concatenate([ref[r, p, 0, 0] for p in range(2)], axis=1) for ref in (pre0_ref, pre1_ref, pre2_ref)]
        pre = jnp.concatenate(pre, axis=0)
        if chunk == 0:
            hist = jnp.concatenate([hist_ref[r, p, 0] for p in range(2)], axis=1)
            pre = jnp.where(tdev == 0, hist, pre)
        return pre

    for ib in range(nb):
        parts = []
        for r in range(2):
            if ib == 0:
                parts.append(jnp.concatenate([prefix_of(r), rows_of(r, 0, span - 48)], axis=0))
            else:
                parts.append(rows_of(r, ib * half - 48, span))
        rhs = jnp.concatenate(parts, axis=0)
        both = jnp.dot(band_ref[...], rhs, preferred_element_type=jnp.float32)
        rows = both.shape[0] // 2
        spec = both[:rows] + both[rows:]
        s_re = spec[:half]
        s_im = spec[half:]
        c_re = (g_re * s_re - g_im * s_im).astype(jnp.bfloat16)
        c_im = (g_re * s_im + g_im * s_re).astype(jnp.bfloat16)
        for p in range(2):
            out_ref[0, ib, 0, p] = c_re[:, p * lanes : (p + 1) * lanes].reshape(IB, TINT, U, lanes)
            out_ref[0, ib, 1, p] = c_im[:, p * lanes : (p + 1) * lanes].reshape(IB, TINT, U, lanes)


def filterbank(voltages, history, gains, band, chunk, chunks, after=None, me=None):
    _, pols, _, samples, feeds = voltages.shape
    nblk = 8
    rows_blk = samples // nblk
    rows_main = rows_blk // chunks
    nb = rows_main // U // FRAMES
    main = voltages.reshape(2, pols, nblk, chunks, rows_main, feeds)
    units = voltages.reshape(2, pols, nblk, rows_blk // 16, 16, feeds)

    def pre_map(m):
        if chunk == 0:
            return lambda t: (0, 0, jnp.maximum(t - 1, 0), rows_blk // 16 - 3 + m, 0, 0)
        return lambda t: (0, 0, t, chunk * rows_main // 16 - 3 + m, 0, 0)

    extra = [] if after is None else [after]
    shifted = me is not None

    def spec(shape, index):
        if shifted:
            return pl.BlockSpec(shape, lambda t, me_ref: index(t))
        return pl.BlockSpec(shape, index)

    if shifted:
        out_spec = pl.BlockSpec(
            (1, nb, 2, pols, IB, TINT, U, feeds),
            lambda t, me_ref: (lax.rem(t - me_ref[0] + nblk, nblk), 0, 0, 0, 0, 0, 0, 0),
        )
    else:
        out_spec = pl.BlockSpec((1, nb, 2, pols, IB, TINT, U, feeds), lambda t: (t, 0, 0, 0, 0, 0, 0, 0))
    in_specs = [
        spec((2, pols, 1, 1, rows_main, feeds), lambda t: (0, 0, t, chunk, 0, 0)),
        spec((2, pols, 1, 1, 16, feeds), pre_map(0)),
        spec((2, pols, 1, 1, 16, feeds), pre_map(1)),
        spec((2, pols, 1, 1, 16, feeds), pre_map(2)),
        spec((2, pols, 1, 48, feeds), lambda t: (0, 0, 0, 0, 0)),
        spec((2, pols, 1, feeds), lambda t: (0, 0, 0, 0)),
        spec(band.shape, lambda t: (0, 0)),
    ] + [spec((1, 1, U, 128), lambda t: (0, 0, 0, 0)) for _ in extra]
    grid_spec = pltpu.PrefetchScalarGridSpec(
        num_scalar_prefetch=1 if shifted else 0, grid=(nblk,), in_specs=in_specs, out_specs=out_spec
    )
    lead = [me] if shifted else []
    return pl.pallas_call(
        lambda *refs: _filter_kernel(chunk, shifted, *refs),
        grid_spec=grid_spec,
        out_shape=jax.ShapeDtypeStruct((nblk, nb, 2, pols, IB, TINT, U, feeds), jnp.bfloat16),
        cost_estimate=pl.CostEstimate(
            flops=2 * band.size * feeds * pols * nblk * nb,
            bytes_accessed=2 * voltages.size * 2 // chunks,
            transcendentals=0,
        ),
    )(*lead, main, units, units, units, history, gains, band, *extra)


def _beam_kernel(cal_ref, w_ref, sel_ref, out_ref):
    nsrc = cal_ref.shape[0]
    rows = 2 * 2 * IB * U
    halves = []
    for s in range(2):
        pieces = [cal_ref[d, 0, s].reshape(rows, 128) for d in range(nsrc)]
        halves.append(jnp.concatenate(pieces, axis=1))
    lhs = jnp.concatenate(halves, axis=0)
    prod_re = jnp.dot(lhs, w_ref[0, 0], preferred_element_type=jnp.float32)
    prod_im = jnp.dot(lhs, w_ref[1, 0], preferred_element_type=jnp.float32)
    real_part = prod_re[:rows] - prod_im[rows:]
    imag_part = prod_im[:rows] + prod_re[rows:]
    power = real_part * real_part + imag_part * imag_part
    quarter = rows // 2
    power = power[:quarter] + power[quarter:]
    power = power.reshape(IB, TINT, U, power.shape[-1])
    power = (power[:, 0] + power[:, 1]).reshape(IB * U, power.shape[-1])
    detected = (power * (1.0 / (4.0 * TINT))).astype(jnp.bfloat16)
    picked = jnp.dot(detected, sel_ref[...], preferred_element_type=jnp.float32).astype(jnp.bfloat16)
    nodes = out_ref.shape[0]
    for n in range(nodes):
        out_ref[n] = picked[:, n * 128 : (n + 1) * 128].reshape(IB, U, 128)


def _beam_pieces_kernel(count, *refs):
    refs = refs[:count + 2] + refs[-1:]

    class Stacked:
        def __getitem__(self, index):
            return refs[index[0]][(0,) + index[1:]]

    shape = (count,) + refs[0].shape[1:]
    stacked = Stacked()
    stacked.shape = shape
    _beam_kernel(stacked, *refs[count:])


def beamform_pieces(pieces, weights, select, after):
    nb = pieces[0].shape[1]
    feeds, beams = weights.shape[2], weights.shape[3]
    slots = select.shape[1]
    nodes = slots // 128
    piece_spec = pl.BlockSpec((1, 1, 2, 2, IB, TINT, U, 128), lambda i: (0, i, 0, 0, 0, 0, 0, 0))
    return pl.pallas_call(
        lambda *refs: _beam_pieces_kernel(len(pieces), *refs),
        grid=(nb,),
        in_specs=[piece_spec] * len(pieces)
        + [
            pl.BlockSpec((2, 1, feeds, beams), lambda i: (0, 0, 0, 0)),
            pl.BlockSpec((beams, slots), lambda i: (0, 0)),
            pl.BlockSpec((1, 1, U, 128), lambda i: (0, 0, 0, 0)),
        ],
        out_specs=pl.BlockSpec((nodes, IB, U, 128), lambda i: (0, i, 0, 0)),
        out_shape=jax.ShapeDtypeStruct((nodes, nb * IB, U, 128), jnp.bfloat16),
        cost_estimate=pl.CostEstimate(
            flops=2 * 2 * (4 * nb * IB * U * TINT) * feeds * beams + 2 * nb * IB * U * beams * slots,
            bytes_accessed=sum(p.size for p in pieces) * 2 + weights.size * 2 + select.size * 2 + nb * IB * U * slots * 2,
            transcendentals=0,
        ),
        compiler_params=pltpu.CompilerParams(vmem_limit_bytes=60 * 1024 * 1024),
    )(*pieces, weights, select, after)


def beamform(cal, weights, select):
    nsrc, nb = cal.shape[0], cal.shape[1]
    feeds, beams = weights.shape[2], weights.shape[3]
    slots = select.shape[1]
    nodes = slots // 128
    return pl.pallas_call(
        _beam_kernel,
        grid=(nb,),
        in_specs=[
            pl.BlockSpec((nsrc, 1, 2, 2, IB, TINT, U, 128), lambda i: (0, i, 0, 0, 0, 0, 0, 0)),
            pl.BlockSpec((2, 1, feeds, beams), lambda i: (0, 0, 0, 0)),
            pl.BlockSpec((beams, slots), lambda i: (0, 0)),
        ],
        out_specs=pl.BlockSpec((nodes, IB, U, 128), lambda i: (0, i, 0, 0)),
        out_shape=jax.ShapeDtypeStruct((nodes, nb * IB, U, 128), jnp.bfloat16),
        cost_estimate=pl.CostEstimate(
            flops=2 * 2 * (4 * nb * IB * U * TINT) * feeds * beams + 2 * nb * IB * U * beams * slots,
            bytes_accessed=cal.size * 2 + weights.size * 2 + select.size * 2 + nb * IB * U * slots * 2,
            transcendentals=0,
        ),
        compiler_params=pltpu.CompilerParams(vmem_limit_bytes=60 * 1024 * 1024),
    )(cal, weights, select)


def on_device(voltages, history, gains, weights, beam_lists, beam_counts):
    capacity = beam_lists.shape[1]
    beams = weights.shape[3]
    flat_ids = beam_lists.reshape(-1)
    live_slots = (jnp.arange(capacity, dtype=jnp.int32)[None, :] < beam_counts[:, None]).reshape(-1)
    select = (
        (jnp.arange(beams, dtype=jnp.int32)[:, None] == flat_ids[None, :]) & live_slots[None, :]
    ).astype(jnp.bfloat16)
    band = jnp.asarray(band_matrix())
    nfeed = lax.axis_size("feed")
    me = lax.axis_index("feed")
    order = lax.rem(me - jnp.arange(nfeed, dtype=jnp.int32) + nfeed, nfeed)
    feeds_local = weights.shape[2] // nfeed
    wperm = jnp.take(weights.reshape(2, 1, nfeed, feeds_local, beams), order, axis=2).reshape(weights.shape)
    first = filterbank(voltages, history, gains, band, 0, CHUNKS)
    gathered = lax.all_to_all(first, "feed", split_axis=0, concat_axis=0, tiled=True)
    second = filterbank(voltages, history, gains, band, 1, CHUNKS, me=me.astype(jnp.int32).reshape(1))
    pieces = [second[0:1]]
    for shift in range(1, nfeed):
        pairs = [(i, (i + shift) % nfeed) for i in range(nfeed)]
        pieces.append(lax.ppermute(second[shift : shift + 1], "feed", perm=pairs))
    outs = []
    picked = beamform(gathered, weights, select)
    outs.append(lax.all_to_all(picked, "chan", split_axis=0, concat_axis=0, tiled=True))
    picked = beamform_pieces(pieces, wperm, select, outs[0].reshape(-1, 1, U, 128))
    outs.append(lax.all_to_all(picked, "chan", split_axis=0, concat_axis=0, tiled=True))
    nodes, part, fine, width = outs[0].shape
    bins = part * len(outs)
    first_part = jnp.transpose(outs[0], (1, 0, 2, 3)).reshape(part, nodes * fine, width)
    result = lax.optimization_barrier(jnp.pad(first_part, ((0, bins - part), (0, 0), (0, 0))))
    last_part = jnp.transpose(outs[1], (1, 0, 2, 3)).reshape(part, nodes * fine, width)
    return lax.dynamic_update_slice_in_dim(result, last_part, part, axis=0)


def solution(mesh):
    in_specs = (
        P(None, None, "chan", None, "feed"),
        P(None, None, "chan", None, "feed"),
        P(None, None, "chan", "feed"),
        P(None, "chan", None, None),
        P(),
        P(),
    )
    out_specs = P("feed", None, "chan")
    return jax.shard_map(
        on_device, mesh=mesh, in_specs=in_specs, out_specs=out_specs, check_vma=False
    )
```

```python
import math

import numpy as np
import jax
import jax.numpy as jnp
from jax import lax
from jax.experimental import pallas as pl
from jax.experimental.pallas import tpu as pltpu
from jax.sharding import PartitionSpec as P

U = 16
TAPS = 4
TINT = 2
IB = 4
CHUNKS = 2
FRAMES = 2 * IB


def window_taps_np():
    length = TAPS * U
    positions = np.arange(length, dtype=np.float64)
    offsets = (positions - (length - 1) / 2.0) / U
    hann_taper = 0.5 - 0.5 * np.cos(2.0 * math.pi * (positions + 0.5) / length)
    taps_window = np.sinc(offsets) * hann_taper
    taps_window = taps_window / np.sqrt(np.sum(taps_window * taps_window) / U)
    return taps_window.astype(np.float32)


def band_matrix():
    taps = window_taps_np().astype(np.float64)
    span = (FRAMES + TAPS - 1) * U
    index_n = np.arange(U)
    phases = 2.0 * math.pi * ((index_n[:, None] * index_n[None, :]) % U) / U
    cosine = np.cos(phases) / math.sqrt(U)
    sine = np.sin(phases) / math.sqrt(U)
    table = np.array([[cosine, -sine], [sine, cosine]])
    band = np.zeros((2, FRAMES, U, 2, span))
    for t in range(FRAMES):
        for m in range(TAPS * U):
            for r in range(2):
                band[:, t, :, r, t * U + m] = taps[m] * table[r, :, m % U, :]
    band = band.reshape(2 * FRAMES * U, 2 * span).astype(np.float32)
    high = band.astype(jnp.bfloat16)
    low = (band - high.astype(np.float32)).astype(jnp.bfloat16)
    return np.concatenate([high, low], axis=0)


def _filter_kernel(chunk, shifted, *refs):
    if shifted:
        refs = refs[1:]
    _filter_body(chunk, *refs)


def _filter_body(chunk, main_ref, pre0_ref, pre1_ref, pre2_ref, hist_ref, gain_ref, band_ref, *rest):
    out_ref = rest[-1]
    tdev = pl.program_id(0)
    rows_main = main_ref.shape[4]
    nb = out_ref.shape[1]
    span = (FRAMES + TAPS - 1) * U
    half = FRAMES * U
    lanes = main_ref.shape[5]
    g_re = jnp.concatenate([gain_ref[0, p] for p in range(2)], axis=1)
    g_im = jnp.concatenate([gain_ref[1, p] for p in range(2)], axis=1)

    def rows_of(r, start, size):
        return jnp.concatenate([main_ref[r, p, 0, 0, pl.ds(start, size), :] for p in range(2)], axis=1)

    def prefix_of(r):
        pre = [jnp.concatenate([ref[r, p, 0, 0] for p in range(2)], axis=1) for ref in (pre0_ref, pre1_ref, pre2_ref)]
        pre = jnp.concatenate(pre, axis=0)
        if chunk == 0:
            hist = jnp.concatenate([hist_ref[r, p, 0] for p in range(2)], axis=1)
            pre = jnp.where(tdev == 0, hist, pre)
        return pre

    for ib in range(nb):
        parts = []
        for r in range(2):
            if ib == 0:
                parts.append(jnp.concatenate([prefix_of(r), rows_of(r, 0, span - 48)], axis=0))
            else:
                parts.append(rows_of(r, ib * half - 48, span))
        rhs = jnp.concatenate(parts, axis=0)
        both = jnp.dot(band_ref[...], rhs, preferred_element_type=jnp.float32)
        rows = both.shape[0] // 2
        spec = both[:rows] + both[rows:]
        s_re = spec[:half]
        s_im = spec[half:]
        c_re = (g_re * s_re - g_im * s_im).astype(jnp.bfloat16)
        c_im = (g_re * s_im + g_im * s_re).astype(jnp.bfloat16)
        for p in range(2):
            out_ref[0, ib, 0, p] = c_re[:, p * lanes : (p + 1) * lanes].reshape(IB, TINT, U, lanes)
            out_ref[0, ib, 1, p] = c_im[:, p * lanes : (p + 1) * lanes].reshape(IB, TINT, U, lanes)


def filterbank(voltages, history, gains, band, chunk, chunks, after=None, me=None):
    _, pols, _, samples, feeds = voltages.shape
    nblk = 8
    rows_blk = samples // nblk
    rows_main = rows_blk // chunks
    nb = rows_main // U // FRAMES
    main = voltages.reshape(2, pols, nblk, chunks, rows_main, feeds)
    units = voltages.reshape(2, pols, nblk, rows_blk // 16, 16, feeds)

    def pre_map(m):
        if chunk == 0:
            return lambda t: (0, 0, jnp.maximum(t - 1, 0), rows_blk // 16 - 3 + m, 0, 0)
        return lambda t: (0, 0, t, chunk * rows_main // 16 - 3 + m, 0, 0)

    extra = [] if after is None else [after]
    shifted = me is not None

    def spec(shape, index):
        if shifted:
            return pl.BlockSpec(shape, lambda t, me_ref: index(t))
        return pl.BlockSpec(shape, index)

    if shifted:
        out_spec = pl.BlockSpec(
            (1, nb, 2, pols, IB, TINT, U, feeds),
            lambda t, me_ref: (lax.rem(t - me_ref[0] + nblk, nblk), 0, 0, 0, 0, 0, 0, 0),
        )
    else:
        out_spec = pl.BlockSpec((1, nb, 2, pols, IB, TINT, U, feeds), lambda t: (t, 0, 0, 0, 0, 0, 0, 0))
    in_specs = [
        spec((2, pols, 1, 1, rows_main, feeds), lambda t: (0, 0, t, chunk, 0, 0)),
        spec((2, pols, 1, 1, 16, feeds), pre_map(0)),
        spec((2, pols, 1, 1, 16, feeds), pre_map(1)),
        spec((2, pols, 1, 1, 16, feeds), pre_map(2)),
        spec((2, pols, 1, 48, feeds), lambda t: (0, 0, 0, 0, 0)),
        spec((2, pols, 1, feeds), lambda t: (0, 0, 0, 0)),
        spec(band.shape, lambda t: (0, 0)),
    ] + [spec((1, 1, U, 128), lambda t: (0, 0, 0, 0)) for _ in extra]
    grid_spec = pltpu.PrefetchScalarGridSpec(
        num_scalar_prefetch=1 if shifted else 0, grid=(nblk,), in_specs=in_specs, out_specs=out_spec
    )
    lead = [me] if shifted else []
    return pl.pallas_call(
        lambda *refs: _filter_kernel(chunk, shifted, *refs),
        grid_spec=grid_spec,
        out_shape=jax.ShapeDtypeStruct((nblk, nb, 2, pols, IB, TINT, U, feeds), jnp.bfloat16),
        cost_estimate=pl.CostEstimate(
            flops=2 * band.size * feeds * pols * nblk * nb,
            bytes_accessed=2 * voltages.size * 2 // chunks,
            transcendentals=0,
        ),
    )(*lead, main, units, units, units, history, gains, band, *extra)


def _beam_kernel(cal_ref, w_ref, sel_ref, out_ref):
    nsrc = cal_ref.shape[0]
    rows = 2 * 2 * IB * U
    halves = []
    for s in range(2):
        pieces = [cal_ref[d, 0, s].reshape(rows, 128) for d in range(nsrc)]
        halves.append(jnp.concatenate(pieces, axis=1))
    lhs = jnp.concatenate(halves, axis=0)
    prod_re = jnp.dot(lhs, w_ref[0, 0], preferred_element_type=jnp.float32)
    prod_im = jnp.dot(lhs, w_ref[1, 0], preferred_element_type=jnp.float32)
    real_part = prod_re[:rows] - prod_im[rows:]
    imag_part = prod_im[:rows] + prod_re[rows:]
    power = real_part * real_part + imag_part * imag_part
    quarter = rows // 2
    power = power[:quarter] + power[quarter:]
    power = power.reshape(IB, TINT, U, power.shape[-1])
    power = (power[:, 0] + power[:, 1]).reshape(IB * U, power.shape[-1])
    detected = (power * (1.0 / (4.0 * TINT))).astype(jnp.bfloat16)
    picked = jnp.dot(detected, sel_ref[...], preferred_element_type=jnp.float32).astype(jnp.bfloat16)
    nodes = out_ref.shape[0]
    for n in range(nodes):
        out_ref[n] = picked[:, n * 128 : (n + 1) * 128].reshape(IB, U, 128)


def _beam_pieces_kernel(count, *refs):
    refs = refs[:count + 2] + refs[-1:]

    class Stacked:
        def __getitem__(self, index):
            return refs[index[0]][(0,) + index[1:]]

    shape = (count,) + refs[0].shape[1:]
    stacked = Stacked()
    stacked.shape = shape
    _beam_kernel(stacked, *refs[count:])


def beamform_pieces(pieces, weights, select, after):
    nb = pieces[0].shape[1]
    feeds, beams = weights.shape[2], weights.shape[3]
    slots = select.shape[1]
    nodes = slots // 128
    piece_spec = pl.BlockSpec((1, 1, 2, 2, IB, TINT, U, 128), lambda i: (0, i, 0, 0, 0, 0, 0, 0))
    return pl.pallas_call(
        lambda *refs: _beam_pieces_kernel(len(pieces), *refs),
        grid=(nb,),
        in_specs=[piece_spec] * len(pieces)
        + [
            pl.BlockSpec((2, 1, feeds, beams), lambda i: (0, 0, 0, 0)),
            pl.BlockSpec((beams, slots), lambda i: (0, 0)),
            pl.BlockSpec((1, 1, U, 128), lambda i: (0, 0, 0, 0)),
        ],
        out_specs=pl.BlockSpec((nodes, IB, U, 128), lambda i: (0, i, 0, 0)),
        out_shape=jax.ShapeDtypeStruct((nodes, nb * IB, U, 128), jnp.bfloat16),
        cost_estimate=pl.CostEstimate(
            flops=2 * 2 * (4 * nb * IB * U * TINT) * feeds * beams + 2 * nb * IB * U * beams * slots,
            bytes_accessed=sum(p.size for p in pieces) * 2 + weights.size * 2 + select.size * 2 + nb * IB * U * slots * 2,
            transcendentals=0,
        ),
        compiler_params=pltpu.CompilerParams(vmem_limit_bytes=60 * 1024 * 1024),
    )(*pieces, weights, select, after)


def beamform(cal, weights, select, after=()):
    nsrc, nb = cal.shape[0], cal.shape[1]
    feeds, beams = weights.shape[2], weights.shape[3]
    slots = select.shape[1]
    nodes = slots // 128
    return pl.pallas_call(
        lambda *refs: _beam_kernel(*refs[:3], refs[-1]),
        grid=(nb,),
        in_specs=[
            pl.BlockSpec((nsrc, 1, 2, 2, IB, TINT, U, 128), lambda i: (0, i, 0, 0, 0, 0, 0, 0)),
            pl.BlockSpec((2, 1, feeds, beams), lambda i: (0, 0, 0, 0)),
            pl.BlockSpec((beams, slots), lambda i: (0, 0)),
        ]
        + [pl.BlockSpec((1, 1, U, 128), lambda i: (0, 0, 0, 0)) for _ in after],
        out_specs=pl.BlockSpec((nodes, IB, U, 128), lambda i: (0, i, 0, 0)),
        out_shape=jax.ShapeDtypeStruct((nodes, nb * IB, U, 128), jnp.bfloat16),
        cost_estimate=pl.CostEstimate(
            flops=2 * 2 * (4 * nb * IB * U * TINT) * feeds * beams + 2 * nb * IB * U * beams * slots,
            bytes_accessed=cal.size * 2 + weights.size * 2 + select.size * 2 + nb * IB * U * slots * 2,
            transcendentals=0,
        ),
        compiler_params=pltpu.CompilerParams(vmem_limit_bytes=60 * 1024 * 1024),
    )(cal, weights, select, *after)


def on_device(voltages, history, gains, weights, beam_lists, beam_counts):
    capacity = beam_lists.shape[1]
    beams = weights.shape[3]
    flat_ids = beam_lists.reshape(-1)
    live_slots = (jnp.arange(capacity, dtype=jnp.int32)[None, :] < beam_counts[:, None]).reshape(-1)
    select = (
        (jnp.arange(beams, dtype=jnp.int32)[:, None] == flat_ids[None, :]) & live_slots[None, :]
    ).astype(jnp.bfloat16)
    band = jnp.asarray(band_matrix())
    nfeed = lax.axis_size("feed")
    me = lax.axis_index("feed")
    order = lax.rem(me - jnp.arange(nfeed, dtype=jnp.int32) + nfeed, nfeed)
    feeds_local = weights.shape[2] // nfeed
    wperm = jnp.take(weights.reshape(2, 1, nfeed, feeds_local, beams), order, axis=2).reshape(weights.shape)
    first = filterbank(voltages, history, gains, band, 0, CHUNKS)
    gathered = lax.all_to_all(first, "feed", split_axis=0, concat_axis=0, tiled=True)
    second = filterbank(voltages, history, gains, band, 1, CHUNKS, me=me.astype(jnp.int32).reshape(1))
    pieces = [second[0:1]]
    for shift in range(1, nfeed):
        pairs = [(i, (i + shift) % nfeed) for i in range(nfeed)]
        pieces.append(lax.ppermute(second[shift : shift + 1], "feed", perm=pairs))
    outs = []
    picked = beamform(gathered, weights, select, [p.reshape(-1, 1, U, 128) for p in pieces[1:3]])
    outs.append(lax.all_to_all(picked, "chan", split_axis=0, concat_axis=0, tiled=True))
    picked = beamform_pieces(pieces, wperm, select, outs[0].reshape(-1, 1, U, 128))
    outs.append(lax.all_to_all(picked, "chan", split_axis=0, concat_axis=0, tiled=True))
    nodes, part, fine, width = outs[0].shape
    bins = part * len(outs)
    first_part = jnp.transpose(outs[0], (1, 0, 2, 3)).reshape(part, nodes * fine, width)
    result = lax.optimization_barrier(jnp.pad(first_part, ((0, bins - part), (0, 0), (0, 0))))
    last_part = jnp.transpose(outs[1], (1, 0, 2, 3)).reshape(part, nodes * fine, width)
    return lax.dynamic_update_slice_in_dim(result, last_part, part, axis=0)


def solution(mesh):
    in_specs = (
        P(None, None, "chan", None, "feed"),
        P(None, None, "chan", None, "feed"),
        P(None, None, "chan", "feed"),
        P(None, "chan", None, None),
        P(),
        P(),
    )
    out_specs = P("feed", None, "chan")
    return jax.shard_map(
        on_device, mesh=mesh, in_specs=in_specs, out_specs=out_specs, check_vma=False
    )
```

```python
import math

import numpy as np
import jax
import jax.numpy as jnp
from jax import lax
from jax.experimental import pallas as pl
from jax.experimental.pallas import tpu as pltpu
from jax.sharding import PartitionSpec as P

U = 16
TAPS = 4
TINT = 2
IB = 4
CHUNKS = 2
FRAMES = 2 * IB


def window_taps_np():
    length = TAPS * U
    positions = np.arange(length, dtype=np.float64)
    offsets = (positions - (length - 1) / 2.0) / U
    hann_taper = 0.5 - 0.5 * np.cos(2.0 * math.pi * (positions + 0.5) / length)
    taps_window = np.sinc(offsets) * hann_taper
    taps_window = taps_window / np.sqrt(np.sum(taps_window * taps_window) / U)
    return taps_window.astype(np.float32)


def band_matrix():
    taps = window_taps_np().astype(np.float64)
    span = (FRAMES + TAPS - 1) * U
    index_n = np.arange(U)
    phases = 2.0 * math.pi * ((index_n[:, None] * index_n[None, :]) % U) / U
    cosine = np.cos(phases) / math.sqrt(U)
    sine = np.sin(phases) / math.sqrt(U)
    table = np.array([[cosine, -sine], [sine, cosine]])
    band = np.zeros((2, FRAMES, U, 2, span))
    for t in range(FRAMES):
        for m in range(TAPS * U):
            for r in range(2):
                band[:, t, :, r, t * U + m] = taps[m] * table[r, :, m % U, :]
    band = band.reshape(2 * FRAMES * U, 2 * span).astype(np.float32)
    high = band.astype(jnp.bfloat16)
    low = (band - high.astype(np.float32)).astype(jnp.bfloat16)
    return np.concatenate([high, low], axis=1)


def _filter_kernel(chunk, shifted, *refs):
    if shifted:
        refs = refs[1:]
    _filter_body(chunk, *refs)


def _filter_body(chunk, main_ref, pre0_ref, pre1_ref, pre2_ref, hist_ref, gain_ref, band_ref, *rest):
    out_ref = rest[-1]
    tdev = pl.program_id(0)
    rows_main = main_ref.shape[4]
    nb = out_ref.shape[1]
    span = (FRAMES + TAPS - 1) * U
    half = FRAMES * U
    lanes = main_ref.shape[5]
    g_re = jnp.concatenate([gain_ref[0, p] for p in range(2)], axis=1)
    g_im = jnp.concatenate([gain_ref[1, p] for p in range(2)], axis=1)

    def rows_of(r, start, size):
        return jnp.concatenate([main_ref[r, p, 0, 0, pl.ds(start, size), :] for p in range(2)], axis=1)

    def prefix_of(r):
        pre = [jnp.concatenate([ref[r, p, 0, 0] for p in range(2)], axis=1) for ref in (pre0_ref, pre1_ref, pre2_ref)]
        pre = jnp.concatenate(pre, axis=0)
        if chunk == 0:
            hist = jnp.concatenate([hist_ref[r, p, 0] for p in range(2)], axis=1)
            pre = jnp.where(tdev == 0, hist, pre)
        return pre

    for ib in range(nb):
        parts = []
        for r in range(2):
            if ib == 0:
                parts.append(jnp.concatenate([prefix_of(r), rows_of(r, 0, span - 48)], axis=0))
            else:
                parts.append(rows_of(r, ib * half - 48, span))
        rhs = jnp.concatenate(parts + parts, axis=0)
        spec = jnp.dot(band_ref[...], rhs, preferred_element_type=jnp.float32)
        s_re = spec[:half]
        s_im = spec[half:]
        c_re = (g_re * s_re - g_im * s_im).astype(jnp.bfloat16)
        c_im = (g_re * s_im + g_im * s_re).astype(jnp.bfloat16)
        for p in range(2):
            out_ref[0, ib, 0, p] = c_re[:, p * lanes : (p + 1) * lanes].reshape(IB, TINT, U, lanes)
            out_ref[0, ib, 1, p] = c_im[:, p * lanes : (p + 1) * lanes].reshape(IB, TINT, U, lanes)


def filterbank(voltages, history, gains, band, chunk, chunks, after=None, me=None):
    _, pols, _, samples, feeds = voltages.shape
    nblk = 8
    rows_blk = samples // nblk
    rows_main = rows_blk // chunks
    nb = rows_main // U // FRAMES
    main = voltages.reshape(2, pols, nblk, chunks, rows_main, feeds)
    units = voltages.reshape(2, pols, nblk, rows_blk // 16, 16, feeds)

    def pre_map(m):
        if chunk == 0:
            return lambda t: (0, 0, jnp.maximum(t - 1, 0), rows_blk // 16 - 3 + m, 0, 0)
        return lambda t: (0, 0, t, chunk * rows_main // 16 - 3 + m, 0, 0)

    extra = [] if after is None else [after]
    shifted = me is not None

    def spec(shape, index):
        if shifted:
            return pl.BlockSpec(shape, lambda t, me_ref: index(t))
        return pl.BlockSpec(shape, index)

    if shifted:
        out_spec = pl.BlockSpec(
            (1, nb, 2, pols, IB, TINT, U, feeds),
            lambda t, me_ref: (lax.rem(t - me_ref[0] + nblk, nblk), 0, 0, 0, 0, 0, 0, 0),
        )
    else:
        out_spec = pl.BlockSpec((1, nb, 2, pols, IB, TINT, U, feeds), lambda t: (t, 0, 0, 0, 0, 0, 0, 0))
    in_specs = [
        spec((2, pols, 1, 1, rows_main, feeds), lambda t: (0, 0, t, chunk, 0, 0)),
        spec((2, pols, 1, 1, 16, feeds), pre_map(0)),
        spec((2, pols, 1, 1, 16, feeds), pre_map(1)),
        spec((2, pols, 1, 1, 16, feeds), pre_map(2)),
        spec((2, pols, 1, 48, feeds), lambda t: (0, 0, 0, 0, 0)),
        spec((2, pols, 1, feeds), lambda t: (0, 0, 0, 0)),
        spec(band.shape, lambda t: (0, 0)),
    ] + [spec((1, 1, U, 128), lambda t: (0, 0, 0, 0)) for _ in extra]
    grid_spec = pltpu.PrefetchScalarGridSpec(
        num_scalar_prefetch=1 if shifted else 0, grid=(nblk,), in_specs=in_specs, out_specs=out_spec
    )
    lead = [me] if shifted else []
    return pl.pallas_call(
        lambda *refs: _filter_kernel(chunk, shifted, *refs),
        grid_spec=grid_spec,
        out_shape=jax.ShapeDtypeStruct((nblk, nb, 2, pols, IB, TINT, U, feeds), jnp.bfloat16),
        cost_estimate=pl.CostEstimate(
            flops=2 * band.size * feeds * pols * nblk * nb,
            bytes_accessed=2 * voltages.size * 2 // chunks,
            transcendentals=0,
        ),
    )(*lead, main, units, units, units, history, gains, band, *extra)


def _beam_kernel(cal_ref, w_ref, sel_ref, out_ref):
    nsrc = cal_ref.shape[0]
    rows = 2 * 2 * IB * U
    halves = []
    for s in range(2):
        pieces = [cal_ref[d, 0, s].reshape(rows, 128) for d in range(nsrc)]
        halves.append(jnp.concatenate(pieces, axis=1))
    lhs = jnp.concatenate(halves, axis=0)
    prod_re = jnp.dot(lhs, w_ref[0, 0], preferred_element_type=jnp.float32)
    prod_im = jnp.dot(lhs, w_ref[1, 0], preferred_element_type=jnp.float32)
    real_part = prod_re[:rows] - prod_im[rows:]
    imag_part = prod_im[:rows] + prod_re[rows:]
    power = real_part * real_part + imag_part * imag_part
    quarter = rows // 2
    power = power[:quarter] + power[quarter:]
    power = power.reshape(IB, TINT, U, power.shape[-1])
    power = (power[:, 0] + power[:, 1]).reshape(IB * U, power.shape[-1])
    detected = (power * (1.0 / (4.0 * TINT))).astype(jnp.bfloat16)
    picked = jnp.dot(detected, sel_ref[...], preferred_element_type=jnp.float32).astype(jnp.bfloat16)
    nodes = out_ref.shape[0]
    for n in range(nodes):
        out_ref[n] = picked[:, n * 128 : (n + 1) * 128].reshape(IB, U, 128)


def _beam_pieces_kernel(count, *refs):
    refs = refs[:count + 2] + refs[-1:]

    class Stacked:
        def __getitem__(self, index):
            return refs[index[0]][(0,) + index[1:]]

    shape = (count,) + refs[0].shape[1:]
    stacked = Stacked()
    stacked.shape = shape
    _beam_kernel(stacked, *refs[count:])


def beamform_pieces(pieces, weights, select, after):
    nb = pieces[0].shape[1]
    feeds, beams = weights.shape[2], weights.shape[3]
    slots = select.shape[1]
    nodes = slots // 128
    piece_spec = pl.BlockSpec((1, 1, 2, 2, IB, TINT, U, 128), lambda i: (0, i, 0, 0, 0, 0, 0, 0))
    return pl.pallas_call(
        lambda *refs: _beam_pieces_kernel(len(pieces), *refs),
        grid=(nb,),
        in_specs=[piece_spec] * len(pieces)
        + [
            pl.BlockSpec((2, 1, feeds, beams), lambda i: (0, 0, 0, 0)),
            pl.BlockSpec((beams, slots), lambda i: (0, 0)),
            pl.BlockSpec((1, 1, U, 128), lambda i: (0, 0, 0, 0)),
        ],
        out_specs=pl.BlockSpec((nodes, IB, U, 128), lambda i: (0, i, 0, 0)),
        out_shape=jax.ShapeDtypeStruct((nodes, nb * IB, U, 128), jnp.bfloat16),
        cost_estimate=pl.CostEstimate(
            flops=2 * 2 * (4 * nb * IB * U * TINT) * feeds * beams + 2 * nb * IB * U * beams * slots,
            bytes_accessed=sum(p.size for p in pieces) * 2 + weights.size * 2 + select.size * 2 + nb * IB * U * slots * 2,
            transcendentals=0,
        ),
        compiler_params=pltpu.CompilerParams(vmem_limit_bytes=60 * 1024 * 1024),
    )(*pieces, weights, select, after)


def beamform(cal, weights, select):
    nsrc, nb = cal.shape[0], cal.shape[1]
    feeds, beams = weights.shape[2], weights.shape[3]
    slots = select.shape[1]
    nodes = slots // 128
    return pl.pallas_call(
        _beam_kernel,
        grid=(nb,),
        in_specs=[
            pl.BlockSpec((nsrc, 1, 2, 2, IB, TINT, U, 128), lambda i: (0, i, 0, 0, 0, 0, 0, 0)),
            pl.BlockSpec((2, 1, feeds, beams), lambda i: (0, 0, 0, 0)),
            pl.BlockSpec((beams, slots), lambda i: (0, 0)),
        ],
        out_specs=pl.BlockSpec((nodes, IB, U, 128), lambda i: (0, i, 0, 0)),
        out_shape=jax.ShapeDtypeStruct((nodes, nb * IB, U, 128), jnp.bfloat16),
        cost_estimate=pl.CostEstimate(
            flops=2 * 2 * (4 * nb * IB * U * TINT) * feeds * beams + 2 * nb * IB * U * beams * slots,
            bytes_accessed=cal.size * 2 + weights.size * 2 + select.size * 2 + nb * IB * U * slots * 2,
            transcendentals=0,
        ),
        compiler_params=pltpu.CompilerParams(vmem_limit_bytes=60 * 1024 * 1024),
    )(cal, weights, select)


def on_device(voltages, history, gains, weights, beam_lists, beam_counts):
    capacity = beam_lists.shape[1]
    beams = weights.shape[3]
    flat_ids = beam_lists.reshape(-1)
    live_slots = (jnp.arange(capacity, dtype=jnp.int32)[None, :] < beam_counts[:, None]).reshape(-1)
    select = (
        (jnp.arange(beams, dtype=jnp.int32)[:, None] == flat_ids[None, :]) & live_slots[None, :]
    ).astype(jnp.bfloat16)
    band = jnp.asarray(band_matrix())
    nfeed = lax.axis_size("feed")
    me = lax.axis_index("feed")
    order = lax.rem(me - jnp.arange(nfeed, dtype=jnp.int32) + nfeed, nfeed)
    feeds_local = weights.shape[2] // nfeed
    wperm = jnp.take(weights.reshape(2, 1, nfeed, feeds_local, beams), order, axis=2).reshape(weights.shape)
    first = filterbank(voltages, history, gains, band, 0, CHUNKS)
    gathered = lax.all_to_all(first, "feed", split_axis=0, concat_axis=0, tiled=True)
    second = filterbank(voltages, history, gains, band, 1, CHUNKS, me=me.astype(jnp.int32).reshape(1))
    pieces = [second[0:1]]
    for shift in range(1, nfeed):
        pairs = [(i, (i + shift) % nfeed) for i in range(nfeed)]
        pieces.append(lax.ppermute(second[shift : shift + 1], "feed", perm=pairs))
    outs = []
    picked = beamform(gathered, weights, select)
    outs.append(lax.all_to_all(picked, "chan", split_axis=0, concat_axis=0, tiled=True))
    picked = beamform_pieces(pieces, wperm, select, outs[0].reshape(-1, 1, U, 128))
    outs.append(lax.all_to_all(picked, "chan", split_axis=0, concat_axis=0, tiled=True))
    nodes, part, fine, width = outs[0].shape
    bins = part * len(outs)
    first_part = jnp.transpose(outs[0], (1, 0, 2, 3)).reshape(part, nodes * fine, width)
    result = lax.optimization_barrier(jnp.pad(first_part, ((0, bins - part), (0, 0), (0, 0))))
    last_part = jnp.transpose(outs[1], (1, 0, 2, 3)).reshape(part, nodes * fine, width)
    return lax.dynamic_update_slice_in_dim(result, last_part, part, axis=0)


def solution(mesh):
    in_specs = (
        P(None, None, "chan", None, "feed"),
        P(None, None, "chan", None, "feed"),
        P(None, None, "chan", "feed"),
        P(None, "chan", None, None),
        P(),
        P(),
    )
    out_specs = P("feed", None, "chan")
    return jax.shard_map(
        on_device, mesh=mesh, in_specs=in_specs, out_specs=out_specs, check_vma=False
    )
```

```python
import math

import numpy as np
import jax
import jax.numpy as jnp
from jax import lax
from jax.experimental import pallas as pl
from jax.experimental.pallas import tpu as pltpu
from jax.sharding import PartitionSpec as P

U = 16
TAPS = 4
TINT = 2
IB = 4
CHUNKS = 2
FRAMES = 2 * IB


def window_taps_np():
    length = TAPS * U
    positions = np.arange(length, dtype=np.float64)
    offsets = (positions - (length - 1) / 2.0) / U
    hann_taper = 0.5 - 0.5 * np.cos(2.0 * math.pi * (positions + 0.5) / length)
    taps_window = np.sinc(offsets) * hann_taper
    taps_window = taps_window / np.sqrt(np.sum(taps_window * taps_window) / U)
    return taps_window.astype(np.float32)


def band_matrix():
    taps = window_taps_np().astype(np.float64)
    span = (FRAMES + TAPS - 1) * U
    index_n = np.arange(U)
    phases = 2.0 * math.pi * ((index_n[:, None] * index_n[None, :]) % U) / U
    cosine = np.cos(phases) / math.sqrt(U)
    sine = np.sin(phases) / math.sqrt(U)
    table = np.array([[cosine, -sine], [sine, cosine]])
    band = np.zeros((2, FRAMES, U, 2, span))
    for t in range(FRAMES):
        for m in range(TAPS * U):
            for r in range(2):
                band[:, t, :, r, t * U + m] = taps[m] * table[r, :, m % U, :]
    band = band.reshape(2 * FRAMES * U, 2 * span).astype(np.float32)
    high = band.astype(jnp.bfloat16)
    low = (band - high.astype(np.float32)).astype(jnp.bfloat16)
    return np.concatenate([high, low], axis=1)


def _filter_kernel(chunk, shifted, *refs):
    if shifted:
        refs = refs[1:]
    _filter_body(chunk, *refs)


def _filter_body(chunk, main_ref, pre0_ref, pre1_ref, pre2_ref, hist_ref, gain_ref, band_ref, *rest):
    out_ref = rest[-1]
    tdev = pl.program_id(0)
    rows_main = main_ref.shape[4]
    nb = out_ref.shape[1]
    span = (FRAMES + TAPS - 1) * U
    half = FRAMES * U
    lanes = main_ref.shape[5]
    g_re = jnp.concatenate([gain_ref[0, p] for p in range(2)], axis=1)
    g_im = jnp.concatenate([gain_ref[1, p] for p in range(2)], axis=1)

    def rows_of(r, start, size):
        return jnp.concatenate([main_ref[r, p, 0, 0, pl.ds(start, size), :] for p in range(2)], axis=1)

    def prefix_of(r):
        pre = [jnp.concatenate([ref[r, p, 0, 0] for p in range(2)], axis=1) for ref in (pre0_ref, pre1_ref, pre2_ref)]
        pre = jnp.concatenate(pre, axis=0)
        if chunk == 0:
            hist = jnp.concatenate([hist_ref[r, p, 0] for p in range(2)], axis=1)
            pre = jnp.where(tdev == 0, hist, pre)
        return pre

    for ib in range(nb):
        parts = []
        for r in range(2):
            if ib == 0:
                parts.append(jnp.concatenate([prefix_of(r), rows_of(r, 0, span - 48)], axis=0))
            else:
                parts.append(rows_of(r, ib * half - 48, span))
        rhs = jnp.concatenate(parts + parts, axis=0)
        spec = jnp.dot(band_ref[...], rhs, preferred_element_type=jnp.float32)
        s_re = spec[:half]
        s_im = spec[half:]
        c_re = (g_re * s_re - g_im * s_im).astype(jnp.bfloat16)
        c_im = (g_re * s_im + g_im * s_re).astype(jnp.bfloat16)
        for p in range(2):
            out_ref[0, ib, 0, p] = c_re[:, p * lanes : (p + 1) * lanes].reshape(IB, TINT, U, lanes)
            out_ref[0, ib, 1, p] = c_im[:, p * lanes : (p + 1) * lanes].reshape(IB, TINT, U, lanes)


def filterbank(voltages, history, gains, band, chunk, chunks, after=None, me=None):
    _, pols, _, samples, feeds = voltages.shape
    nblk = 8
    rows_blk = samples // nblk
    rows_main = rows_blk // chunks
    nb = rows_main // U // FRAMES
    main = voltages.reshape(2, pols, nblk, chunks, rows_main, feeds)
    units = voltages.reshape(2, pols, nblk, rows_blk // 16, 16, feeds)

    def pre_map(m):
        if chunk == 0:
            return lambda t: (0, 0, jnp.maximum(t - 1, 0), rows_blk // 16 - 3 + m, 0, 0)
        return lambda t: (0, 0, t, chunk * rows_main // 16 - 3 + m, 0, 0)

    extra = [] if after is None else [after]
    shifted = me is not None

    def spec(shape, index):
        if shifted:
            return pl.BlockSpec(shape, lambda t, me_ref: index(t))
        return pl.BlockSpec(shape, index)

    if shifted:
        out_spec = pl.BlockSpec(
            (1, nb, 2, pols, IB, TINT, U, feeds),
            lambda t, me_ref: (lax.rem(t - me_ref[0] + nblk, nblk), 0, 0, 0, 0, 0, 0, 0),
        )
    else:
        out_spec = pl.BlockSpec((1, nb, 2, pols, IB, TINT, U, feeds), lambda t: (t, 0, 0, 0, 0, 0, 0, 0))
    in_specs = [
        spec((2, pols, 1, 1, rows_main, feeds), lambda t: (0, 0, t, chunk, 0, 0)),
        spec((2, pols, 1, 1, 16, feeds), pre_map(0)),
        spec((2, pols, 1, 1, 16, feeds), pre_map(1)),
        spec((2, pols, 1, 1, 16, feeds), pre_map(2)),
        spec((2, pols, 1, 48, feeds), lambda t: (0, 0, 0, 0, 0)),
        spec((2, pols, 1, feeds), lambda t: (0, 0, 0, 0)),
        spec(band.shape, lambda t: (0, 0)),
    ] + [spec((1, 1, U, 128), lambda t: (0, 0, 0, 0)) for _ in extra]
    grid_spec = pltpu.PrefetchScalarGridSpec(
        num_scalar_prefetch=1 if shifted else 0, grid=(nblk,), in_specs=in_specs, out_specs=out_spec
    )
    lead = [me] if shifted else []
    return pl.pallas_call(
        lambda *refs: _filter_kernel(chunk, shifted, *refs),
        grid_spec=grid_spec,
        out_shape=jax.ShapeDtypeStruct((nblk, nb, 2, pols, IB, TINT, U, feeds), jnp.bfloat16),
        cost_estimate=pl.CostEstimate(
            flops=2 * band.size * feeds * pols * nblk * nb,
            bytes_accessed=2 * voltages.size * 2 // chunks,
            transcendentals=0,
        ),
    )(*lead, main, units, units, units, history, gains, band, *extra)


def _beam_kernel(cal_ref, w_ref, sel_ref, out_ref):
    nsrc = cal_ref.shape[0]
    rows = 2 * 2 * IB * U
    halves = []
    for s in range(2):
        pieces = [cal_ref[d, 0, s].reshape(rows, 128) for d in range(nsrc)]
        halves.append(jnp.concatenate(pieces, axis=1))
    lhs = jnp.concatenate(halves, axis=0)
    prod_re = jnp.dot(lhs, w_ref[0, 0], preferred_element_type=jnp.float32)
    prod_im = jnp.dot(lhs, w_ref[1, 0], preferred_element_type=jnp.float32)
    real_part = prod_re[:rows] - prod_im[rows:]
    imag_part = prod_im[:rows] + prod_re[rows:]
    power = real_part * real_part + imag_part * imag_part
    quarter = rows // 2
    power = power[:quarter] + power[quarter:]
    power = power.reshape(IB, TINT, U, power.shape[-1])
    power = (power[:, 0] + power[:, 1]).reshape(IB * U, power.shape[-1])
    detected = (power * (1.0 / (4.0 * TINT))).astype(jnp.bfloat16)
    picked = jnp.dot(detected, sel_ref[...], preferred_element_type=jnp.float32).astype(jnp.bfloat16)
    nodes = out_ref.shape[0]
    for n in range(nodes):
        out_ref[n] = picked[:, n * 128 : (n + 1) * 128].reshape(IB, U, 128)


def _beam_pieces_kernel(count, *refs):
    refs = refs[:count + 2] + refs[-1:]

    class Stacked:
        def __getitem__(self, index):
            return refs[index[0]][(0,) + index[1:]]

    shape = (count,) + refs[0].shape[1:]
    stacked = Stacked()
    stacked.shape = shape
    _beam_kernel(stacked, *refs[count:])


def beamform_pieces(pieces, weights, select, after):
    nb = pieces[0].shape[1]
    feeds, beams = weights.shape[2], weights.shape[3]
    slots = select.shape[1]
    nodes = slots // 128
    piece_spec = pl.BlockSpec((1, 1, 2, 2, IB, TINT, U, 128), lambda i: (0, i, 0, 0, 0, 0, 0, 0))
    return pl.pallas_call(
        lambda *refs: _beam_pieces_kernel(len(pieces), *refs),
        grid=(nb,),
        in_specs=[piece_spec] * len(pieces)
        + [
            pl.BlockSpec((2, 1, feeds, beams), lambda i: (0, 0, 0, 0)),
            pl.BlockSpec((beams, slots), lambda i: (0, 0)),
            pl.BlockSpec((1, 1, U, 128), lambda i: (0, 0, 0, 0)),
        ],
        out_specs=pl.BlockSpec((nodes, IB, U, 128), lambda i: (0, i, 0, 0)),
        out_shape=jax.ShapeDtypeStruct((nodes, nb * IB, U, 128), jnp.bfloat16),
        cost_estimate=pl.CostEstimate(
            flops=2 * 2 * (4 * nb * IB * U * TINT) * feeds * beams + 2 * nb * IB * U * beams * slots,
            bytes_accessed=sum(p.size for p in pieces) * 2 + weights.size * 2 + select.size * 2 + nb * IB * U * slots * 2,
            transcendentals=0,
        ),
        compiler_params=pltpu.CompilerParams(vmem_limit_bytes=36 * 1024 * 1024),
    )(*pieces, weights, select, after)


def beamform(cal, weights, select):
    nsrc, nb = cal.shape[0], cal.shape[1]
    feeds, beams = weights.shape[2], weights.shape[3]
    slots = select.shape[1]
    nodes = slots // 128
    return pl.pallas_call(
        _beam_kernel,
        grid=(nb,),
        in_specs=[
            pl.BlockSpec((nsrc, 1, 2, 2, IB, TINT, U, 128), lambda i: (0, i, 0, 0, 0, 0, 0, 0)),
            pl.BlockSpec((2, 1, feeds, beams), lambda i: (0, 0, 0, 0)),
            pl.BlockSpec((beams, slots), lambda i: (0, 0)),
        ],
        out_specs=pl.BlockSpec((nodes, IB, U, 128), lambda i: (0, i, 0, 0)),
        out_shape=jax.ShapeDtypeStruct((nodes, nb * IB, U, 128), jnp.bfloat16),
        cost_estimate=pl.CostEstimate(
            flops=2 * 2 * (4 * nb * IB * U * TINT) * feeds * beams + 2 * nb * IB * U * beams * slots,
            bytes_accessed=cal.size * 2 + weights.size * 2 + select.size * 2 + nb * IB * U * slots * 2,
            transcendentals=0,
        ),
        compiler_params=pltpu.CompilerParams(vmem_limit_bytes=36 * 1024 * 1024),
    )(cal, weights, select)


def on_device(voltages, history, gains, weights, beam_lists, beam_counts):
    capacity = beam_lists.shape[1]
    beams = weights.shape[3]
    flat_ids = beam_lists.reshape(-1)
    live_slots = (jnp.arange(capacity, dtype=jnp.int32)[None, :] < beam_counts[:, None]).reshape(-1)
    select = (
        (jnp.arange(beams, dtype=jnp.int32)[:, None] == flat_ids[None, :]) & live_slots[None, :]
    ).astype(jnp.bfloat16)
    band = jnp.asarray(band_matrix())
    nfeed = lax.axis_size("feed")
    me = lax.axis_index("feed")
    order = lax.rem(me - jnp.arange(nfeed, dtype=jnp.int32) + nfeed, nfeed)
    feeds_local = weights.shape[2] // nfeed
    wperm = jnp.take(weights.reshape(2, 1, nfeed, feeds_local, beams), order, axis=2).reshape(weights.shape)
    first = filterbank(voltages, history, gains, band, 0, CHUNKS)
    gathered = lax.all_to_all(first, "feed", split_axis=0, concat_axis=0, tiled=True)
    second = filterbank(voltages, history, gains, band, 1, CHUNKS, me=me.astype(jnp.int32).reshape(1))
    pieces = [second[0:1]]
    for shift in range(1, nfeed):
        pairs = [(i, (i + shift) % nfeed) for i in range(nfeed)]
        pieces.append(lax.ppermute(second[shift : shift + 1], "feed", perm=pairs))
    outs = []
    picked = beamform(gathered, weights, select)
    outs.append(lax.all_to_all(picked, "chan", split_axis=0, concat_axis=0, tiled=True))
    picked = beamform_pieces(pieces, wperm, select, outs[0].reshape(-1, 1, U, 128))
    outs.append(lax.all_to_all(picked, "chan", split_axis=0, concat_axis=0, tiled=True))
    nodes, part, fine, width = outs[0].shape
    bins = part * len(outs)
    first_part = jnp.transpose(outs[0], (1, 0, 2, 3)).reshape(part, nodes * fine, width)
    result = lax.optimization_barrier(jnp.pad(first_part, ((0, bins - part), (0, 0), (0, 0))))
    last_part = jnp.transpose(outs[1], (1, 0, 2, 3)).reshape(part, nodes * fine, width)
    return lax.dynamic_update_slice_in_dim(result, last_part, part, axis=0)


def solution(mesh):
    in_specs = (
        P(None, None, "chan", None, "feed"),
        P(None, None, "chan", None, "feed"),
        P(None, None, "chan", "feed"),
        P(None, "chan", None, None),
        P(),
        P(),
    )
    out_specs = P("feed", None, "chan")
    return jax.shard_map(
        on_device, mesh=mesh, in_specs=in_specs, out_specs=out_specs, check_vma=False
    )
```
